32 devices in a mesh: groups: 2 (over x), gz: 16 (over z, y, core).
Axes of the slice: x: 2, y: 2, z: 4, core: 2. Of those that a mesh axis runs over, the one named last changes fastest.
Arguments:
- waves: bfloat16 [192, 8, 64, 256], P(('groups', 'gz')), parts along dimension 0, may hold values from -6 to 6
- potential: float32 [192, 512], P(('groups', 'gz')), parts along dimension 0, may hold values from 0.25 to 4
- domain_of: int32 [32], P('groups'), parts along dimension 0, may hold values from 0 to 7, never falling along the last dimension, each value on 1 to 9 neighbouring positions
Outputs:
- orbitals: bfloat16 [192, 8, 64, 256], P(('groups', 'gz')), parts along dimension 0
The draws below stay inside these ranges and needn't reach their ends.
There are 2 independent parts, one for each index of `groups`. The reference program is written for one: setup_inputs(seed, part) draws one part's arguments, and reference() takes and returns one part's arrays. A program takes and returns all parts, laid end to end along the dimension named above; each array names one. Nothing has to cross between parts.
Inputs may be any that keep to these rules, and one draw needn't show every extreme that they name: `domain_of`: never falls; every domain holds 1 to 9 blocks, one domain exactly that many.
All inputs are finite; a program needn't handle non-finite values.
Results may differ from the reference program's by a relative error of at most 0.0038.
The reference program's roundings to bfloat16 on the way count: a program that leaves them out, or rounds other values in their place, can miss the bound.
Values may be sent and summed in bfloat16 or wider, within the bound.
No kernel may reach another device: no remote copies, remote signals or barrier semaphores. Data moves between devices by JAX's collectives and lax.ppermute only.
A program may use at most 64 MiB of HBM per device.

```python
import math
import jax
import jax.numpy as jnp
import numpy as np
from jax import lax

NB = 256
PANEL = 128
NX = 64
NY = 8
CZ = 6
DOMS = 8
DEGREE = 4
NZ = 96
N_GZ = 16


def level_of(rng, extent, cuts, low, top_value):
    level = 1.0
    for dim, parts in cuts:
        draws = jax.random.uniform(jax.random.fold_in(jax.random.fold_in(rng, 6), dim), (parts,), jnp.float32, low / len(cuts), top_value / len(cuts))
        level = level * jnp.repeat(jnp.exp(draws), extent[dim] // parts).reshape((-1,) + (1,) * (len(extent) - 1 - dim))
    return level


def split_up(amount, total, reach, slope):
    weights = [(1 << 20) // math.isqrt(standing ** slope) + 1 for standing in range(2, amount + 1)]
    spare, holding = total - reach - (amount - 1), [1] * (amount - 1)
    while spare > 0:
        free = [i for i in range(amount - 1) if holding[i] < reach]
        pool, budget = sum([weights[i] for i in free]), spare
        for i in free:
            addition = min(reach - holding[i], max(1, budget * weights[i] // pool), spare)
            holding[i] = holding[i] + addition
            spare = spare - addition
    return np.array([reach] + holding)


def uneven_parts(stream_key, amount, total, reach, slope):
    if amount == 2:
        one = jax.random.randint(stream_key, (), max(1, total - reach), min(reach, total - 1) + 1)
        return jnp.stack([one, total - one])
    sizes = jnp.asarray(split_up(amount, total, reach, slope), jnp.int32)
    couples = (amount - 1) // 2
    giver, sink = sizes[1:1 + 2 * couples:2], sizes[2:2 + 2 * couples:2]
    room = jnp.minimum(giver - 1, reach - sink)
    passed = jax.random.randint(jax.random.fold_in(stream_key, 1), (couples,), 0, 1 << 20) % (room + 1)
    sizes = sizes.at[1:1 + 2 * couples:2].set(giver - passed).at[2:2 + 2 * couples:2].set(sink + passed)
    return sizes[jax.random.permutation(jax.random.fold_in(stream_key, 2), amount)]


def scatter_about(own_key, dims, deviation, reach, shards=(), held_as=jnp.bfloat16):
    drawn = jax.random.normal(own_key, dims, jnp.float32) * deviation
    if len(shards) > 0:
        drawn = level_of(own_key, dims, shards, -0.22, 0.18) * drawn
    return jnp.clip(drawn, min=-reach, max=reach).astype(held_as)


def setup_inputs(seed: int = 0, part: int = 0) -> dict:
    key_list = jax.random.split(jax.random.key(seed), 4)
    part_splits = jax.random.split(jax.random.fold_in(key_list[3], part), 4)
    waves = scatter_about(part_splits[0], (NZ, NY, NX, NB), 1.0, 6.0, ((0, 16),))
    potential = jnp.clip(jnp.exp(math.log(4.0) - 2.7725887 * jax.random.uniform(part_splits[1], (NZ, NY * NX), jnp.float32) ** level_of(part_splits[1], (NZ, NY * NX), ((0, 16),), -0.2, 0.2)), 0.25, 4.0)
    domain_of = jnp.searchsorted(jnp.cumsum(uneven_parts(part_splits[2], DOMS, N_GZ, N_GZ // 2 + 1, 2)), jnp.arange(N_GZ), side="right").astype(jnp.int32)
    return dict(waves=waves, potential=potential, domain_of=domain_of)


COEF = (-49.0 / 18.0, 1.5, -0.15, 1.0 / 90.0)
CSHIFT = 7.0
EWIDTH = 5.0

def hamiltonian(extended, potential):
    inner = extended[3:-3]
    planes = inner.shape[0]
    rows_y = inner.shape[1]
    rows_x = inner.shape[2]
    padded_y = jnp.pad(inner, ((0, 0), (3, 3), (0, 0), (0, 0)))
    padded_x = jnp.pad(inner, ((0, 0), (0, 0), (3, 3), (0, 0)))
    total = 3.0 * COEF[0] * inner
    for distance in (1, 2, 3):
        along_z = extended[3 + distance:3 + distance + planes] + extended[3 - distance:3 - distance + planes]
        along_y = padded_y[:, 3 + distance:3 + distance + rows_y] + padded_y[:, 3 - distance:3 - distance + rows_y]
        along_x = padded_x[:, :, 3 + distance:3 + distance + rows_x] + padded_x[:, :, 3 - distance:3 - distance + rows_x]
        total = total + COEF[distance] * (along_z + along_y + along_x)
    return potential[:, :, :, None] * inner - 0.5 * total

def reference(waves, potential, domain_of):
    slabs = N_GZ
    shaped = waves.reshape(slabs, CZ, NY, NX, NB)
    grid = potential.reshape(slabs, CZ, NY, NX)
    below = jnp.concatenate([jnp.zeros((1,), jnp.float32), (domain_of[1:] == domain_of[:-1]).astype(jnp.float32)])
    above = jnp.concatenate([(domain_of[:-1] == domain_of[1:]).astype(jnp.float32), jnp.zeros((1,), jnp.float32)])
    below_mask = below[:, None, None, None, None]
    above_mask = above[:, None, None, None, None]

    def extend(field):
        zeros = jnp.zeros_like(field[:1, :3])
        lower_rim = jnp.concatenate([zeros, field[:-1, -3:]], axis=0) * below_mask
        upper_rim = jnp.concatenate([field[1:, :3], zeros], axis=0) * above_mask
        return jnp.concatenate([lower_rim, field, upper_rim], axis=1)
    apply_all = jax.vmap(hamiltonian)

    def filter_bands(block):
        field = block.astype(jnp.float32)
        image = apply_all(extend(field), grid)
        older = block
        current = ((image - CSHIFT * field) / EWIDTH).astype(jnp.bfloat16)
        for turn in range(DEGREE - 1):
            field = current.astype(jnp.float32)
            image = apply_all(extend(field), grid)
            newer = (2.0 / EWIDTH * (image - CSHIFT * field) - older.astype(jnp.float32)).astype(jnp.bfloat16)
            older, current = (current, newer)
        return current
    width = 32
    blocks = jnp.moveaxis(shaped.reshape(slabs, CZ, NY, NX, NB // width, width), 4, 0)
    filtered = lax.map(filter_bands, blocks)
    filtered = jnp.moveaxis(filtered, 0, 4).reshape(slabs, CZ * NY * NX, NB)
    picker = (domain_of[:, None] == jnp.arange(DOMS)[None, :]).astype(jnp.float32)
    cells = jnp.sum(picker, axis=0) * (CZ * NY * NX)

    def domain_mean(local):
        summed = jnp.einsum('sd,sab->dab', picker, local)
        return summed / cells[:, None, None]
    eye = jnp.eye(PANEL, dtype=jnp.float32)
    pieces = []
    for panel in range(NB // PANEL):
        block = filtered[:, :, panel * PANEL:(panel + 1) * PANEL]
        if panel > 0:
            earlier = jnp.concatenate(pieces, axis=-1)
            correlation = domain_mean(jnp.einsum('sca,scb->sab', earlier.astype(jnp.float32), block.astype(jnp.float32)))
            mine = correlation.astype(jnp.bfloat16)[domain_of]
            block = (block.astype(jnp.float32) - jnp.einsum('sca,sab->scb', earlier.astype(jnp.float32), mine.astype(jnp.float32))).astype(jnp.bfloat16)
        gram = domain_mean(jnp.einsum('sca,scb->sab', block.astype(jnp.float32), block.astype(jnp.float32)))
        factor = jnp.linalg.cholesky(gram)
        inverse = jax.vmap(lambda item: jax.scipy.linalg.solve_triangular(item, eye, lower=True))(factor)
        whitening = jnp.swapaxes(inverse, 1, 2).astype(jnp.bfloat16)[domain_of]
        pieces.append(jnp.einsum('sca,sab->scb', block.astype(jnp.float32), whitening.astype(jnp.float32)).astype(jnp.bfloat16))
    return jnp.concatenate(pieces, axis=-1).reshape(slabs * CZ, NY, NX, NB)
```

```python
import jax
import jax.numpy as jnp
from jax import lax
from jax.sharding import PartitionSpec as P

PANEL = 128
NX = 64
NY = 8
DOMS = 8
DEGREE = 4


COEF = (-49.0 / 18.0, 1.5, -0.15, 1.0 / 90.0)
CSHIFT = 7.0
EWIDTH = 5.0


def extended_2(block, sides, width):
    for axis, dim in sides:
        count = lax.axis_size(axis)
        forward = [(i, i + 1) for i in range(count - 1)]
        backward = [(target, source) for source, target in forward]
        low = lax.ppermute(
            lax.slice_in_dim(block, block.shape[dim] - width, None, axis=dim), axis, forward
        )
        high = lax.ppermute(lax.slice_in_dim(block, 0, width, axis=dim), axis, backward)
        block = jnp.concatenate([low, block, high], axis=dim)
    return block


def hamiltonian(extended, potential):
    inner = extended[3:-3]
    planes = inner.shape[0]
    rows_y = inner.shape[1]
    rows_x = inner.shape[2]
    padded_y = jnp.pad(inner, ((0, 0), (3, 3), (0, 0), (0, 0)))
    padded_x = jnp.pad(inner, ((0, 0), (0, 0), (3, 3), (0, 0)))
    total = 3.0 * COEF[0] * inner
    for distance in (1, 2, 3):
        along_z = (
            extended[3 + distance : 3 + distance + planes]
            + extended[3 - distance : 3 - distance + planes]
        )
        along_y = (
            padded_y[:, 3 + distance : 3 + distance + rows_y]
            + padded_y[:, 3 - distance : 3 - distance + rows_y]
        )
        along_x = (
            padded_x[:, :, 3 + distance : 3 + distance + rows_x]
            + padded_x[:, :, 3 - distance : 3 - distance + rows_x]
        )
        total = total + COEF[distance] * (along_z + along_y + along_x)
    return potential[:, :, :, None] * inner - 0.5 * total


def shards(waves, potential, domain_of):
    slabs = lax.axis_size("gz")
    position = lax.axis_index("gz")
    planes = waves.shape[0]
    bands = waves.shape[3]
    grid = potential.reshape(planes, NY, NX)
    owner = domain_of[position]
    below = jnp.where(position > 0, domain_of[jnp.maximum(position - 1, 0)] == owner, False).astype(
        jnp.float32
    )
    above = jnp.where(
        position < slabs - 1, domain_of[jnp.minimum(position + 1, slabs - 1)] == owner, False
    ).astype(jnp.float32)
    mask_three = jnp.concatenate(
        [
            jnp.broadcast_to(below, (3,)),
            jnp.ones((planes,), jnp.float32),
            jnp.broadcast_to(above, (3,)),
        ]
    )[:, None, None, None]

    def rimmed(field):
        return extended_2(field, (("gz", 0),), 3).astype(jnp.float32) * mask_three

    extended = rimmed(waves)
    image = hamiltonian(extended, grid)
    older = waves
    current = ((image - CSHIFT * extended[3:-3]) / EWIDTH).astype(jnp.bfloat16)
    for turn in range(DEGREE - 1):
        extended = rimmed(current)
        image = hamiltonian(extended, grid)
        newer = (
            2.0 / EWIDTH * (image - CSHIFT * extended[3:-3]) - older.astype(jnp.float32)
        ).astype(jnp.bfloat16)
        older, current = (current, newer)
    cells = jnp.sum((domain_of == owner).astype(jnp.float32)) * (planes * NY * NX)
    rows = current.reshape(planes * NY * NX, bands)

    def domain_total(term):
        forward = term
        backward = term
        distance = 1
        while distance < slabs:
            ahead = [(i, i + distance) for i in range(slabs - distance)]
            behind = [(i + distance, i) for i in range(slabs - distance)]
            from_low = lax.ppermute(forward, "gz", ahead)
            from_high = lax.ppermute(backward, "gz", behind)
            low_same = jnp.where(
                position >= distance,
                domain_of[jnp.maximum(position - distance, 0)] == owner,
                False,
            ).astype(jnp.float32)
            high_same = jnp.where(
                position + distance < slabs,
                domain_of[jnp.minimum(position + distance, slabs - 1)] == owner,
                False,
            ).astype(jnp.float32)
            forward = forward + low_same * from_low
            backward = backward + high_same * from_high
            distance *= 2
        return forward + backward - term

    identity = jnp.eye(PANEL, dtype=jnp.float32)
    panels = bands // PANEL
    blocks = [rows[:, p * PANEL : (p + 1) * PANEL] for p in range(panels)]
    first = blocks[0]
    cross = jnp.einsum("ca,cb->ab", first, rows, preferred_element_type=jnp.float32)
    cross = domain_total(cross) / cells
    pieces = []
    whitenings = []
    for panel in range(panels):
        block = blocks[panel]
        if panel == 0:
            gram = cross[:, :PANEL]
        else:
            if panel == 1:
                correlation = jnp.dot(
                    whitenings[0].T.astype(jnp.float32),
                    cross[:, PANEL : 2 * PANEL],
                    preferred_element_type=jnp.float32,
                )
            else:
                earlier = jnp.concatenate(pieces, axis=1)
                correlation = (
                    domain_total(
                        jnp.einsum("ca,cb->ab", earlier, block, preferred_element_type=jnp.float32)
                    )
                    / cells
                )
            earlier = jnp.concatenate(pieces, axis=1)
            block = (
                block.astype(jnp.float32)
                - jnp.dot(
                    earlier, correlation.astype(jnp.bfloat16), preferred_element_type=jnp.float32
                )
            ).astype(jnp.bfloat16)
            gram = (
                domain_total(
                    jnp.einsum("ca,cb->ab", block, block, preferred_element_type=jnp.float32)
                )
                / cells
            )
        factor = jnp.linalg.cholesky(gram)
        inverse = jax.scipy.linalg.solve_triangular(factor, identity, lower=True)
        whitening = inverse.T.astype(jnp.bfloat16)
        whitenings.append(whitening)
        pieces.append(
            jnp.dot(block, whitening, preferred_element_type=jnp.float32).astype(jnp.bfloat16)
        )
    return jnp.concatenate(pieces, axis=1).reshape(planes, NY, NX, bands)


def solution(mesh):
    return jax.shard_map(
        shards,
        mesh=mesh,
        in_specs=(P(("groups", "gz"), None, None, None), P(("groups", "gz"), None), P("groups")),
        out_specs=P(("groups", "gz"), None, None, None),
        check_vma=False,
    )
```

```python
import jax
import jax.numpy as jnp
from jax import lax
from jax.sharding import PartitionSpec as P


PANEL = 128
NX = 64
NY = 8
DOMS = 8
DEGREE = 4


COEF = (-49.0 / 18.0, 1.5, -0.15, 1.0 / 90.0)
CSHIFT = 7.0
EWIDTH = 5.0


def extended_2(block, sides, width):
    for axis, dim in sides:
        count = lax.axis_size(axis)
        forward = [(i, i + 1) for i in range(count - 1)]
        backward = [(target, source) for source, target in forward]
        low = lax.ppermute(
            lax.slice_in_dim(block, block.shape[dim] - width, None, axis=dim), axis, forward
        )
        high = lax.ppermute(lax.slice_in_dim(block, 0, width, axis=dim), axis, backward)
        block = jnp.concatenate([low, block, high], axis=dim)
    return block


def hamiltonian(extended, potential):
    inner = extended[3:-3]
    planes = inner.shape[0]
    rows_y = inner.shape[1]
    rows_x = inner.shape[2]
    padded_y = jnp.pad(inner, ((0, 0), (3, 3), (0, 0), (0, 0)))
    padded_x = jnp.pad(inner, ((0, 0), (0, 0), (3, 3), (0, 0)))
    total = 3.0 * COEF[0] * inner
    for distance in (1, 2, 3):
        along_z = (
            extended[3 + distance : 3 + distance + planes]
            + extended[3 - distance : 3 - distance + planes]
        )
        along_y = (
            padded_y[:, 3 + distance : 3 + distance + rows_y]
            + padded_y[:, 3 - distance : 3 - distance + rows_y]
        )
        along_x = (
            padded_x[:, :, 3 + distance : 3 + distance + rows_x]
            + padded_x[:, :, 3 - distance : 3 - distance + rows_x]
        )
        total = total + COEF[distance] * (along_z + along_y + along_x)
    return potential[:, :, :, None] * inner - 0.5 * total


def shards(waves, potential, domain_of):
    slabs = lax.axis_size("gz")
    position = lax.axis_index("gz")
    planes = waves.shape[0]
    bands = waves.shape[3]
    reach = 2

    def neighbour(block, distance):
        if distance > 0:
            pairs = [(i + distance, i) for i in range(slabs - distance)]
        else:
            pairs = [(i, i - distance) for i in range(slabs + distance)]
        return lax.ppermute(block, "gz", pairs)

    offsets = list(range(-reach, reach + 1))
    owner = domain_of[position]
    weights = []
    wave_parts = []
    potential_parts = []
    for offset in offsets:
        if offset == 0:
            wave_parts.append(waves)
            potential_parts.append(potential)
            weights.append(jnp.ones((), jnp.float32))
            continue
        wave_parts.append(neighbour(waves, offset))
        potential_parts.append(neighbour(potential, offset))
        place = position + offset
        inside = (place >= 0) & (place < slabs)
        same = domain_of[jnp.clip(place, 0, slabs - 1)] == owner
        weights.append((inside & same).astype(jnp.float32))
    mask = jnp.concatenate([jnp.broadcast_to(w, (planes,)) for w in weights])[:, None, None, None]
    grid = jnp.concatenate(potential_parts, axis=0).reshape(-1, NY, NX)
    depth = reach * planes

    def trimmed(array, cut):
        return array[cut : array.shape[0] - cut]

    older = jnp.concatenate(wave_parts, axis=0)
    field = older.astype(jnp.float32) * mask
    older = field.astype(jnp.bfloat16)
    image = hamiltonian(field, trimmed(grid, 3))
    current = ((image - CSHIFT * trimmed(field, 3)) / EWIDTH) * trimmed(mask, 3)
    current = current.astype(jnp.bfloat16)
    for turn in range(DEGREE - 1):
        cut = 3 * (turn + 1)
        field = current.astype(jnp.float32)
        image = hamiltonian(field, trimmed(grid, cut + 3))
        newer = (
            2.0 / EWIDTH * (image - CSHIFT * trimmed(field, 3))
            - trimmed(older, 6).astype(jnp.float32)
        ) * trimmed(mask, cut + 3)
        older, current = (current, newer.astype(jnp.bfloat16))
    current = trimmed(current, depth - 3 * DEGREE)
    cells = jnp.sum((domain_of == owner).astype(jnp.float32)) * (planes * NY * NX)
    rows = current.reshape(planes * NY * NX, bands)

    def domain_total(term):
        forward = term
        backward = term
        distance = 1
        while distance < slabs:
            ahead = [(i, i + distance) for i in range(slabs - distance)]
            behind = [(i + distance, i) for i in range(slabs - distance)]
            from_low = lax.ppermute(forward, "gz", ahead)
            from_high = lax.ppermute(backward, "gz", behind)
            low_same = jnp.where(
                position >= distance,
                domain_of[jnp.maximum(position - distance, 0)] == owner,
                False,
            ).astype(jnp.float32)
            high_same = jnp.where(
                position + distance < slabs,
                domain_of[jnp.minimum(position + distance, slabs - 1)] == owner,
                False,
            ).astype(jnp.float32)
            forward = forward + low_same * from_low
            backward = backward + high_same * from_high
            distance *= 2
        return forward + backward - term

    identity = jnp.eye(PANEL, dtype=jnp.float32)
    panels = bands // PANEL
    blocks = [rows[:, p * PANEL : (p + 1) * PANEL] for p in range(panels)]
    first = blocks[0]
    cross = jnp.einsum("ca,cb->ab", first, rows, preferred_element_type=jnp.float32)
    cross = domain_total(cross) / cells
    pieces = []
    whitenings = []
    for panel in range(panels):
        block = blocks[panel]
        if panel == 0:
            gram = cross[:, :PANEL]
        else:
            if panel == 1:
                correlation = jnp.dot(
                    whitenings[0].T.astype(jnp.float32),
                    cross[:, PANEL : 2 * PANEL],
                    preferred_element_type=jnp.float32,
                )
            else:
                earlier = jnp.concatenate(pieces, axis=1)
                correlation = (
                    domain_total(
                        jnp.einsum("ca,cb->ab", earlier, block, preferred_element_type=jnp.float32)
                    )
                    / cells
                )
            earlier = jnp.concatenate(pieces, axis=1)
            block = (
                block.astype(jnp.float32)
                - jnp.dot(
                    earlier, correlation.astype(jnp.bfloat16), preferred_element_type=jnp.float32
                )
            ).astype(jnp.bfloat16)
            gram = (
                domain_total(
                    jnp.einsum("ca,cb->ab", block, block, preferred_element_type=jnp.float32)
                )
                / cells
            )
        factor = jnp.linalg.cholesky(gram)
        inverse = jax.scipy.linalg.solve_triangular(factor, identity, lower=True)
        whitening = inverse.T.astype(jnp.bfloat16)
        whitenings.append(whitening)
        pieces.append(
            jnp.dot(block, whitening, preferred_element_type=jnp.float32).astype(jnp.bfloat16)
        )
    return jnp.concatenate(pieces, axis=1).reshape(planes, NY, NX, bands)


def solution(mesh):
    return jax.shard_map(
        shards,
        mesh=mesh,
        in_specs=(P(("groups", "gz"), None, None, None), P(("groups", "gz"), None), P("groups")),
        out_specs=P(("groups", "gz"), None, None, None),
        check_vma=False,
    )
```

```python
import jax
import jax.numpy as jnp
from jax import lax
from jax.experimental import pallas as pl
from jax.experimental.pallas import tpu as pltpu
from jax.sharding import PartitionSpec as P

PANEL = 128
NX = 64
NY = 8
DOMS = 8
DEGREE = 4


COEF = (-49.0 / 18.0, 1.5, -0.15, 1.0 / 90.0)
CSHIFT = 7.0
EWIDTH = 5.0


def _lower_inverse_kernel(gram_ref, out_ref, work_ref):
    n = gram_ref.shape[0]
    rows = lax.broadcasted_iota(jnp.int32, (n, 2 * n), 0)
    lanes = lax.broadcasted_iota(jnp.int32, (n, 2 * n), 1)
    work_ref[:, :n] = gram_ref[...]
    work_ref[:, n:] = (lax.broadcasted_iota(jnp.int32, (n, n), 0) == lax.broadcasted_iota(jnp.int32, (n, n), 1)).astype(jnp.float32)

    def step(k, carry):
        row = work_ref[pl.ds(k, 1), :]
        lane = lax.broadcasted_iota(jnp.int32, (1, 2 * n), 1)
        pivot = jnp.sum(jnp.where(lane == k, row, 0.0), axis=1, keepdims=True)
        scale = 1.0 / jnp.sqrt(pivot)
        scaled = row * scale
        whole = work_ref[...]
        left = whole[:, :n]
        column = jnp.sum(jnp.where(lanes[:, :n] == k, left, 0.0), axis=1, keepdims=True) * scale
        updated = jnp.where(rows > k, whole - column * scaled, whole)
        work_ref[...] = jnp.where(rows == k, scaled, updated)
        return carry

    lax.fori_loop(0, n, step, 0)
    out_ref[...] = work_ref[:, n:]


def lower_inverse(gram):
    n = gram.shape[0]
    return pl.pallas_call(
        _lower_inverse_kernel,
        out_shape=jax.ShapeDtypeStruct((n, n), jnp.float32),
        scratch_shapes=[pltpu.VMEM((n, 2 * n), jnp.float32)],
    )(gram)


def extended_2(block, sides, width):
    for axis, dim in sides:
        count = lax.axis_size(axis)
        forward = [(i, i + 1) for i in range(count - 1)]
        backward = [(target, source) for source, target in forward]
        low = lax.ppermute(
            lax.slice_in_dim(block, block.shape[dim] - width, None, axis=dim), axis, forward
        )
        high = lax.ppermute(lax.slice_in_dim(block, 0, width, axis=dim), axis, backward)
        block = jnp.concatenate([low, block, high], axis=dim)
    return block


def hamiltonian(extended, potential):
    inner = extended[3:-3]
    planes = inner.shape[0]
    rows_y = inner.shape[1]
    rows_x = inner.shape[2]
    padded_y = jnp.pad(inner, ((0, 0), (3, 3), (0, 0), (0, 0)))
    padded_x = jnp.pad(inner, ((0, 0), (0, 0), (3, 3), (0, 0)))
    total = 3.0 * COEF[0] * inner
    for distance in (1, 2, 3):
        along_z = (
            extended[3 + distance : 3 + distance + planes]
            + extended[3 - distance : 3 - distance + planes]
        )
        along_y = (
            padded_y[:, 3 + distance : 3 + distance + rows_y]
            + padded_y[:, 3 - distance : 3 - distance + rows_y]
        )
        along_x = (
            padded_x[:, :, 3 + distance : 3 + distance + rows_x]
            + padded_x[:, :, 3 - distance : 3 - distance + rows_x]
        )
        total = total + COEF[distance] * (along_z + along_y + along_x)
    return potential[:, :, :, None] * inner - 0.5 * total


def shards(waves, potential, domain_of):
    slabs = lax.axis_size("gz")
    position = lax.axis_index("gz")
    planes = waves.shape[0]
    bands = waves.shape[3]
    grid = potential.reshape(planes, NY, NX)
    owner = domain_of[position]
    below = jnp.where(position > 0, domain_of[jnp.maximum(position - 1, 0)] == owner, False).astype(
        jnp.float32
    )
    above = jnp.where(
        position < slabs - 1, domain_of[jnp.minimum(position + 1, slabs - 1)] == owner, False
    ).astype(jnp.float32)
    mask_three = jnp.concatenate(
        [
            jnp.broadcast_to(below, (3,)),
            jnp.ones((planes,), jnp.float32),
            jnp.broadcast_to(above, (3,)),
        ]
    )[:, None, None, None]

    def rimmed(field):
        return extended_2(field, (("gz", 0),), 3).astype(jnp.float32) * mask_three

    extended = rimmed(waves)
    image = hamiltonian(extended, grid)
    older = waves
    current = ((image - CSHIFT * extended[3:-3]) / EWIDTH).astype(jnp.bfloat16)
    for turn in range(DEGREE - 1):
        extended = rimmed(current)
        image = hamiltonian(extended, grid)
        newer = (
            2.0 / EWIDTH * (image - CSHIFT * extended[3:-3]) - older.astype(jnp.float32)
        ).astype(jnp.bfloat16)
        older, current = (current, newer)
    cells = jnp.sum((domain_of == owner).astype(jnp.float32)) * (planes * NY * NX)
    rows = current.reshape(planes * NY * NX, bands)

    def domain_total(term):
        forward = term
        backward = term
        distance = 1
        while distance < slabs:
            ahead = [(i, i + distance) for i in range(slabs - distance)]
            behind = [(i + distance, i) for i in range(slabs - distance)]
            from_low = lax.ppermute(forward, "gz", ahead)
            from_high = lax.ppermute(backward, "gz", behind)
            low_same = jnp.where(
                position >= distance,
                domain_of[jnp.maximum(position - distance, 0)] == owner,
                False,
            ).astype(jnp.float32)
            high_same = jnp.where(
                position + distance < slabs,
                domain_of[jnp.minimum(position + distance, slabs - 1)] == owner,
                False,
            ).astype(jnp.float32)
            forward = forward + low_same * from_low
            backward = backward + high_same * from_high
            distance *= 2
        return forward + backward - term

    identity = jnp.eye(PANEL, dtype=jnp.float32)
    panels = bands // PANEL
    blocks = [rows[:, p * PANEL : (p + 1) * PANEL] for p in range(panels)]
    first = blocks[0]
    cross = jnp.einsum("ca,cb->ab", first, rows, preferred_element_type=jnp.float32)
    cross = domain_total(cross) / cells
    pieces = []
    whitenings = []
    for panel in range(panels):
        block = blocks[panel]
        if panel == 0:
            gram = cross[:, :PANEL]
        else:
            if panel == 1:
                correlation = jnp.dot(
                    whitenings[0].T.astype(jnp.float32),
                    cross[:, PANEL : 2 * PANEL],
                    preferred_element_type=jnp.float32,
                )
            else:
                earlier = jnp.concatenate(pieces, axis=1)
                correlation = (
                    domain_total(
                        jnp.einsum("ca,cb->ab", earlier, block, preferred_element_type=jnp.float32)
                    )
                    / cells
                )
            earlier = jnp.concatenate(pieces, axis=1)
            block = (
                block.astype(jnp.float32)
                - jnp.dot(
                    earlier, correlation.astype(jnp.bfloat16), preferred_element_type=jnp.float32
                )
            ).astype(jnp.bfloat16)
            gram = (
                domain_total(
                    jnp.einsum("ca,cb->ab", block, block, preferred_element_type=jnp.float32)
                )
                / cells
            )
        inverse = lower_inverse(gram)
        whitening = inverse.T.astype(jnp.bfloat16)
        whitenings.append(whitening)
        pieces.append(
            jnp.dot(block, whitening, preferred_element_type=jnp.float32).astype(jnp.bfloat16)
        )
    return jnp.concatenate(pieces, axis=1).reshape(planes, NY, NX, bands)


def solution(mesh):
    return jax.shard_map(
        shards,
        mesh=mesh,
        in_specs=(P(("groups", "gz"), None, None, None), P(("groups", "gz"), None), P("groups")),
        out_specs=P(("groups", "gz"), None, None, None),
        check_vma=False,
    )
```

```python
import functools

import jax
import jax.numpy as jnp
from jax import lax
from jax.experimental import pallas as pl
from jax.experimental.pallas import tpu as pltpu
from jax.sharding import PartitionSpec as P

PANEL = 128
NX = 64
NY = 8
DOMS = 8
DEGREE = 4


COEF = (-49.0 / 18.0, 1.5, -0.15, 1.0 / 90.0)
CSHIFT = 7.0
EWIDTH = 5.0


def _lower_inverse_kernel(gram_ref, out_ref, work_ref):
    n = gram_ref.shape[0]
    rows = lax.broadcasted_iota(jnp.int32, (n, 2 * n), 0)
    lanes = lax.broadcasted_iota(jnp.int32, (n, 2 * n), 1)
    work_ref[:, :n] = gram_ref[...]
    work_ref[:, n:] = (lax.broadcasted_iota(jnp.int32, (n, n), 0) == lax.broadcasted_iota(jnp.int32, (n, n), 1)).astype(jnp.float32)

    def step(k, carry):
        row = work_ref[pl.ds(k, 1), :]
        lane = lax.broadcasted_iota(jnp.int32, (1, 2 * n), 1)
        pivot = jnp.sum(jnp.where(lane == k, row, 0.0), axis=1, keepdims=True)
        scale = 1.0 / jnp.sqrt(pivot)
        scaled = row * scale
        whole = work_ref[...]
        left = whole[:, :n]
        column = jnp.sum(jnp.where(lanes[:, :n] == k, left, 0.0), axis=1, keepdims=True) * scale
        updated = jnp.where(rows > k, whole - column * scaled, whole)
        work_ref[...] = jnp.where(rows == k, scaled, updated)
        return carry

    lax.fori_loop(0, n, step, 0)
    out_ref[...] = work_ref[:, n:]


def lower_inverse(gram):
    n = gram.shape[0]
    return pl.pallas_call(
        _lower_inverse_kernel,
        out_shape=jax.ShapeDtypeStruct((n, n), jnp.float32),
        scratch_shapes=[pltpu.VMEM((n, 2 * n), jnp.float32)],
    )(gram)


def _step_kernel(first, extended_ref, older_ref, potential_ref, out_ref):
    z = pl.program_id(1)
    rows_y = extended_ref.shape[1]
    rows_x = extended_ref.shape[2]
    place = lax.broadcasted_iota(jnp.int32, (rows_x, extended_ref.shape[3]), 0)

    def plane(offset, y):
        return extended_ref[z + 3 + offset, y].astype(jnp.float32)

    for y in range(rows_y):
        inner = plane(0, y)
        total = 3.0 * COEF[0] * inner
        for distance in (1, 2, 3):
            along_z = plane(distance, y) + plane(-distance, y)
            up = plane(0, y + distance) if y + distance < rows_y else None
            down = plane(0, y - distance) if y - distance >= 0 else None
            if up is None:
                along_y = down
            elif down is None:
                along_y = up
            else:
                along_y = up + down
            ahead = jnp.where(place + distance < rows_x, pltpu.roll(inner, rows_x - distance, 0), 0.0)
            behind = jnp.where(place >= distance, pltpu.roll(inner, distance, 0), 0.0)
            along_x = ahead + behind
            total = total + COEF[distance] * (along_z + along_y + along_x)
        image = potential_ref[0, y] * inner - 0.5 * total
        if first:
            newer = (image - CSHIFT * inner) / EWIDTH
        else:
            newer = 2.0 / EWIDTH * (image - CSHIFT * inner) - older_ref[0, y].astype(jnp.float32)
        out_ref[0, y] = newer.astype(out_ref.dtype)


def chebyshev_step(extended, older, potential, first):
    planes = older.shape[0]
    rows_y, rows_x, bands = older.shape[1:]
    lanes = 128
    grid = (bands // lanes, planes)
    return pl.pallas_call(
        functools.partial(_step_kernel, first),
        out_shape=jax.ShapeDtypeStruct(older.shape, jnp.bfloat16),
        grid=grid,
        in_specs=[
            pl.BlockSpec((planes + 6, rows_y, rows_x, lanes), lambda j, z: (0, 0, 0, j)),
            pl.BlockSpec((1, rows_y, rows_x, lanes), lambda j, z: (z, 0, 0, j)),
            pl.BlockSpec((1, rows_y, rows_x, lanes), lambda j, z: (z, 0, 0, 0)),
        ],
        out_specs=pl.BlockSpec((1, rows_y, rows_x, lanes), lambda j, z: (z, 0, 0, j)),
    )(extended, older, potential)


def extended_2(block, sides, width):
    for axis, dim in sides:
        count = lax.axis_size(axis)
        forward = [(i, i + 1) for i in range(count - 1)]
        backward = [(target, source) for source, target in forward]
        low = lax.ppermute(
            lax.slice_in_dim(block, block.shape[dim] - width, None, axis=dim), axis, forward
        )
        high = lax.ppermute(lax.slice_in_dim(block, 0, width, axis=dim), axis, backward)
        block = jnp.concatenate([low, block, high], axis=dim)
    return block


def hamiltonian(extended, potential):
    inner = extended[3:-3]
    planes = inner.shape[0]
    rows_y = inner.shape[1]
    rows_x = inner.shape[2]
    padded_y = jnp.pad(inner, ((0, 0), (3, 3), (0, 0), (0, 0)))
    padded_x = jnp.pad(inner, ((0, 0), (0, 0), (3, 3), (0, 0)))
    total = 3.0 * COEF[0] * inner
    for distance in (1, 2, 3):
        along_z = (
            extended[3 + distance : 3 + distance + planes]
            + extended[3 - distance : 3 - distance + planes]
        )
        along_y = (
            padded_y[:, 3 + distance : 3 + distance + rows_y]
            + padded_y[:, 3 - distance : 3 - distance + rows_y]
        )
        along_x = (
            padded_x[:, :, 3 + distance : 3 + distance + rows_x]
            + padded_x[:, :, 3 - distance : 3 - distance + rows_x]
        )
        total = total + COEF[distance] * (along_z + along_y + along_x)
    return potential[:, :, :, None] * inner - 0.5 * total


def shards(waves, potential, domain_of):
    slabs = lax.axis_size("gz")
    position = lax.axis_index("gz")
    planes = waves.shape[0]
    bands = waves.shape[3]
    grid = potential.reshape(planes, NY, NX)
    owner = domain_of[position]
    below = jnp.where(position > 0, domain_of[jnp.maximum(position - 1, 0)] == owner, False).astype(
        jnp.float32
    )
    above = jnp.where(
        position < slabs - 1, domain_of[jnp.minimum(position + 1, slabs - 1)] == owner, False
    ).astype(jnp.float32)
    mask_three = jnp.concatenate(
        [
            jnp.broadcast_to(below, (3,)),
            jnp.ones((planes,), jnp.float32),
            jnp.broadcast_to(above, (3,)),
        ]
    )[:, None, None, None]

    def rimmed(field):
        return extended_2(field, (("gz", 0),), 3) * mask_three.astype(jnp.bfloat16)

    lanes = jnp.broadcast_to(grid[..., None], grid.shape + (128,))
    older = waves
    current = chebyshev_step(rimmed(waves), waves, lanes, True)
    for turn in range(DEGREE - 1):
        newer = chebyshev_step(rimmed(current), older, lanes, False)
        older, current = (current, newer)
    cells = jnp.sum((domain_of == owner).astype(jnp.float32)) * (planes * NY * NX)
    rows = current.reshape(planes * NY * NX, bands)

    def domain_total(term):
        forward = term
        backward = term
        distance = 1
        while distance < slabs:
            ahead = [(i, i + distance) for i in range(slabs - distance)]
            behind = [(i + distance, i) for i in range(slabs - distance)]
            from_low = lax.ppermute(forward, "gz", ahead)
            from_high = lax.ppermute(backward, "gz", behind)
            low_same = jnp.where(
                position >= distance,
                domain_of[jnp.maximum(position - distance, 0)] == owner,
                False,
            ).astype(jnp.float32)
            high_same = jnp.where(
                position + distance < slabs,
                domain_of[jnp.minimum(position + distance, slabs - 1)] == owner,
                False,
            ).astype(jnp.float32)
            forward = forward + low_same * from_low
            backward = backward + high_same * from_high
            distance *= 2
        return forward + backward - term

    identity = jnp.eye(PANEL, dtype=jnp.float32)
    panels = bands // PANEL
    blocks = [rows[:, p * PANEL : (p + 1) * PANEL] for p in range(panels)]
    first = blocks[0]
    cross = jnp.einsum("ca,cb->ab", first, rows, preferred_element_type=jnp.float32)
    cross = domain_total(cross) / cells
    pieces = []
    whitenings = []
    for panel in range(panels):
        block = blocks[panel]
        if panel == 0:
            gram = cross[:, :PANEL]
        else:
            if panel == 1:
                correlation = jnp.dot(
                    whitenings[0].T.astype(jnp.float32),
                    cross[:, PANEL : 2 * PANEL],
                    preferred_element_type=jnp.float32,
                )
            else:
                earlier = jnp.concatenate(pieces, axis=1)
                correlation = (
                    domain_total(
                        jnp.einsum("ca,cb->ab", earlier, block, preferred_element_type=jnp.float32)
                    )
                    / cells
                )
            earlier = jnp.concatenate(pieces, axis=1)
            block = (
                block.astype(jnp.float32)
                - jnp.dot(
                    earlier, correlation.astype(jnp.bfloat16), preferred_element_type=jnp.float32
                )
            ).astype(jnp.bfloat16)
            gram = (
                domain_total(
                    jnp.einsum("ca,cb->ab", block, block, preferred_element_type=jnp.float32)
                )
                / cells
            )
        inverse = lower_inverse(gram)
        whitening = inverse.T.astype(jnp.bfloat16)
        whitenings.append(whitening)
        pieces.append(
            jnp.dot(block, whitening, preferred_element_type=jnp.float32).astype(jnp.bfloat16)
        )
    return jnp.concatenate(pieces, axis=1).reshape(planes, NY, NX, bands)


def solution(mesh):
    return jax.shard_map(
        shards,
        mesh=mesh,
        in_specs=(P(("groups", "gz"), None, None, None), P(("groups", "gz"), None), P("groups")),
        out_specs=P(("groups", "gz"), None, None, None),
        check_vma=False,
    )
```

```python
import functools

import jax
import jax.numpy as jnp
from jax import lax
from jax.experimental import pallas as pl
from jax.experimental.pallas import tpu as pltpu
from jax.sharding import PartitionSpec as P

PANEL = 128
NX = 64
NY = 8
DOMS = 8
DEGREE = 4


COEF = (-49.0 / 18.0, 1.5, -0.15, 1.0 / 90.0)
CSHIFT = 7.0
EWIDTH = 5.0


def _lower_inverse_kernel(gram_ref, out_ref, work_ref):
    n = gram_ref.shape[0]
    work_ref[:, :n] = gram_ref[...]
    work_ref[:, n:] = (lax.broadcasted_iota(jnp.int32, (n, n), 0) == lax.broadcasted_iota(jnp.int32, (n, n), 1)).astype(jnp.float32)

    def step(k, carry):
        row = work_ref[pl.ds(k, 1), :]
        lane = lax.broadcasted_iota(jnp.int32, (1, 2 * n), 1)
        pivot = jnp.sum(jnp.where(lane == k, row, 0.0), axis=1, keepdims=True)
        scale = 1.0 / jnp.sqrt(pivot)
        scaled = row * scale
        block_rows = lax.broadcasted_iota(jnp.int32, (8, 2 * n), 0)
        block_lanes = lax.broadcasted_iota(jnp.int32, (8, n), 1)
        for start in range(0, n, 8):

            @pl.when(start + 7 >= k)
            def _():
                whole = work_ref[start : start + 8, :]
                left = whole[:, :n]
                column = (
                    jnp.sum(jnp.where(block_lanes == k, left, 0.0), axis=1, keepdims=True) * scale
                )
                place = block_rows + start
                updated = jnp.where(place > k, whole - column * scaled, whole)
                work_ref[start : start + 8, :] = jnp.where(place == k, scaled, updated)

        return carry

    lax.fori_loop(0, n, step, 0)
    out_ref[...] = work_ref[:, n:]


def lower_inverse(gram):
    n = gram.shape[0]
    return pl.pallas_call(
        _lower_inverse_kernel,
        out_shape=jax.ShapeDtypeStruct((n, n), jnp.float32),
        scratch_shapes=[pltpu.VMEM((n, 2 * n), jnp.float32)],
    )(gram)


def _step_kernel(first, extended_ref, older_ref, potential_ref, out_ref):
    z = pl.program_id(1)
    rows_y = extended_ref.shape[1]
    rows_x = extended_ref.shape[2]
    place = lax.broadcasted_iota(jnp.int32, (rows_x, extended_ref.shape[3]), 0)

    def plane(offset, y):
        return extended_ref[z + 3 + offset, y].astype(jnp.float32)

    for y in range(rows_y):
        inner = plane(0, y)
        total = 3.0 * COEF[0] * inner
        for distance in (1, 2, 3):
            along_z = plane(distance, y) + plane(-distance, y)
            up = plane(0, y + distance) if y + distance < rows_y else None
            down = plane(0, y - distance) if y - distance >= 0 else None
            if up is None:
                along_y = down
            elif down is None:
                along_y = up
            else:
                along_y = up + down
            ahead = jnp.where(place + distance < rows_x, pltpu.roll(inner, rows_x - distance, 0), 0.0)
            behind = jnp.where(place >= distance, pltpu.roll(inner, distance, 0), 0.0)
            along_x = ahead + behind
            total = total + COEF[distance] * (along_z + along_y + along_x)
        image = potential_ref[0, y] * inner - 0.5 * total
        if first:
            newer = (image - CSHIFT * inner) / EWIDTH
        else:
            newer = 2.0 / EWIDTH * (image - CSHIFT * inner) - older_ref[0, y].astype(jnp.float32)
        out_ref[0, y] = newer.astype(out_ref.dtype)


def chebyshev_step(extended, older, potential, first):
    planes = older.shape[0]
    rows_y, rows_x, bands = older.shape[1:]
    lanes = 128
    grid = (bands // lanes, planes)
    return pl.pallas_call(
        functools.partial(_step_kernel, first),
        out_shape=jax.ShapeDtypeStruct(older.shape, jnp.bfloat16),
        grid=grid,
        in_specs=[
            pl.BlockSpec((planes + 6, rows_y, rows_x, lanes), lambda j, z: (0, 0, 0, j)),
            pl.BlockSpec((1, rows_y, rows_x, lanes), lambda j, z: (z, 0, 0, j)),
            pl.BlockSpec((1, rows_y, rows_x, lanes), lambda j, z: (z, 0, 0, 0)),
        ],
        out_specs=pl.BlockSpec((1, rows_y, rows_x, lanes), lambda j, z: (z, 0, 0, j)),
    )(extended, older, potential)


def extended_2(block, sides, width):
    for axis, dim in sides:
        count = lax.axis_size(axis)
        forward = [(i, i + 1) for i in range(count - 1)]
        backward = [(target, source) for source, target in forward]
        low = lax.ppermute(
            lax.slice_in_dim(block, block.shape[dim] - width, None, axis=dim), axis, forward
        )
        high = lax.ppermute(lax.slice_in_dim(block, 0, width, axis=dim), axis, backward)
        block = jnp.concatenate([low, block, high], axis=dim)
    return block


def hamiltonian(extended, potential):
    inner = extended[3:-3]
    planes = inner.shape[0]
    rows_y = inner.shape[1]
    rows_x = inner.shape[2]
    padded_y = jnp.pad(inner, ((0, 0), (3, 3), (0, 0), (0, 0)))
    padded_x = jnp.pad(inner, ((0, 0), (0, 0), (3, 3), (0, 0)))
    total = 3.0 * COEF[0] * inner
    for distance in (1, 2, 3):
        along_z = (
            extended[3 + distance : 3 + distance + planes]
            + extended[3 - distance : 3 - distance + planes]
        )
        along_y = (
            padded_y[:, 3 + distance : 3 + distance + rows_y]
            + padded_y[:, 3 - distance : 3 - distance + rows_y]
        )
        along_x = (
            padded_x[:, :, 3 + distance : 3 + distance + rows_x]
            + padded_x[:, :, 3 - distance : 3 - distance + rows_x]
        )
        total = total + COEF[distance] * (along_z + along_y + along_x)
    return potential[:, :, :, None] * inner - 0.5 * total


def shards(waves, potential, domain_of):
    slabs = lax.axis_size("gz")
    position = lax.axis_index("gz")
    planes = waves.shape[0]
    bands = waves.shape[3]
    grid = potential.reshape(planes, NY, NX)
    owner = domain_of[position]
    below = jnp.where(position > 0, domain_of[jnp.maximum(position - 1, 0)] == owner, False).astype(
        jnp.float32
    )
    above = jnp.where(
        position < slabs - 1, domain_of[jnp.minimum(position + 1, slabs - 1)] == owner, False
    ).astype(jnp.float32)
    mask_three = jnp.concatenate(
        [
            jnp.broadcast_to(below, (3,)),
            jnp.ones((planes,), jnp.float32),
            jnp.broadcast_to(above, (3,)),
        ]
    )[:, None, None, None]

    def rimmed(field):
        return extended_2(field, (("gz", 0),), 3) * mask_three.astype(jnp.bfloat16)

    lanes = jnp.broadcast_to(grid[..., None], grid.shape + (128,))
    older = waves
    current = chebyshev_step(rimmed(waves), waves, lanes, True)
    for turn in range(DEGREE - 1):
        newer = chebyshev_step(rimmed(current), older, lanes, False)
        older, current = (current, newer)
    cells = jnp.sum((domain_of == owner).astype(jnp.float32)) * (planes * NY * NX)
    rows = current.reshape(planes * NY * NX, bands)

    def domain_total(term):
        forward = term
        backward = term
        distance = 1
        while distance < slabs:
            ahead = [(i, i + distance) for i in range(slabs - distance)]
            behind = [(i + distance, i) for i in range(slabs - distance)]
            from_low = lax.ppermute(forward, "gz", ahead)
            from_high = lax.ppermute(backward, "gz", behind)
            low_same = jnp.where(
                position >= distance,
                domain_of[jnp.maximum(position - distance, 0)] == owner,
                False,
            ).astype(jnp.float32)
            high_same = jnp.where(
                position + distance < slabs,
                domain_of[jnp.minimum(position + distance, slabs - 1)] == owner,
                False,
            ).astype(jnp.float32)
            forward = forward + low_same * from_low
            backward = backward + high_same * from_high
            distance *= 2
        return forward + backward - term

    identity = jnp.eye(PANEL, dtype=jnp.float32)
    panels = bands // PANEL
    blocks = [rows[:, p * PANEL : (p + 1) * PANEL] for p in range(panels)]
    first = blocks[0]
    cross = jnp.einsum("ca,cb->ab", first, rows, preferred_element_type=jnp.float32)
    cross = domain_total(cross) / cells
    pieces = []
    whitenings = []
    for panel in range(panels):
        block = blocks[panel]
        if panel == 0:
            gram = cross[:, :PANEL]
        else:
            if panel == 1:
                correlation = jnp.dot(
                    whitenings[0].T.astype(jnp.float32),
                    cross[:, PANEL : 2 * PANEL],
                    preferred_element_type=jnp.float32,
                )
            else:
                earlier = jnp.concatenate(pieces, axis=1)
                correlation = (
                    domain_total(
                        jnp.einsum("ca,cb->ab", earlier, block, preferred_element_type=jnp.float32)
                    )
                    / cells
                )
            earlier = jnp.concatenate(pieces, axis=1)
            block = (
                block.astype(jnp.float32)
                - jnp.dot(
                    earlier, correlation.astype(jnp.bfloat16), preferred_element_type=jnp.float32
                )
            ).astype(jnp.bfloat16)
            gram = (
                domain_total(
                    jnp.einsum("ca,cb->ab", block, block, preferred_element_type=jnp.float32)
                )
                / cells
            )
        inverse = lower_inverse(gram)
        whitening = inverse.T.astype(jnp.bfloat16)
        whitenings.append(whitening)
        pieces.append(
            jnp.dot(block, whitening, preferred_element_type=jnp.float32).astype(jnp.bfloat16)
        )
    return jnp.concatenate(pieces, axis=1).reshape(planes, NY, NX, bands)


def solution(mesh):
    return jax.shard_map(
        shards,
        mesh=mesh,
        in_specs=(P(("groups", "gz"), None, None, None), P(("groups", "gz"), None), P("groups")),
        out_specs=P(("groups", "gz"), None, None, None),
        check_vma=False,
    )
```

```python
import functools

import jax
import jax.numpy as jnp
from jax import lax
from jax.experimental import pallas as pl
from jax.experimental.pallas import tpu as pltpu
from jax.sharding import PartitionSpec as P

PANEL = 128
NX = 64
NY = 8
DOMS = 8
DEGREE = 4


COEF = (-49.0 / 18.0, 1.5, -0.15, 1.0 / 90.0)
CSHIFT = 7.0
EWIDTH = 5.0


def _lower_inverse_kernel(gram_ref, out_ref, work_ref):
    n = gram_ref.shape[0]
    work_ref[:, :n] = gram_ref[...]
    work_ref[:, n:] = (lax.broadcasted_iota(jnp.int32, (n, n), 0) == lax.broadcasted_iota(jnp.int32, (n, n), 1)).astype(jnp.float32)

    def step(k, carry):
        row = work_ref[pl.ds(k, 1), :]
        lane = lax.broadcasted_iota(jnp.int32, (1, 2 * n), 1)
        pivot = jnp.sum(jnp.where(lane == k, row, 0.0), axis=1, keepdims=True)
        scale = 1.0 / jnp.sqrt(pivot)
        scaled = row * scale
        block_rows = lax.broadcasted_iota(jnp.int32, (8, 2 * n), 0)
        block_lanes = lax.broadcasted_iota(jnp.int32, (8, n), 1)
        for start in range(0, n, 8):

            @pl.when(start + 7 >= k)
            def _():
                whole = work_ref[start : start + 8, :]
                left = whole[:, :n]
                column = (
                    jnp.sum(jnp.where(block_lanes == k, left, 0.0), axis=1, keepdims=True) * scale
                )
                place = block_rows + start
                updated = jnp.where(place > k, whole - column * scaled, whole)
                work_ref[start : start + 8, :] = jnp.where(place == k, scaled, updated)

        return carry

    lax.fori_loop(0, n, step, 0)
    out_ref[...] = work_ref[:, n:]


def lower_inverse(gram):
    n = gram.shape[0]
    return pl.pallas_call(
        _lower_inverse_kernel,
        out_shape=jax.ShapeDtypeStruct((n, n), jnp.float32),
        scratch_shapes=[pltpu.VMEM((n, 2 * n), jnp.float32)],
    )(gram)


def _step_kernel(first, extended_ref, older_low_ref, older_high_ref, low_pot_ref, high_pot_ref,
                 low_ref, high_ref):
    z = pl.program_id(1)
    half = (extended_ref.shape[0] - 6) // 2
    rows_y = extended_ref.shape[1]
    rows_x = extended_ref.shape[2]
    place = lax.broadcasted_iota(jnp.int32, (rows_x, extended_ref.shape[3]), 0)

    def one_plane(centre, older_ref, potential_ref, out_ref):
        def plane(offset, y):
            return extended_ref[centre + offset, y].astype(jnp.float32)

        for y in range(rows_y):
            inner = plane(0, y)
            total = 3.0 * COEF[0] * inner
            for distance in (1, 2, 3):
                along_z = plane(distance, y) + plane(-distance, y)
                up = plane(0, y + distance) if y + distance < rows_y else None
                down = plane(0, y - distance) if y - distance >= 0 else None
                if up is None:
                    along_y = down
                elif down is None:
                    along_y = up
                else:
                    along_y = up + down
                ahead = jnp.where(
                    place + distance < rows_x, pltpu.roll(inner, rows_x - distance, 0), 0.0
                )
                behind = jnp.where(place >= distance, pltpu.roll(inner, distance, 0), 0.0)
                along_x = ahead + behind
                total = total + COEF[distance] * (along_z + along_y + along_x)
            image = potential_ref[0, y] * inner - 0.5 * total
            if first:
                newer = (image - CSHIFT * inner) / EWIDTH
            else:
                newer = 2.0 / EWIDTH * (image - CSHIFT * inner) - older_ref[0, y].astype(
                    jnp.float32
                )
            out_ref[0, y] = newer.astype(out_ref.dtype)

    one_plane(z + 3, older_low_ref, low_pot_ref, low_ref)
    one_plane(z + 3 + half, older_high_ref, high_pot_ref, high_ref)


def chebyshev_step(extended, older_low, older_high, potential, first):
    half = (extended.shape[0] - 6) // 2
    rows_y, rows_x, bands = extended.shape[1:]
    lanes = 128
    grid = (bands // lanes, half)
    block = (1, rows_y, rows_x, lanes)
    high_shift = half if older_high.shape[0] == 2 * half else 0
    piece = jax.ShapeDtypeStruct((half, rows_y, rows_x, bands), jnp.bfloat16)
    return pl.pallas_call(
        functools.partial(_step_kernel, first),
        out_shape=(piece, piece),
        grid=grid,
        in_specs=[
            pl.BlockSpec((2 * half + 6, rows_y, rows_x, lanes), lambda j, z: (0, 0, 0, j)),
            pl.BlockSpec(block, lambda j, z: (z, 0, 0, j)),
            pl.BlockSpec(block, lambda j, z: (z + high_shift, 0, 0, j)),
            pl.BlockSpec(block, lambda j, z: (z, 0, 0, 0)),
            pl.BlockSpec(block, lambda j, z: (z + half, 0, 0, 0)),
        ],
        out_specs=(
            pl.BlockSpec(block, lambda j, z: (z, 0, 0, j)),
            pl.BlockSpec(block, lambda j, z: (z, 0, 0, j)),
        ),
    )(extended, older_low, older_high, potential, potential)


def extended_2(block, sides, width):
    for axis, dim in sides:
        count = lax.axis_size(axis)
        forward = [(i, i + 1) for i in range(count - 1)]
        backward = [(target, source) for source, target in forward]
        low = lax.ppermute(
            lax.slice_in_dim(block, block.shape[dim] - width, None, axis=dim), axis, forward
        )
        high = lax.ppermute(lax.slice_in_dim(block, 0, width, axis=dim), axis, backward)
        block = jnp.concatenate([low, block, high], axis=dim)
    return block


def hamiltonian(extended, potential):
    inner = extended[3:-3]
    planes = inner.shape[0]
    rows_y = inner.shape[1]
    rows_x = inner.shape[2]
    padded_y = jnp.pad(inner, ((0, 0), (3, 3), (0, 0), (0, 0)))
    padded_x = jnp.pad(inner, ((0, 0), (0, 0), (3, 3), (0, 0)))
    total = 3.0 * COEF[0] * inner
    for distance in (1, 2, 3):
        along_z = (
            extended[3 + distance : 3 + distance + planes]
            + extended[3 - distance : 3 - distance + planes]
        )
        along_y = (
            padded_y[:, 3 + distance : 3 + distance + rows_y]
            + padded_y[:, 3 - distance : 3 - distance + rows_y]
        )
        along_x = (
            padded_x[:, :, 3 + distance : 3 + distance + rows_x]
            + padded_x[:, :, 3 - distance : 3 - distance + rows_x]
        )
        total = total + COEF[distance] * (along_z + along_y + along_x)
    return potential[:, :, :, None] * inner - 0.5 * total


def shards(waves, potential, domain_of):
    slabs = lax.axis_size("gz")
    position = lax.axis_index("gz")
    planes = waves.shape[0]
    bands = waves.shape[3]
    grid = potential.reshape(planes, NY, NX)
    owner = domain_of[position]
    below = jnp.where(position > 0, domain_of[jnp.maximum(position - 1, 0)] == owner, False).astype(
        jnp.float32
    )
    above = jnp.where(
        position < slabs - 1, domain_of[jnp.minimum(position + 1, slabs - 1)] == owner, False
    ).astype(jnp.float32)
    mask_three = jnp.concatenate(
        [
            jnp.broadcast_to(below, (3,)),
            jnp.ones((planes,), jnp.float32),
            jnp.broadcast_to(above, (3,)),
        ]
    )[:, None, None, None]

    forward = [(i, i + 1) for i in range(slabs - 1)]
    backward = [(target, source) for source, target in forward]
    bf_below = below.astype(jnp.bfloat16)
    bf_above = above.astype(jnp.bfloat16)

    def rimmed(low, high):
        from_below = lax.ppermute(high, "gz", forward)
        from_above = lax.ppermute(low, "gz", backward)
        return jnp.concatenate([from_below * bf_below, low, high, from_above * bf_above], axis=0)

    lanes = jnp.broadcast_to(grid[..., None], grid.shape + (128,))
    half = planes // 2
    low, high = chebyshev_step(rimmed(waves[:half], waves[half:]), waves, waves, lanes, True)
    older_low, older_high = waves, waves
    for turn in range(DEGREE - 1):
        newer = chebyshev_step(rimmed(low, high), older_low, older_high, lanes, False)
        older_low, older_high = low, high
        low, high = newer
    current = jnp.concatenate([low, high], axis=0)
    cells = jnp.sum((domain_of == owner).astype(jnp.float32)) * (planes * NY * NX)
    rows = current.reshape(planes * NY * NX, bands)

    def domain_total(term):
        forward = term
        backward = term
        distance = 1
        while distance < slabs:
            ahead = [(i, i + distance) for i in range(slabs - distance)]
            behind = [(i + distance, i) for i in range(slabs - distance)]
            from_low = lax.ppermute(forward, "gz", ahead)
            from_high = lax.ppermute(backward, "gz", behind)
            low_same = jnp.where(
                position >= distance,
                domain_of[jnp.maximum(position - distance, 0)] == owner,
                False,
            ).astype(jnp.float32)
            high_same = jnp.where(
                position + distance < slabs,
                domain_of[jnp.minimum(position + distance, slabs - 1)] == owner,
                False,
            ).astype(jnp.float32)
            forward = forward + low_same * from_low
            backward = backward + high_same * from_high
            distance *= 2
        return forward + backward - term

    identity = jnp.eye(PANEL, dtype=jnp.float32)
    panels = bands // PANEL
    blocks = [rows[:, p * PANEL : (p + 1) * PANEL] for p in range(panels)]
    first = blocks[0]
    cross = jnp.einsum("ca,cb->ab", first, rows, preferred_element_type=jnp.float32)
    cross = domain_total(cross) / cells
    pieces = []
    whitenings = []
    for panel in range(panels):
        block = blocks[panel]
        if panel == 0:
            gram = cross[:, :PANEL]
        else:
            if panel == 1:
                correlation = jnp.dot(
                    whitenings[0].T.astype(jnp.float32),
                    cross[:, PANEL : 2 * PANEL],
                    preferred_element_type=jnp.float32,
                )
            else:
                earlier = jnp.concatenate(pieces, axis=1)
                correlation = (
                    domain_total(
                        jnp.einsum("ca,cb->ab", earlier, block, preferred_element_type=jnp.float32)
                    )
                    / cells
                )
            earlier = jnp.concatenate(pieces, axis=1)
            block = (
                block.astype(jnp.float32)
                - jnp.dot(
                    earlier, correlation.astype(jnp.bfloat16), preferred_element_type=jnp.float32
                )
            ).astype(jnp.bfloat16)
            gram = (
                domain_total(
                    jnp.einsum("ca,cb->ab", block, block, preferred_element_type=jnp.float32)
                )
                / cells
            )
        inverse = lower_inverse(gram)
        whitening = inverse.T.astype(jnp.bfloat16)
        whitenings.append(whitening)
        pieces.append(
            jnp.dot(block, whitening, preferred_element_type=jnp.float32).astype(jnp.bfloat16)
        )
    return jnp.concatenate(pieces, axis=1).reshape(planes, NY, NX, bands)


def solution(mesh):
    return jax.shard_map(
        shards,
        mesh=mesh,
        in_specs=(P(("groups", "gz"), None, None, None), P(("groups", "gz"), None), P("groups")),
        out_specs=P(("groups", "gz"), None, None, None),
        check_vma=False,
    )
```

```python
import functools

import jax
import jax.numpy as jnp
from jax import lax
from jax.experimental import pallas as pl
from jax.experimental.pallas import tpu as pltpu
from jax.sharding import PartitionSpec as P

PANEL = 128
NX = 64
NY = 8
DOMS = 8
DEGREE = 4


COEF = (-49.0 / 18.0, 1.5, -0.15, 1.0 / 90.0)
CSHIFT = 7.0
EWIDTH = 5.0


def _lower_inverse_kernel(gram_ref, out_ref, work_ref):
    n = gram_ref.shape[0]
    rows = lax.broadcasted_iota(jnp.int32, (n, 2 * n), 0)
    lanes = lax.broadcasted_iota(jnp.int32, (n, 2 * n), 1)
    work_ref[:, :n] = gram_ref[...]
    work_ref[:, n:] = (lax.broadcasted_iota(jnp.int32, (n, n), 0) == lax.broadcasted_iota(jnp.int32, (n, n), 1)).astype(jnp.float32)

    def step(k, carry):
        row = work_ref[pl.ds(k, 1), :]
        lane = lax.broadcasted_iota(jnp.int32, (1, 2 * n), 1)
        pivot = jnp.sum(jnp.where(lane == k, row, 0.0), axis=1, keepdims=True)
        scale = 1.0 / jnp.sqrt(pivot)
        scaled = row * scale
        whole = work_ref[...]
        left = whole[:, :n]
        column = jnp.sum(jnp.where(lanes[:, :n] == k, left, 0.0), axis=1, keepdims=True) * scale
        updated = jnp.where(rows > k, whole - column * scaled, whole)
        work_ref[...] = jnp.where(rows == k, scaled, updated)
        return carry

    lax.fori_loop(0, n, step, 0)
    out_ref[...] = work_ref[:, n:]


def lower_inverse(gram):
    n = gram.shape[0]
    return pl.pallas_call(
        _lower_inverse_kernel,
        out_shape=jax.ShapeDtypeStruct((n, n), jnp.float32),
        scratch_shapes=[pltpu.VMEM((n, 2 * n), jnp.float32)],
    )(gram)


def _step_kernel(first, extended_ref, older_low_ref, older_high_ref, low_pot_ref, high_pot_ref,
                 low_ref, high_ref):
    z = pl.program_id(1)
    half = (extended_ref.shape[0] - 6) // 2
    rows_y = extended_ref.shape[1]
    rows_x = extended_ref.shape[2]
    place = lax.broadcasted_iota(jnp.int32, (rows_x, extended_ref.shape[3]), 0)

    def one_plane(centre, older_ref, potential_ref, out_ref):
        def plane(offset, y):
            return extended_ref[centre + offset, y].astype(jnp.float32)

        for y in range(rows_y):
            inner = plane(0, y)
            total = 3.0 * COEF[0] * inner
            for distance in (1, 2, 3):
                along_z = plane(distance, y) + plane(-distance, y)
                up = plane(0, y + distance) if y + distance < rows_y else None
                down = plane(0, y - distance) if y - distance >= 0 else None
                if up is None:
                    along_y = down
                elif down is None:
                    along_y = up
                else:
                    along_y = up + down
                ahead = jnp.where(
                    place + distance < rows_x, pltpu.roll(inner, rows_x - distance, 0), 0.0
                )
                behind = jnp.where(place >= distance, pltpu.roll(inner, distance, 0), 0.0)
                along_x = ahead + behind
                total = total + COEF[distance] * (along_z + along_y + along_x)
            image = potential_ref[0, y] * inner - 0.5 * total
            if first:
                newer = (image - CSHIFT * inner) / EWIDTH
            else:
                newer = 2.0 / EWIDTH * (image - CSHIFT * inner) - older_ref[0, y].astype(
                    jnp.float32
                )
            out_ref[0, y] = newer.astype(out_ref.dtype)

    one_plane(z + 3, older_low_ref, low_pot_ref, low_ref)
    one_plane(z + 3 + half, older_high_ref, high_pot_ref, high_ref)


def chebyshev_step(extended, older_low, older_high, potential, first):
    half = (extended.shape[0] - 6) // 2
    rows_y, rows_x, bands = extended.shape[1:]
    lanes = 128
    grid = (bands // lanes, half)
    block = (1, rows_y, rows_x, lanes)
    high_shift = half if older_high.shape[0] == 2 * half else 0
    piece = jax.ShapeDtypeStruct((half, rows_y, rows_x, bands), jnp.bfloat16)
    return pl.pallas_call(
        functools.partial(_step_kernel, first),
        out_shape=(piece, piece),
        grid=grid,
        in_specs=[
            pl.BlockSpec((2 * half + 6, rows_y, rows_x, lanes), lambda j, z: (0, 0, 0, j)),
            pl.BlockSpec(block, lambda j, z: (z, 0, 0, j)),
            pl.BlockSpec(block, lambda j, z: (z + high_shift, 0, 0, j)),
            pl.BlockSpec(block, lambda j, z: (z, 0, 0, 0)),
            pl.BlockSpec(block, lambda j, z: (z + half, 0, 0, 0)),
        ],
        out_specs=(
            pl.BlockSpec(block, lambda j, z: (z, 0, 0, j)),
            pl.BlockSpec(block, lambda j, z: (z, 0, 0, j)),
        ),
    )(extended, older_low, older_high, potential, potential)


def extended_2(block, sides, width):
    for axis, dim in sides:
        count = lax.axis_size(axis)
        forward = [(i, i + 1) for i in range(count - 1)]
        backward = [(target, source) for source, target in forward]
        low = lax.ppermute(
            lax.slice_in_dim(block, block.shape[dim] - width, None, axis=dim), axis, forward
        )
        high = lax.ppermute(lax.slice_in_dim(block, 0, width, axis=dim), axis, backward)
        block = jnp.concatenate([low, block, high], axis=dim)
    return block


def hamiltonian(extended, potential):
    inner = extended[3:-3]
    planes = inner.shape[0]
    rows_y = inner.shape[1]
    rows_x = inner.shape[2]
    padded_y = jnp.pad(inner, ((0, 0), (3, 3), (0, 0), (0, 0)))
    padded_x = jnp.pad(inner, ((0, 0), (0, 0), (3, 3), (0, 0)))
    total = 3.0 * COEF[0] * inner
    for distance in (1, 2, 3):
        along_z = (
            extended[3 + distance : 3 + distance + planes]
            + extended[3 - distance : 3 - distance + planes]
        )
        along_y = (
            padded_y[:, 3 + distance : 3 + distance + rows_y]
            + padded_y[:, 3 - distance : 3 - distance + rows_y]
        )
        along_x = (
            padded_x[:, :, 3 + distance : 3 + distance + rows_x]
            + padded_x[:, :, 3 - distance : 3 - distance + rows_x]
        )
        total = total + COEF[distance] * (along_z + along_y + along_x)
    return potential[:, :, :, None] * inner - 0.5 * total


def shards(waves, potential, domain_of):
    slabs = lax.axis_size("gz")
    position = lax.axis_index("gz")
    planes = waves.shape[0]
    bands = waves.shape[3]
    grid = potential.reshape(planes, NY, NX)
    owner = domain_of[position]
    below = jnp.where(position > 0, domain_of[jnp.maximum(position - 1, 0)] == owner, False).astype(
        jnp.float32
    )
    above = jnp.where(
        position < slabs - 1, domain_of[jnp.minimum(position + 1, slabs - 1)] == owner, False
    ).astype(jnp.float32)
    mask_three = jnp.concatenate(
        [
            jnp.broadcast_to(below, (3,)),
            jnp.ones((planes,), jnp.float32),
            jnp.broadcast_to(above, (3,)),
        ]
    )[:, None, None, None]

    forward = [(i, i + 1) for i in range(slabs - 1)]
    backward = [(target, source) for source, target in forward]
    bf_below = below.astype(jnp.bfloat16)
    bf_above = above.astype(jnp.bfloat16)

    def rimmed(low, high):
        from_below = lax.ppermute(high, "gz", forward)
        from_above = lax.ppermute(low, "gz", backward)
        return jnp.concatenate([from_below * bf_below, low, high, from_above * bf_above], axis=0)

    lanes = jnp.broadcast_to(grid[..., None], grid.shape + (128,))
    half = planes // 2
    low, high = chebyshev_step(rimmed(waves[:half], waves[half:]), waves, waves, lanes, True)
    older_low, older_high = waves, waves
    for turn in range(DEGREE - 1):
        newer = chebyshev_step(rimmed(low, high), older_low, older_high, lanes, False)
        older_low, older_high = low, high
        low, high = newer
    current = jnp.concatenate([low, high], axis=0)
    cells = jnp.sum((domain_of == owner).astype(jnp.float32)) * (planes * NY * NX)
    rows = current.reshape(planes * NY * NX, bands)

    def domain_total(term):
        forward = term
        backward = term
        distance = 1
        while distance < slabs:
            ahead = [(i, i + distance) for i in range(slabs - distance)]
            behind = [(i + distance, i) for i in range(slabs - distance)]
            from_low = lax.ppermute(forward, "gz", ahead)
            from_high = lax.ppermute(backward, "gz", behind)
            low_same = jnp.where(
                position >= distance,
                domain_of[jnp.maximum(position - distance, 0)] == owner,
                False,
            ).astype(jnp.float32)
            high_same = jnp.where(
                position + distance < slabs,
                domain_of[jnp.minimum(position + distance, slabs - 1)] == owner,
                False,
            ).astype(jnp.float32)
            forward = forward + low_same * from_low
            backward = backward + high_same * from_high
            distance *= 2
        return forward + backward - term

    identity = jnp.eye(PANEL, dtype=jnp.float32)
    panels = bands // PANEL
    blocks = [rows[:, p * PANEL : (p + 1) * PANEL] for p in range(panels)]
    first = blocks[0]
    cross = jnp.einsum("ca,cb->ab", first, rows, preferred_element_type=jnp.float32)
    cross = domain_total(cross) / cells
    pieces = []
    whitenings = []
    for panel in range(panels):
        block = blocks[panel]
        if panel == 0:
            gram = cross[:, :PANEL]
        else:
            if panel == 1:
                correlation = jnp.dot(
                    whitenings[0].T.astype(jnp.float32),
                    cross[:, PANEL : 2 * PANEL],
                    preferred_element_type=jnp.float32,
                )
            else:
                earlier = jnp.concatenate(pieces, axis=1)
                correlation = (
                    domain_total(
                        jnp.einsum("ca,cb->ab", earlier, block, preferred_element_type=jnp.float32)
                    )
                    / cells
                )
            earlier = jnp.concatenate(pieces, axis=1)
            block = (
                block.astype(jnp.float32)
                - jnp.dot(
                    earlier, correlation.astype(jnp.bfloat16), preferred_element_type=jnp.float32
                )
            ).astype(jnp.bfloat16)
            gram = (
                domain_total(
                    jnp.einsum("ca,cb->ab", block, block, preferred_element_type=jnp.float32)
                )
                / cells
            )
        inverse = lower_inverse(gram)
        whitening = inverse.T.astype(jnp.bfloat16)
        whitenings.append(whitening)
        pieces.append(
            jnp.dot(block, whitening, preferred_element_type=jnp.float32).astype(jnp.bfloat16)
        )
    return jnp.concatenate(pieces, axis=1).reshape(planes, NY, NX, bands)


def solution(mesh):
    return jax.shard_map(
        shards,
        mesh=mesh,
        in_specs=(P(("groups", "gz"), None, None, None), P(("groups", "gz"), None), P("groups")),
        out_specs=P(("groups", "gz"), None, None, None),
        check_vma=False,
    )
```

```python
import functools

import jax
import jax.numpy as jnp
from jax import lax
from jax.experimental import pallas as pl
from jax.experimental.pallas import tpu as pltpu
from jax.sharding import PartitionSpec as P

PANEL = 128
NX = 64
NY = 8
DOMS = 8
DEGREE = 4


COEF = (-49.0 / 18.0, 1.5, -0.15, 1.0 / 90.0)
CSHIFT = 7.0
EWIDTH = 5.0


def _lower_inverse_kernel(gram_ref, out_ref, work_ref):
    n = gram_ref.shape[0]
    rows = lax.broadcasted_iota(jnp.int32, (n, 2 * n), 0)
    lanes = lax.broadcasted_iota(jnp.int32, (n, 2 * n), 1)
    work_ref[:, :n] = gram_ref[...]
    work_ref[:, n:] = (lax.broadcasted_iota(jnp.int32, (n, n), 0) == lax.broadcasted_iota(jnp.int32, (n, n), 1)).astype(jnp.float32)

    def step(k, carry):
        row = work_ref[pl.ds(k, 1), :]
        lane = lax.broadcasted_iota(jnp.int32, (1, 2 * n), 1)
        pivot = jnp.sum(jnp.where(lane == k, row, 0.0), axis=1, keepdims=True)
        scale = 1.0 / jnp.sqrt(pivot)
        scaled = row * scale
        whole = work_ref[...]
        left = whole[:, :n]
        column = jnp.sum(jnp.where(lanes[:, :n] == k, left, 0.0), axis=1, keepdims=True) * scale
        updated = jnp.where(rows > k, whole - column * scaled, whole)
        work_ref[...] = jnp.where(rows == k, scaled, updated)
        return carry

    lax.fori_loop(0, n, step, 0)
    out_ref[...] = work_ref[:, n:]


def lower_inverse(gram):
    n = gram.shape[0]
    return pl.pallas_call(
        _lower_inverse_kernel,
        out_shape=jax.ShapeDtypeStruct((n, n), jnp.float32),
        scratch_shapes=[pltpu.VMEM((n, 2 * n), jnp.float32)],
    )(gram)


def _step_kernel(first, extended_ref, older_low_ref, older_high_ref, low_pot_ref, high_pot_ref,
                 low_ref, high_ref):
    z = pl.program_id(1)
    half = (extended_ref.shape[0] - 6) // 2
    rows_y = extended_ref.shape[1]
    rows_x = extended_ref.shape[2]
    place = lax.broadcasted_iota(jnp.int32, (rows_x, extended_ref.shape[3]), 0)

    def one_plane(centre, older_ref, potential_ref, out_ref):
        def plane(offset, y):
            return extended_ref[centre + offset, y].astype(jnp.float32)

        for y in range(rows_y):
            inner = plane(0, y)
            total = 3.0 * COEF[0] * inner
            for distance in (1, 2, 3):
                along_z = plane(distance, y) + plane(-distance, y)
                up = plane(0, y + distance) if y + distance < rows_y else None
                down = plane(0, y - distance) if y - distance >= 0 else None
                if up is None:
                    along_y = down
                elif down is None:
                    along_y = up
                else:
                    along_y = up + down
                ahead = jnp.where(
                    place + distance < rows_x, pltpu.roll(inner, rows_x - distance, 0), 0.0
                )
                behind = jnp.where(place >= distance, pltpu.roll(inner, distance, 0), 0.0)
                along_x = ahead + behind
                total = total + COEF[distance] * (along_z + along_y + along_x)
            image = potential_ref[0, y] * inner - 0.5 * total
            if first:
                newer = (image - CSHIFT * inner) / EWIDTH
            else:
                newer = 2.0 / EWIDTH * (image - CSHIFT * inner) - older_ref[0, y].astype(
                    jnp.float32
                )
            out_ref[0, y] = newer.astype(out_ref.dtype)

    one_plane(z + 3, older_low_ref, low_pot_ref, low_ref)
    one_plane(z + 3 + half, older_high_ref, high_pot_ref, high_ref)


def chebyshev_step(extended, older_low, older_high, potential, first):
    half = (extended.shape[0] - 6) // 2
    rows_y, rows_x, bands = extended.shape[1:]
    lanes = 128
    grid = (bands // lanes, half)
    block = (1, rows_y, rows_x, lanes)
    high_shift = half if older_high.shape[0] == 2 * half else 0
    piece = jax.ShapeDtypeStruct((half, rows_y, rows_x, bands), jnp.bfloat16)
    return pl.pallas_call(
        functools.partial(_step_kernel, first),
        out_shape=(piece, piece),
        grid=grid,
        in_specs=[
            pl.BlockSpec((2 * half + 6, rows_y, rows_x, lanes), lambda j, z: (0, 0, 0, j)),
            pl.BlockSpec(block, lambda j, z: (z, 0, 0, j)),
            pl.BlockSpec(block, lambda j, z: (z + high_shift, 0, 0, j)),
            pl.BlockSpec(block, lambda j, z: (z, 0, 0, 0)),
            pl.BlockSpec(block, lambda j, z: (z + half, 0, 0, 0)),
        ],
        out_specs=(
            pl.BlockSpec(block, lambda j, z: (z, 0, 0, j)),
            pl.BlockSpec(block, lambda j, z: (z, 0, 0, j)),
        ),
    )(extended, older_low, older_high, potential, potential)


def extended_2(block, sides, width):
    for axis, dim in sides:
        count = lax.axis_size(axis)
        forward = [(i, i + 1) for i in range(count - 1)]
        backward = [(target, source) for source, target in forward]
        low = lax.ppermute(
            lax.slice_in_dim(block, block.shape[dim] - width, None, axis=dim), axis, forward
        )
        high = lax.ppermute(lax.slice_in_dim(block, 0, width, axis=dim), axis, backward)
        block = jnp.concatenate([low, block, high], axis=dim)
    return block


def hamiltonian(extended, potential):
    inner = extended[3:-3]
    planes = inner.shape[0]
    rows_y = inner.shape[1]
    rows_x = inner.shape[2]
    padded_y = jnp.pad(inner, ((0, 0), (3, 3), (0, 0), (0, 0)))
    padded_x = jnp.pad(inner, ((0, 0), (0, 0), (3, 3), (0, 0)))
    total = 3.0 * COEF[0] * inner
    for distance in (1, 2, 3):
        along_z = (
            extended[3 + distance : 3 + distance + planes]
            + extended[3 - distance : 3 - distance + planes]
        )
        along_y = (
            padded_y[:, 3 + distance : 3 + distance + rows_y]
            + padded_y[:, 3 - distance : 3 - distance + rows_y]
        )
        along_x = (
            padded_x[:, :, 3 + distance : 3 + distance + rows_x]
            + padded_x[:, :, 3 - distance : 3 - distance + rows_x]
        )
        total = total + COEF[distance] * (along_z + along_y + along_x)
    return potential[:, :, :, None] * inner - 0.5 * total


def shards(waves, potential, domain_of):
    slabs = lax.axis_size("gz")
    position = lax.axis_index("gz")
    planes = waves.shape[0]

    def shifted(field, distance):
        step = abs(distance)
        pairs = [(i, i + step) for i in range(slabs - step)]
        if distance < 0:
            pairs = [(target, source) for source, target in pairs]
        first = [(s, t) for s, t in pairs if (min(s, t) // step) % 2 == 0]
        second = [(s, t) for s, t in pairs if (min(s, t) // step) % 2 == 1]
        got = lax.ppermute(field, "gz", first)
        if not second:
            return got
        other = lax.ppermute(field, "gz", second)
        table = [0] * slabs
        for s, t in second:
            table[t] = 1
        late = jnp.asarray(table, jnp.int32)[position] == 1
        return jnp.where(late, other, got)
    bands = waves.shape[3]
    grid = potential.reshape(planes, NY, NX)
    owner = domain_of[position]
    below = jnp.where(position > 0, domain_of[jnp.maximum(position - 1, 0)] == owner, False).astype(
        jnp.float32
    )
    above = jnp.where(
        position < slabs - 1, domain_of[jnp.minimum(position + 1, slabs - 1)] == owner, False
    ).astype(jnp.float32)
    mask_three = jnp.concatenate(
        [
            jnp.broadcast_to(below, (3,)),
            jnp.ones((planes,), jnp.float32),
            jnp.broadcast_to(above, (3,)),
        ]
    )[:, None, None, None]

    bf_below = below.astype(jnp.bfloat16)
    bf_above = above.astype(jnp.bfloat16)

    def rimmed(low, high):
        from_below = shifted(high, 1)
        from_above = shifted(low, -1)
        return jnp.concatenate([from_below * bf_below, low, high, from_above * bf_above], axis=0)

    lanes = jnp.broadcast_to(grid[..., None], grid.shape + (128,))
    half = planes // 2
    low, high = chebyshev_step(rimmed(waves[:half], waves[half:]), waves, waves, lanes, True)
    older_low, older_high = waves, waves
    for turn in range(DEGREE - 1):
        newer = chebyshev_step(rimmed(low, high), older_low, older_high, lanes, False)
        older_low, older_high = low, high
        low, high = newer
    current = jnp.concatenate([low, high], axis=0)
    cells = jnp.sum((domain_of == owner).astype(jnp.float32)) * (planes * NY * NX)
    rows = current.reshape(planes * NY * NX, bands)

    def domain_total(term):
        forward = term
        backward = term
        distance = 1
        while distance < slabs:
            from_low = shifted(forward, distance)
            from_high = shifted(backward, -distance)
            low_same = jnp.where(
                position >= distance,
                domain_of[jnp.maximum(position - distance, 0)] == owner,
                False,
            ).astype(jnp.float32)
            high_same = jnp.where(
                position + distance < slabs,
                domain_of[jnp.minimum(position + distance, slabs - 1)] == owner,
                False,
            ).astype(jnp.float32)
            forward = forward + low_same * from_low
            backward = backward + high_same * from_high
            distance *= 2
        return forward + backward - term

    identity = jnp.eye(PANEL, dtype=jnp.float32)
    panels = bands // PANEL
    blocks = [rows[:, p * PANEL : (p + 1) * PANEL] for p in range(panels)]
    first = blocks[0]
    cross = jnp.einsum("ca,cb->ab", first, rows, preferred_element_type=jnp.float32)
    cross = domain_total(cross) / cells
    pieces = []
    whitenings = []
    for panel in range(panels):
        block = blocks[panel]
        if panel == 0:
            gram = cross[:, :PANEL]
        else:
            if panel == 1:
                correlation = jnp.dot(
                    whitenings[0].T.astype(jnp.float32),
                    cross[:, PANEL : 2 * PANEL],
                    preferred_element_type=jnp.float32,
                )
            else:
                earlier = jnp.concatenate(pieces, axis=1)
                correlation = (
                    domain_total(
                        jnp.einsum("ca,cb->ab", earlier, block, preferred_element_type=jnp.float32)
                    )
                    / cells
                )
            earlier = jnp.concatenate(pieces, axis=1)
            block = (
                block.astype(jnp.float32)
                - jnp.dot(
                    earlier, correlation.astype(jnp.bfloat16), preferred_element_type=jnp.float32
                )
            ).astype(jnp.bfloat16)
            gram = (
                domain_total(
                    jnp.einsum("ca,cb->ab", block, block, preferred_element_type=jnp.float32)
                )
                / cells
            )
        inverse = lower_inverse(gram)
        whitening = inverse.T.astype(jnp.bfloat16)
        whitenings.append(whitening)
        pieces.append(
            jnp.dot(block, whitening, preferred_element_type=jnp.float32).astype(jnp.bfloat16)
        )
    return jnp.concatenate(pieces, axis=1).reshape(planes, NY, NX, bands)


def solution(mesh):
    return jax.shard_map(
        shards,
        mesh=mesh,
        in_specs=(P(("groups", "gz"), None, None, None), P(("groups", "gz"), None), P("groups")),
        out_specs=P(("groups", "gz"), None, None, None),
        check_vma=False,
    )
```

```python
import functools

import jax
import jax.numpy as jnp
from jax import lax
from jax.experimental import pallas as pl
from jax.experimental.pallas import tpu as pltpu
from jax.sharding import PartitionSpec as P

PANEL = 128
NX = 64
NY = 8
DOMS = 8
DEGREE = 4


COEF = (-49.0 / 18.0, 1.5, -0.15, 1.0 / 90.0)
CSHIFT = 7.0
EWIDTH = 5.0


def _lower_inverse_kernel(gram_ref, out_ref, work_ref):
    n = gram_ref.shape[0]
    rows = lax.broadcasted_iota(jnp.int32, (n, 2 * n), 0)
    lanes = lax.broadcasted_iota(jnp.int32, (n, 2 * n), 1)
    work_ref[:, :n] = gram_ref[...]
    work_ref[:, n:] = (lax.broadcasted_iota(jnp.int32, (n, n), 0) == lax.broadcasted_iota(jnp.int32, (n, n), 1)).astype(jnp.float32)

    def step(k, carry):
        row = work_ref[pl.ds(k, 1), :]
        lane = lax.broadcasted_iota(jnp.int32, (1, 2 * n), 1)
        pivot = jnp.sum(jnp.where(lane == k, row, 0.0), axis=1, keepdims=True)
        scale = 1.0 / jnp.sqrt(pivot)
        scaled = row * scale
        whole = work_ref[...]
        left = whole[:, :n]
        column = jnp.sum(jnp.where(lanes[:, :n] == k, left, 0.0), axis=1, keepdims=True) * scale
        updated = jnp.where(rows > k, whole - column * scaled, whole)
        work_ref[...] = jnp.where(rows == k, scaled, updated)
        return carry

    lax.fori_loop(0, n, step, 0)
    out_ref[...] = work_ref[:, n:]


def lower_inverse(gram):
    n = gram.shape[0]
    return pl.pallas_call(
        _lower_inverse_kernel,
        out_shape=jax.ShapeDtypeStruct((n, n), jnp.float32),
        scratch_shapes=[pltpu.VMEM((n, 2 * n), jnp.float32)],
    )(gram)


def _step_kernel(first, below_ref, low_ref, high_ref, above_ref, older_low_ref, older_high_ref,
                 low_pot_ref, high_pot_ref, out_low_ref, out_high_ref):
    half = low_ref.shape[0]
    rows_y = low_ref.shape[1]
    rows_x = low_ref.shape[2]
    place = lax.broadcasted_iota(jnp.int32, (rows_x, low_ref.shape[3]), 0)
    sources = (below_ref, low_ref, high_ref, above_ref)

    def plane(index, y):
        return sources[index // half][index % half, y].astype(jnp.float32)

    for centre in range(half, 3 * half):
        own = centre - half
        older_ref = older_low_ref if own < half else older_high_ref
        potential_ref = low_pot_ref if own < half else high_pot_ref
        out_ref = out_low_ref if own < half else out_high_ref
        local = own % half
        for y in range(rows_y):
            inner = plane(centre, y)
            total = 3.0 * COEF[0] * inner
            for distance in (1, 2, 3):
                along_z = plane(centre + distance, y) + plane(centre - distance, y)
                up = plane(centre, y + distance) if y + distance < rows_y else None
                down = plane(centre, y - distance) if y - distance >= 0 else None
                if up is None:
                    along_y = down
                elif down is None:
                    along_y = up
                else:
                    along_y = up + down
                ahead = jnp.where(
                    place + distance < rows_x, pltpu.roll(inner, rows_x - distance, 0), 0.0
                )
                behind = jnp.where(place >= distance, pltpu.roll(inner, distance, 0), 0.0)
                along_x = ahead + behind
                total = total + COEF[distance] * (along_z + along_y + along_x)
            image = potential_ref[local, y] * inner - 0.5 * total
            if first:
                newer = (image - CSHIFT * inner) / EWIDTH
            else:
                newer = 2.0 / EWIDTH * (image - CSHIFT * inner) - older_ref[local, y].astype(
                    jnp.float32
                )
            out_ref[local, y] = newer.astype(out_ref.dtype)


def chebyshev_step(below, low, high, above, older_low, older_high, potential, first):
    half, rows_y, rows_x, bands = low.shape
    lanes = 128
    block = (half, rows_y, rows_x, lanes)

    def spec(array, part):
        shift = part if array.shape[0] == 2 * half else 0
        return pl.BlockSpec(block, lambda j: (shift, 0, 0, j))

    piece = jax.ShapeDtypeStruct((half, rows_y, rows_x, bands), jnp.bfloat16)
    return pl.pallas_call(
        functools.partial(_step_kernel, first),
        out_shape=(piece, piece),
        grid=(bands // lanes,),
        in_specs=[
            spec(below, 0),
            spec(low, 0),
            spec(high, 0),
            spec(above, 0),
            spec(older_low, 0),
            spec(older_high, 1),
            pl.BlockSpec(block, lambda j: (0, 0, 0, 0)),
            pl.BlockSpec(block, lambda j: (1, 0, 0, 0)),
        ],
        out_specs=(
            pl.BlockSpec(block, lambda j: (0, 0, 0, j)),
            pl.BlockSpec(block, lambda j: (0, 0, 0, j)),
        ),
    )(below, low, high, above, older_low, older_high, potential, potential)


def extended_2(block, sides, width):
    for axis, dim in sides:
        count = lax.axis_size(axis)
        forward = [(i, i + 1) for i in range(count - 1)]
        backward = [(target, source) for source, target in forward]
        low = lax.ppermute(
            lax.slice_in_dim(block, block.shape[dim] - width, None, axis=dim), axis, forward
        )
        high = lax.ppermute(lax.slice_in_dim(block, 0, width, axis=dim), axis, backward)
        block = jnp.concatenate([low, block, high], axis=dim)
    return block


def hamiltonian(extended, potential):
    inner = extended[3:-3]
    planes = inner.shape[0]
    rows_y = inner.shape[1]
    rows_x = inner.shape[2]
    padded_y = jnp.pad(inner, ((0, 0), (3, 3), (0, 0), (0, 0)))
    padded_x = jnp.pad(inner, ((0, 0), (0, 0), (3, 3), (0, 0)))
    total = 3.0 * COEF[0] * inner
    for distance in (1, 2, 3):
        along_z = (
            extended[3 + distance : 3 + distance + planes]
            + extended[3 - distance : 3 - distance + planes]
        )
        along_y = (
            padded_y[:, 3 + distance : 3 + distance + rows_y]
            + padded_y[:, 3 - distance : 3 - distance + rows_y]
        )
        along_x = (
            padded_x[:, :, 3 + distance : 3 + distance + rows_x]
            + padded_x[:, :, 3 - distance : 3 - distance + rows_x]
        )
        total = total + COEF[distance] * (along_z + along_y + along_x)
    return potential[:, :, :, None] * inner - 0.5 * total


def shards(waves, potential, domain_of):
    slabs = lax.axis_size("gz")
    position = lax.axis_index("gz")
    planes = waves.shape[0]
    bands = waves.shape[3]
    grid = potential.reshape(planes, NY, NX)
    owner = domain_of[position]
    below = jnp.where(position > 0, domain_of[jnp.maximum(position - 1, 0)] == owner, False).astype(
        jnp.float32
    )
    above = jnp.where(
        position < slabs - 1, domain_of[jnp.minimum(position + 1, slabs - 1)] == owner, False
    ).astype(jnp.float32)
    mask_three = jnp.concatenate(
        [
            jnp.broadcast_to(below, (3,)),
            jnp.ones((planes,), jnp.float32),
            jnp.broadcast_to(above, (3,)),
        ]
    )[:, None, None, None]

    forward = [(i, i + 1) for i in range(slabs - 1)]
    backward = [(target, source) for source, target in forward]
    bf_below = below.astype(jnp.bfloat16)
    bf_above = above.astype(jnp.bfloat16)

    def rimmed(low, high):
        from_below = lax.ppermute(high, "gz", forward)
        from_above = lax.ppermute(low, "gz", backward)
        return from_below * bf_below, from_above * bf_above

    lanes = jnp.broadcast_to(grid[..., None], grid.shape + (128,))
    half = planes // 2
    low, high = waves[:half], waves[half:]
    from_below, from_above = rimmed(low, high)
    low, high = chebyshev_step(from_below, low, high, from_above, waves, waves, lanes, True)
    older_low, older_high = waves, waves
    for turn in range(DEGREE - 1):
        from_below, from_above = rimmed(low, high)
        newer = chebyshev_step(from_below, low, high, from_above, older_low, older_high, lanes, False)
        older_low, older_high = low, high
        low, high = newer
    current = jnp.concatenate([low, high], axis=0)
    cells = jnp.sum((domain_of == owner).astype(jnp.float32)) * (planes * NY * NX)
    rows = current.reshape(planes * NY * NX, bands)

    def domain_total(term):
        forward = term
        backward = term
        distance = 1
        while distance < slabs:
            ahead = [(i, i + distance) for i in range(slabs - distance)]
            behind = [(i + distance, i) for i in range(slabs - distance)]
            from_low = lax.ppermute(forward, "gz", ahead)
            from_high = lax.ppermute(backward, "gz", behind)
            low_same = jnp.where(
                position >= distance,
                domain_of[jnp.maximum(position - distance, 0)] == owner,
                False,
            ).astype(jnp.float32)
            high_same = jnp.where(
                position + distance < slabs,
                domain_of[jnp.minimum(position + distance, slabs - 1)] == owner,
                False,
            ).astype(jnp.float32)
            forward = forward + low_same * from_low
            backward = backward + high_same * from_high
            distance *= 2
        return forward + backward - term

    identity = jnp.eye(PANEL, dtype=jnp.float32)
    panels = bands // PANEL
    blocks = [rows[:, p * PANEL : (p + 1) * PANEL] for p in range(panels)]
    first = blocks[0]
    cross = jnp.einsum("ca,cb->ab", first, rows, preferred_element_type=jnp.float32)
    cross = domain_total(cross) / cells
    pieces = []
    whitenings = []
    for panel in range(panels):
        block = blocks[panel]
        if panel == 0:
            gram = cross[:, :PANEL]
        else:
            if panel == 1:
                correlation = jnp.dot(
                    whitenings[0].T.astype(jnp.float32),
                    cross[:, PANEL : 2 * PANEL],
                    preferred_element_type=jnp.float32,
                )
            else:
                earlier = jnp.concatenate(pieces, axis=1)
                correlation = (
                    domain_total(
                        jnp.einsum("ca,cb->ab", earlier, block, preferred_element_type=jnp.float32)
                    )
                    / cells
                )
            earlier = jnp.concatenate(pieces, axis=1)
            block = (
                block.astype(jnp.float32)
                - jnp.dot(
                    earlier, correlation.astype(jnp.bfloat16), preferred_element_type=jnp.float32
                )
            ).astype(jnp.bfloat16)
            gram = (
                domain_total(
                    jnp.einsum("ca,cb->ab", block, block, preferred_element_type=jnp.float32)
                )
                / cells
            )
        inverse = lower_inverse(gram)
        whitening = inverse.T.astype(jnp.bfloat16)
        whitenings.append(whitening)
        pieces.append(
            jnp.dot(block, whitening, preferred_element_type=jnp.float32).astype(jnp.bfloat16)
        )
    return jnp.concatenate(pieces, axis=1).reshape(planes, NY, NX, bands)


def solution(mesh):
    return jax.shard_map(
        shards,
        mesh=mesh,
        in_specs=(P(("groups", "gz"), None, None, None), P(("groups", "gz"), None), P("groups")),
        out_specs=P(("groups", "gz"), None, None, None),
        check_vma=False,
    )
```

```python
import functools

import jax
import jax.numpy as jnp
from jax import lax
from jax.experimental import pallas as pl
from jax.experimental.pallas import tpu as pltpu
from jax.sharding import PartitionSpec as P

PANEL = 128
NX = 64
NY = 8
DOMS = 8
DEGREE = 4


COEF = (-49.0 / 18.0, 1.5, -0.15, 1.0 / 90.0)
CSHIFT = 7.0
EWIDTH = 5.0


def _lower_inverse_kernel(gram_ref, out_ref, work_ref):
    n = gram_ref.shape[0]
    rows = lax.broadcasted_iota(jnp.int32, (n, 2 * n), 0)
    lanes = lax.broadcasted_iota(jnp.int32, (n, 2 * n), 1)
    work_ref[:, :n] = gram_ref[...]
    work_ref[:, n:] = (lax.broadcasted_iota(jnp.int32, (n, n), 0) == lax.broadcasted_iota(jnp.int32, (n, n), 1)).astype(jnp.float32)

    def step(k, carry):
        row = work_ref[pl.ds(k, 1), :]
        lane = lax.broadcasted_iota(jnp.int32, (1, 2 * n), 1)
        pivot = jnp.sum(jnp.where(lane == k, row, 0.0), axis=1, keepdims=True)
        scale = 1.0 / jnp.sqrt(pivot)
        scaled = row * scale
        whole = work_ref[...]
        left = whole[:, :n]
        column = jnp.sum(jnp.where(lanes[:, :n] == k, left, 0.0), axis=1, keepdims=True) * scale
        updated = jnp.where(rows > k, whole - column * scaled, whole)
        work_ref[...] = jnp.where(rows == k, scaled, updated)
        return carry

    lax.fori_loop(0, n, step, 0)
    out_ref[...] = work_ref[:, n:]


def lower_inverse(gram):
    n = gram.shape[0]
    return pl.pallas_call(
        _lower_inverse_kernel,
        out_shape=jax.ShapeDtypeStruct((n, n), jnp.float32),
        scratch_shapes=[pltpu.VMEM((n, 2 * n), jnp.float32)],
    )(gram)


def _step_kernel(first, below_ref, low_ref, high_ref, above_ref, older_low_ref, older_high_ref,
                 low_pot_ref, high_pot_ref, out_low_ref, out_high_ref):
    half = low_ref.shape[0]
    rows_y = low_ref.shape[1]
    rows_x = low_ref.shape[2]
    place = lax.broadcasted_iota(jnp.int32, (rows_x, low_ref.shape[3]), 0)
    sources = (below_ref, low_ref, high_ref, above_ref)

    def plane(index, y):
        return sources[index // half][index % half, y].astype(jnp.float32)

    for centre in range(half, 3 * half):
        own = centre - half
        older_ref = older_low_ref if own < half else older_high_ref
        potential_ref = low_pot_ref if own < half else high_pot_ref
        out_ref = out_low_ref if own < half else out_high_ref
        local = own % half
        for y in range(rows_y):
            inner = plane(centre, y)
            total = 3.0 * COEF[0] * inner
            for distance in (1, 2, 3):
                along_z = plane(centre + distance, y) + plane(centre - distance, y)
                up = plane(centre, y + distance) if y + distance < rows_y else None
                down = plane(centre, y - distance) if y - distance >= 0 else None
                if up is None:
                    along_y = down
                elif down is None:
                    along_y = up
                else:
                    along_y = up + down
                ahead = jnp.where(
                    place + distance < rows_x, pltpu.roll(inner, rows_x - distance, 0), 0.0
                )
                behind = jnp.where(place >= distance, pltpu.roll(inner, distance, 0), 0.0)
                along_x = ahead + behind
                total = total + COEF[distance] * (along_z + along_y + along_x)
            image = potential_ref[local, y] * inner - 0.5 * total
            if first:
                newer = (image - CSHIFT * inner) / EWIDTH
            else:
                newer = 2.0 / EWIDTH * (image - CSHIFT * inner) - older_ref[local, y].astype(
                    jnp.float32
                )
            out_ref[local, y] = newer.astype(out_ref.dtype)


def chebyshev_step(below, low, high, above, older_low, older_high, potential, first):
    half, rows_y, rows_x, bands = low.shape
    lanes = 128
    block = (half, rows_y, rows_x, lanes)

    def spec(array, part):
        shift = part if array.shape[0] == 2 * half else 0
        return pl.BlockSpec(block, lambda j: (shift, 0, 0, j))

    piece = jax.ShapeDtypeStruct((half, rows_y, rows_x, bands), jnp.bfloat16)
    return pl.pallas_call(
        functools.partial(_step_kernel, first),
        out_shape=(piece, piece),
        grid=(bands // lanes,),
        in_specs=[
            spec(below, 0),
            spec(low, 0),
            spec(high, 0),
            spec(above, 0),
            spec(older_low, 0),
            spec(older_high, 1),
            pl.BlockSpec(block, lambda j: (0, 0, 0, 0)),
            pl.BlockSpec(block, lambda j: (1, 0, 0, 0)),
        ],
        out_specs=(
            pl.BlockSpec(block, lambda j: (0, 0, 0, j)),
            pl.BlockSpec(block, lambda j: (0, 0, 0, j)),
        ),
    )(below, low, high, above, older_low, older_high, potential, potential)


def extended_2(block, sides, width):
    for axis, dim in sides:
        count = lax.axis_size(axis)
        forward = [(i, i + 1) for i in range(count - 1)]
        backward = [(target, source) for source, target in forward]
        low = lax.ppermute(
            lax.slice_in_dim(block, block.shape[dim] - width, None, axis=dim), axis, forward
        )
        high = lax.ppermute(lax.slice_in_dim(block, 0, width, axis=dim), axis, backward)
        block = jnp.concatenate([low, block, high], axis=dim)
    return block


def hamiltonian(extended, potential):
    inner = extended[3:-3]
    planes = inner.shape[0]
    rows_y = inner.shape[1]
    rows_x = inner.shape[2]
    padded_y = jnp.pad(inner, ((0, 0), (3, 3), (0, 0), (0, 0)))
    padded_x = jnp.pad(inner, ((0, 0), (0, 0), (3, 3), (0, 0)))
    total = 3.0 * COEF[0] * inner
    for distance in (1, 2, 3):
        along_z = (
            extended[3 + distance : 3 + distance + planes]
            + extended[3 - distance : 3 - distance + planes]
        )
        along_y = (
            padded_y[:, 3 + distance : 3 + distance + rows_y]
            + padded_y[:, 3 - distance : 3 - distance + rows_y]
        )
        along_x = (
            padded_x[:, :, 3 + distance : 3 + distance + rows_x]
            + padded_x[:, :, 3 - distance : 3 - distance + rows_x]
        )
        total = total + COEF[distance] * (along_z + along_y + along_x)
    return potential[:, :, :, None] * inner - 0.5 * total


def shards(waves, potential, domain_of):
    slabs = lax.axis_size("gz")
    position = lax.axis_index("gz")
    planes = waves.shape[0]
    bands = waves.shape[3]
    grid = potential.reshape(planes, NY, NX)
    owner = domain_of[position]
    below = jnp.where(position > 0, domain_of[jnp.maximum(position - 1, 0)] == owner, False).astype(
        jnp.float32
    )
    above = jnp.where(
        position < slabs - 1, domain_of[jnp.minimum(position + 1, slabs - 1)] == owner, False
    ).astype(jnp.float32)
    mask_three = jnp.concatenate(
        [
            jnp.broadcast_to(below, (3,)),
            jnp.ones((planes,), jnp.float32),
            jnp.broadcast_to(above, (3,)),
        ]
    )[:, None, None, None]

    forward = [(i, i + 1) for i in range(slabs - 1)]
    backward = [(target, source) for source, target in forward]
    bf_below = below.astype(jnp.bfloat16)
    bf_above = above.astype(jnp.bfloat16)

    def rimmed(low, high):
        from_below = jnp.concatenate(
            [lax.ppermute(high[k : k + 1], "gz", forward) for k in range(high.shape[0])], axis=0
        )
        from_above = jnp.concatenate(
            [lax.ppermute(low[k : k + 1], "gz", backward) for k in range(low.shape[0])], axis=0
        )
        return from_below * bf_below, from_above * bf_above

    lanes = jnp.broadcast_to(grid[..., None], grid.shape + (128,))
    half = planes // 2
    low, high = waves[:half], waves[half:]
    from_below, from_above = rimmed(low, high)
    low, high = chebyshev_step(from_below, low, high, from_above, waves, waves, lanes, True)
    older_low, older_high = waves, waves
    for turn in range(DEGREE - 1):
        from_below, from_above = rimmed(low, high)
        newer = chebyshev_step(from_below, low, high, from_above, older_low, older_high, lanes, False)
        older_low, older_high = low, high
        low, high = newer
    current = jnp.concatenate([low, high], axis=0)
    cells = jnp.sum((domain_of == owner).astype(jnp.float32)) * (planes * NY * NX)
    rows = current.reshape(planes * NY * NX, bands)

    def domain_total(term):
        forward = term
        backward = term
        distance = 1
        while distance < slabs:
            ahead = [(i, i + distance) for i in range(slabs - distance)]
            behind = [(i + distance, i) for i in range(slabs - distance)]
            from_low = lax.ppermute(forward, "gz", ahead)
            from_high = lax.ppermute(backward, "gz", behind)
            low_same = jnp.where(
                position >= distance,
                domain_of[jnp.maximum(position - distance, 0)] == owner,
                False,
            ).astype(jnp.float32)
            high_same = jnp.where(
                position + distance < slabs,
                domain_of[jnp.minimum(position + distance, slabs - 1)] == owner,
                False,
            ).astype(jnp.float32)
            forward = forward + low_same * from_low
            backward = backward + high_same * from_high
            distance *= 2
        return forward + backward - term

    identity = jnp.eye(PANEL, dtype=jnp.float32)
    panels = bands // PANEL
    blocks = [rows[:, p * PANEL : (p + 1) * PANEL] for p in range(panels)]
    first = blocks[0]
    cross = jnp.einsum("ca,cb->ab", first, rows, preferred_element_type=jnp.float32)
    cross = domain_total(cross) / cells
    pieces = []
    whitenings = []
    for panel in range(panels):
        block = blocks[panel]
        if panel == 0:
            gram = cross[:, :PANEL]
        else:
            if panel == 1:
                correlation = jnp.dot(
                    whitenings[0].T.astype(jnp.float32),
                    cross[:, PANEL : 2 * PANEL],
                    preferred_element_type=jnp.float32,
                )
            else:
                earlier = jnp.concatenate(pieces, axis=1)
                correlation = (
                    domain_total(
                        jnp.einsum("ca,cb->ab", earlier, block, preferred_element_type=jnp.float32)
                    )
                    / cells
                )
            earlier = jnp.concatenate(pieces, axis=1)
            block = (
                block.astype(jnp.float32)
                - jnp.dot(
                    earlier, correlation.astype(jnp.bfloat16), preferred_element_type=jnp.float32
                )
            ).astype(jnp.bfloat16)
            gram = (
                domain_total(
                    jnp.einsum("ca,cb->ab", block, block, preferred_element_type=jnp.float32)
                )
                / cells
            )
        inverse = lower_inverse(gram)
        whitening = inverse.T.astype(jnp.bfloat16)
        whitenings.append(whitening)
        pieces.append(
            jnp.dot(block, whitening, preferred_element_type=jnp.float32).astype(jnp.bfloat16)
        )
    return jnp.concatenate(pieces, axis=1).reshape(planes, NY, NX, bands)


def solution(mesh):
    return jax.shard_map(
        shards,
        mesh=mesh,
        in_specs=(P(("groups", "gz"), None, None, None), P(("groups", "gz"), None), P("groups")),
        out_specs=P(("groups", "gz"), None, None, None),
        check_vma=False,
    )
```

```python
import functools

import jax
import jax.numpy as jnp
from jax import lax
from jax.experimental import pallas as pl
from jax.experimental.pallas import tpu as pltpu
from jax.sharding import PartitionSpec as P

PANEL = 128
NX = 64
NY = 8
DOMS = 8
DEGREE = 4


COEF = (-49.0 / 18.0, 1.5, -0.15, 1.0 / 90.0)
CSHIFT = 7.0
EWIDTH = 5.0


def _lower_inverse_kernel(gram_ref, out_ref, work_ref):
    n = gram_ref.shape[0]
    rows = lax.broadcasted_iota(jnp.int32, (n, 2 * n), 0)
    lanes = lax.broadcasted_iota(jnp.int32, (n, 2 * n), 1)
    work_ref[:, :n] = gram_ref[...]
    work_ref[:, n:] = (lax.broadcasted_iota(jnp.int32, (n, n), 0) == lax.broadcasted_iota(jnp.int32, (n, n), 1)).astype(jnp.float32)

    def step(k, carry):
        row = work_ref[pl.ds(k, 1), :]
        lane = lax.broadcasted_iota(jnp.int32, (1, 2 * n), 1)
        pivot = jnp.sum(jnp.where(lane == k, row, 0.0), axis=1, keepdims=True)
        scale = 1.0 / jnp.sqrt(pivot)
        scaled = row * scale
        whole = work_ref[...]
        left = whole[:, :n]
        column = jnp.sum(jnp.where(lanes[:, :n] == k, left, 0.0), axis=1, keepdims=True) * scale
        updated = jnp.where(rows > k, whole - column * scaled, whole)
        work_ref[...] = jnp.where(rows == k, scaled, updated)
        return carry

    lax.fori_loop(0, n, step, 0, unroll=4)
    out_ref[...] = work_ref[:, n:]


def lower_inverse(gram):
    n = gram.shape[0]
    return pl.pallas_call(
        _lower_inverse_kernel,
        out_shape=jax.ShapeDtypeStruct((n, n), jnp.float32),
        scratch_shapes=[pltpu.VMEM((n, 2 * n), jnp.float32)],
    )(gram)


def _step_kernel(first, below_ref, low_ref, high_ref, above_ref, older_low_ref, older_high_ref,
                 low_pot_ref, high_pot_ref, out_low_ref, out_high_ref):
    half = low_ref.shape[0]
    rows_y = low_ref.shape[1]
    rows_x = low_ref.shape[2]
    place = lax.broadcasted_iota(jnp.int32, (rows_x, low_ref.shape[3]), 0)
    sources = (below_ref, low_ref, high_ref, above_ref)

    def plane(index, y):
        return sources[index // half][index % half, y].astype(jnp.float32)

    for centre in range(half, 3 * half):
        own = centre - half
        older_ref = older_low_ref if own < half else older_high_ref
        potential_ref = low_pot_ref if own < half else high_pot_ref
        out_ref = out_low_ref if own < half else out_high_ref
        local = own % half
        for y in range(rows_y):
            inner = plane(centre, y)
            total = 3.0 * COEF[0] * inner
            for distance in (1, 2, 3):
                along_z = plane(centre + distance, y) + plane(centre - distance, y)
                up = plane(centre, y + distance) if y + distance < rows_y else None
                down = plane(centre, y - distance) if y - distance >= 0 else None
                if up is None:
                    along_y = down
                elif down is None:
                    along_y = up
                else:
                    along_y = up + down
                ahead = jnp.where(
                    place + distance < rows_x, pltpu.roll(inner, rows_x - distance, 0), 0.0
                )
                behind = jnp.where(place >= distance, pltpu.roll(inner, distance, 0), 0.0)
                along_x = ahead + behind
                total = total + COEF[distance] * (along_z + along_y + along_x)
            image = potential_ref[local, y] * inner - 0.5 * total
            if first:
                newer = (image - CSHIFT * inner) / EWIDTH
            else:
                newer = 2.0 / EWIDTH * (image - CSHIFT * inner) - older_ref[local, y].astype(
                    jnp.float32
                )
            out_ref[local, y] = newer.astype(out_ref.dtype)


def chebyshev_step(below, low, high, above, older_low, older_high, potential, first):
    half, rows_y, rows_x, bands = low.shape
    lanes = 128
    block = (half, rows_y, rows_x, lanes)

    def spec(array, part):
        shift = part if array.shape[0] == 2 * half else 0
        return pl.BlockSpec(block, lambda j: (shift, 0, 0, j))

    piece = jax.ShapeDtypeStruct((half, rows_y, rows_x, bands), jnp.bfloat16)
    return pl.pallas_call(
        functools.partial(_step_kernel, first),
        out_shape=(piece, piece),
        grid=(bands // lanes,),
        in_specs=[
            spec(below, 0),
            spec(low, 0),
            spec(high, 0),
            spec(above, 0),
            spec(older_low, 0),
            spec(older_high, 1),
            pl.BlockSpec(block, lambda j: (0, 0, 0, 0)),
            pl.BlockSpec(block, lambda j: (1, 0, 0, 0)),
        ],
        out_specs=(
            pl.BlockSpec(block, lambda j: (0, 0, 0, j)),
            pl.BlockSpec(block, lambda j: (0, 0, 0, j)),
        ),
    )(below, low, high, above, older_low, older_high, potential, potential)


def extended_2(block, sides, width):
    for axis, dim in sides:
        count = lax.axis_size(axis)
        forward = [(i, i + 1) for i in range(count - 1)]
        backward = [(target, source) for source, target in forward]
        low = lax.ppermute(
            lax.slice_in_dim(block, block.shape[dim] - width, None, axis=dim), axis, forward
        )
        high = lax.ppermute(lax.slice_in_dim(block, 0, width, axis=dim), axis, backward)
        block = jnp.concatenate([low, block, high], axis=dim)
    return block


def hamiltonian(extended, potential):
    inner = extended[3:-3]
    planes = inner.shape[0]
    rows_y = inner.shape[1]
    rows_x = inner.shape[2]
    padded_y = jnp.pad(inner, ((0, 0), (3, 3), (0, 0), (0, 0)))
    padded_x = jnp.pad(inner, ((0, 0), (0, 0), (3, 3), (0, 0)))
    total = 3.0 * COEF[0] * inner
    for distance in (1, 2, 3):
        along_z = (
            extended[3 + distance : 3 + distance + planes]
            + extended[3 - distance : 3 - distance + planes]
        )
        along_y = (
            padded_y[:, 3 + distance : 3 + distance + rows_y]
            + padded_y[:, 3 - distance : 3 - distance + rows_y]
        )
        along_x = (
            padded_x[:, :, 3 + distance : 3 + distance + rows_x]
            + padded_x[:, :, 3 - distance : 3 - distance + rows_x]
        )
        total = total + COEF[distance] * (along_z + along_y + along_x)
    return potential[:, :, :, None] * inner - 0.5 * total


def shards(waves, potential, domain_of):
    slabs = lax.axis_size("gz")
    position = lax.axis_index("gz")
    planes = waves.shape[0]
    bands = waves.shape[3]
    grid = potential.reshape(planes, NY, NX)
    owner = domain_of[position]
    below = jnp.where(position > 0, domain_of[jnp.maximum(position - 1, 0)] == owner, False).astype(
        jnp.float32
    )
    above = jnp.where(
        position < slabs - 1, domain_of[jnp.minimum(position + 1, slabs - 1)] == owner, False
    ).astype(jnp.float32)
    mask_three = jnp.concatenate(
        [
            jnp.broadcast_to(below, (3,)),
            jnp.ones((planes,), jnp.float32),
            jnp.broadcast_to(above, (3,)),
        ]
    )[:, None, None, None]

    forward = [(i, i + 1) for i in range(slabs - 1)]
    backward = [(target, source) for source, target in forward]
    bf_below = below.astype(jnp.bfloat16)
    bf_above = above.astype(jnp.bfloat16)

    def rimmed(low, high):
        from_below = lax.ppermute(high, "gz", forward)
        from_above = lax.ppermute(low, "gz", backward)
        return from_below * bf_below, from_above * bf_above

    lanes = jnp.broadcast_to(grid[..., None], grid.shape + (128,))
    half = planes // 2
    low, high = waves[:half], waves[half:]
    from_below, from_above = rimmed(low, high)
    low, high = chebyshev_step(from_below, low, high, from_above, waves, waves, lanes, True)
    older_low, older_high = waves, waves
    for turn in range(DEGREE - 1):
        from_below, from_above = rimmed(low, high)
        newer = chebyshev_step(from_below, low, high, from_above, older_low, older_high, lanes, False)
        older_low, older_high = low, high
        low, high = newer
    current = jnp.concatenate([low, high], axis=0)
    cells = jnp.sum((domain_of == owner).astype(jnp.float32)) * (planes * NY * NX)
    rows = current.reshape(planes * NY * NX, bands)

    def domain_total(term):
        forward = term
        backward = term
        distance = 1
        while distance < slabs:
            ahead = [(i, i + distance) for i in range(slabs - distance)]
            behind = [(i + distance, i) for i in range(slabs - distance)]
            from_low = lax.ppermute(forward, "gz", ahead)
            from_high = lax.ppermute(backward, "gz", behind)
            low_same = jnp.where(
                position >= distance,
                domain_of[jnp.maximum(position - distance, 0)] == owner,
                False,
            ).astype(jnp.float32)
            high_same = jnp.where(
                position + distance < slabs,
                domain_of[jnp.minimum(position + distance, slabs - 1)] == owner,
                False,
            ).astype(jnp.float32)
            forward = forward + low_same * from_low
            backward = backward + high_same * from_high
            distance *= 2
        return forward + backward - term

    identity = jnp.eye(PANEL, dtype=jnp.float32)
    panels = bands // PANEL
    blocks = [rows[:, p * PANEL : (p + 1) * PANEL] for p in range(panels)]
    first = blocks[0]
    cross = jnp.einsum("ca,cb->ab", first, rows, preferred_element_type=jnp.float32)
    cross = domain_total(cross) / cells
    pieces = []
    whitenings = []
    for panel in range(panels):
        block = blocks[panel]
        if panel == 0:
            gram = cross[:, :PANEL]
        else:
            if panel == 1:
                correlation = jnp.dot(
                    whitenings[0].T.astype(jnp.float32),
                    cross[:, PANEL : 2 * PANEL],
                    preferred_element_type=jnp.float32,
                )
            else:
                earlier = jnp.concatenate(pieces, axis=1)
                correlation = (
                    domain_total(
                        jnp.einsum("ca,cb->ab", earlier, block, preferred_element_type=jnp.float32)
                    )
                    / cells
                )
            earlier = jnp.concatenate(pieces, axis=1)
            block = (
                block.astype(jnp.float32)
                - jnp.dot(
                    earlier, correlation.astype(jnp.bfloat16), preferred_element_type=jnp.float32
                )
            ).astype(jnp.bfloat16)
            gram = (
                domain_total(
                    jnp.einsum("ca,cb->ab", block, block, preferred_element_type=jnp.float32)
                )
                / cells
            )
        inverse = lower_inverse(gram)
        whitening = inverse.T.astype(jnp.bfloat16)
        whitenings.append(whitening)
        pieces.append(
            jnp.dot(block, whitening, preferred_element_type=jnp.float32).astype(jnp.bfloat16)
        )
    return jnp.concatenate(pieces, axis=1).reshape(planes, NY, NX, bands)


def solution(mesh):
    return jax.shard_map(
        shards,
        mesh=mesh,
        in_specs=(P(("groups", "gz"), None, None, None), P(("groups", "gz"), None), P("groups")),
        out_specs=P(("groups", "gz"), None, None, None),
        check_vma=False,
    )
```

```python
import functools

import jax
import jax.numpy as jnp
from jax import lax
from jax.experimental import pallas as pl
from jax.experimental.pallas import tpu as pltpu
from jax.sharding import PartitionSpec as P

PANEL = 128
NX = 64
NY = 8
DOMS = 8
DEGREE = 4


COEF = (-49.0 / 18.0, 1.5, -0.15, 1.0 / 90.0)
CSHIFT = 7.0
EWIDTH = 5.0


def _lower_inverse_kernel(gram_ref, out_ref, work_ref):
    n = gram_ref.shape[0]
    rows = lax.broadcasted_iota(jnp.int32, (n, 2 * n), 0)
    lanes = lax.broadcasted_iota(jnp.int32, (n, 2 * n), 1)
    work_ref[:, :n] = gram_ref[...]
    work_ref[:, n:] = (lax.broadcasted_iota(jnp.int32, (n, n), 0) == lax.broadcasted_iota(jnp.int32, (n, n), 1)).astype(jnp.float32)

    def step(k, carry):
        row = work_ref[pl.ds(k, 1), :]
        lane = lax.broadcasted_iota(jnp.int32, (1, 2 * n), 1)
        pivot = jnp.sum(jnp.where(lane == k, row, 0.0), axis=1, keepdims=True)
        scale = 1.0 / jnp.sqrt(pivot)
        scaled = row * scale
        whole = work_ref[...]
        left = whole[:, :n]
        column = jnp.sum(jnp.where(lanes[:, :n] == k, left, 0.0), axis=1, keepdims=True) * scale
        updated = jnp.where(rows > k, whole - column * scaled, whole)
        work_ref[...] = jnp.where(rows == k, scaled, updated)
        return carry

    lax.fori_loop(0, n, step, 0)
    out_ref[...] = work_ref[:, n:]


def lower_inverse(gram):
    n = gram.shape[0]
    return pl.pallas_call(
        _lower_inverse_kernel,
        out_shape=jax.ShapeDtypeStruct((n, n), jnp.float32),
        scratch_shapes=[pltpu.VMEM((n, 2 * n), jnp.float32)],
    )(gram)


def _step_kernel(first, rim_ref, below_ref, low_ref, high_ref, above_ref, older_low_ref,
                 older_high_ref, low_pot_ref, high_pot_ref, out_low_ref, out_high_ref):
    half = low_ref.shape[0]
    rows_y = low_ref.shape[1]
    rows_x = low_ref.shape[2]
    place = lax.broadcasted_iota(jnp.int32, (rows_x, low_ref.shape[3]), 0)
    sources = (below_ref, low_ref, high_ref, above_ref)

    def plane(index, y):
        value = sources[index // half][index % half, y].astype(jnp.float32)
        if index < half:
            return value * rim_ref[0]
        if index >= 3 * half:
            return value * rim_ref[1]
        return value

    for centre in range(half, 3 * half):
        own = centre - half
        older_ref = older_low_ref if own < half else older_high_ref
        potential_ref = low_pot_ref if own < half else high_pot_ref
        out_ref = out_low_ref if own < half else out_high_ref
        local = own % half
        for y in range(rows_y):
            inner = plane(centre, y)
            total = 3.0 * COEF[0] * inner
            for distance in (1, 2, 3):
                along_z = plane(centre + distance, y) + plane(centre - distance, y)
                up = plane(centre, y + distance) if y + distance < rows_y else None
                down = plane(centre, y - distance) if y - distance >= 0 else None
                if up is None:
                    along_y = down
                elif down is None:
                    along_y = up
                else:
                    along_y = up + down
                ahead = jnp.where(
                    place + distance < rows_x, pltpu.roll(inner, rows_x - distance, 0), 0.0
                )
                behind = jnp.where(place >= distance, pltpu.roll(inner, distance, 0), 0.0)
                along_x = ahead + behind
                total = total + COEF[distance] * (along_z + along_y + along_x)
            image = potential_ref[local, y] * inner - 0.5 * total
            if first:
                newer = (image - CSHIFT * inner) / EWIDTH
            else:
                newer = 2.0 / EWIDTH * (image - CSHIFT * inner) - older_ref[local, y].astype(
                    jnp.float32
                )
            out_ref[local, y] = newer.astype(out_ref.dtype)


def chebyshev_step(rim, below, low, high, above, older_low, older_high, potential, first):
    half, rows_y, rows_x, bands = low.shape
    lanes = 128
    block = (half, rows_y, rows_x, lanes)

    def spec(array, part):
        shift = part if array.shape[0] == 2 * half else 0
        return pl.BlockSpec(block, lambda j: (shift, 0, 0, j))

    piece = jax.ShapeDtypeStruct((half, rows_y, rows_x, bands), jnp.bfloat16)
    return pl.pallas_call(
        functools.partial(_step_kernel, first),
        out_shape=(piece, piece),
        grid=(bands // lanes,),
        in_specs=[
            pl.BlockSpec(memory_space=pltpu.SMEM),
            spec(below, 0),
            spec(low, 0),
            spec(high, 0),
            spec(above, 0),
            spec(older_low, 0),
            spec(older_high, 1),
            pl.BlockSpec(block, lambda j: (0, 0, 0, 0)),
            pl.BlockSpec(block, lambda j: (1, 0, 0, 0)),
        ],
        out_specs=(
            pl.BlockSpec(block, lambda j: (0, 0, 0, j)),
            pl.BlockSpec(block, lambda j: (0, 0, 0, j)),
        ),
    )(rim, below, low, high, above, older_low, older_high, potential, potential)


def extended_2(block, sides, width):
    for axis, dim in sides:
        count = lax.axis_size(axis)
        forward = [(i, i + 1) for i in range(count - 1)]
        backward = [(target, source) for source, target in forward]
        low = lax.ppermute(
            lax.slice_in_dim(block, block.shape[dim] - width, None, axis=dim), axis, forward
        )
        high = lax.ppermute(lax.slice_in_dim(block, 0, width, axis=dim), axis, backward)
        block = jnp.concatenate([low, block, high], axis=dim)
    return block


def hamiltonian(extended, potential):
    inner = extended[3:-3]
    planes = inner.shape[0]
    rows_y = inner.shape[1]
    rows_x = inner.shape[2]
    padded_y = jnp.pad(inner, ((0, 0), (3, 3), (0, 0), (0, 0)))
    padded_x = jnp.pad(inner, ((0, 0), (0, 0), (3, 3), (0, 0)))
    total = 3.0 * COEF[0] * inner
    for distance in (1, 2, 3):
        along_z = (
            extended[3 + distance : 3 + distance + planes]
            + extended[3 - distance : 3 - distance + planes]
        )
        along_y = (
            padded_y[:, 3 + distance : 3 + distance + rows_y]
            + padded_y[:, 3 - distance : 3 - distance + rows_y]
        )
        along_x = (
            padded_x[:, :, 3 + distance : 3 + distance + rows_x]
            + padded_x[:, :, 3 - distance : 3 - distance + rows_x]
        )
        total = total + COEF[distance] * (along_z + along_y + along_x)
    return potential[:, :, :, None] * inner - 0.5 * total


def shards(waves, potential, domain_of):
    slabs = lax.axis_size("gz")
    position = lax.axis_index("gz")
    planes = waves.shape[0]
    bands = waves.shape[3]
    grid = potential.reshape(planes, NY, NX)
    owner = domain_of[position]
    below = jnp.where(position > 0, domain_of[jnp.maximum(position - 1, 0)] == owner, False).astype(
        jnp.float32
    )
    above = jnp.where(
        position < slabs - 1, domain_of[jnp.minimum(position + 1, slabs - 1)] == owner, False
    ).astype(jnp.float32)
    mask_three = jnp.concatenate(
        [
            jnp.broadcast_to(below, (3,)),
            jnp.ones((planes,), jnp.float32),
            jnp.broadcast_to(above, (3,)),
        ]
    )[:, None, None, None]

    forward = [(i, i + 1) for i in range(slabs - 1)]
    backward = [(target, source) for source, target in forward]
    rim = jnp.stack([below, above])

    def rimmed(low, high):
        from_below = lax.ppermute(high, "gz", forward)
        from_above = lax.ppermute(low, "gz", backward)
        return from_below, from_above

    lanes = jnp.broadcast_to(grid[..., None], grid.shape + (128,))
    half = planes // 2
    low, high = waves[:half], waves[half:]
    from_below, from_above = rimmed(low, high)
    low, high = chebyshev_step(rim, from_below, low, high, from_above, waves, waves, lanes, True)
    older_low, older_high = waves, waves
    for turn in range(DEGREE - 1):
        from_below, from_above = rimmed(low, high)
        newer = chebyshev_step(
            rim, from_below, low, high, from_above, older_low, older_high, lanes, False
        )
        older_low, older_high = low, high
        low, high = newer
    current = jnp.concatenate([low, high], axis=0)
    cells = jnp.sum((domain_of == owner).astype(jnp.float32)) * (planes * NY * NX)
    rows = current.reshape(planes * NY * NX, bands)

    def domain_total(term):
        forward = term
        backward = term
        distance = 1
        while distance < slabs:
            ahead = [(i, i + distance) for i in range(slabs - distance)]
            behind = [(i + distance, i) for i in range(slabs - distance)]
            from_low = lax.ppermute(forward, "gz", ahead)
            from_high = lax.ppermute(backward, "gz", behind)
            low_same = jnp.where(
                position >= distance,
                domain_of[jnp.maximum(position - distance, 0)] == owner,
                False,
            ).astype(jnp.float32)
            high_same = jnp.where(
                position + distance < slabs,
                domain_of[jnp.minimum(position + distance, slabs - 1)] == owner,
                False,
            ).astype(jnp.float32)
            forward = forward + low_same * from_low
            backward = backward + high_same * from_high
            distance *= 2
        return forward + backward - term

    identity = jnp.eye(PANEL, dtype=jnp.float32)
    panels = bands // PANEL
    blocks = [rows[:, p * PANEL : (p + 1) * PANEL] for p in range(panels)]
    first = blocks[0]
    cross = jnp.einsum("ca,cb->ab", first, rows, preferred_element_type=jnp.float32)
    cross = domain_total(cross) / cells
    pieces = []
    whitenings = []
    for panel in range(panels):
        block = blocks[panel]
        if panel == 0:
            gram = cross[:, :PANEL]
        else:
            if panel == 1:
                correlation = jnp.dot(
                    whitenings[0].T.astype(jnp.float32),
                    cross[:, PANEL : 2 * PANEL],
                    preferred_element_type=jnp.float32,
                )
            else:
                earlier = jnp.concatenate(pieces, axis=1)
                correlation = (
                    domain_total(
                        jnp.einsum("ca,cb->ab", earlier, block, preferred_element_type=jnp.float32)
                    )
                    / cells
                )
            earlier = jnp.concatenate(pieces, axis=1)
            block = (
                block.astype(jnp.float32)
                - jnp.dot(
                    earlier, correlation.astype(jnp.bfloat16), preferred_element_type=jnp.float32
                )
            ).astype(jnp.bfloat16)
            gram = (
                domain_total(
                    jnp.einsum("ca,cb->ab", block, block, preferred_element_type=jnp.float32)
                )
                / cells
            )
        inverse = lower_inverse(gram)
        whitening = inverse.T.astype(jnp.bfloat16)
        whitenings.append(whitening)
        pieces.append(
            jnp.dot(block, whitening, preferred_element_type=jnp.float32).astype(jnp.bfloat16)
        )
    return jnp.concatenate(pieces, axis=1).reshape(planes, NY, NX, bands)


def solution(mesh):
    return jax.shard_map(
        shards,
        mesh=mesh,
        in_specs=(P(("groups", "gz"), None, None, None), P(("groups", "gz"), None), P("groups")),
        out_specs=P(("groups", "gz"), None, None, None),
        check_vma=False,
    )
```

```python
import functools

import jax
import jax.numpy as jnp
from jax import lax
from jax.experimental import pallas as pl
from jax.experimental.pallas import tpu as pltpu
from jax.sharding import PartitionSpec as P

PANEL = 128
NX = 64
NY = 8
DOMS = 8
DEGREE = 4


COEF = (-49.0 / 18.0, 1.5, -0.15, 1.0 / 90.0)
CSHIFT = 7.0
EWIDTH = 5.0


def _lower_inverse_kernel(gram_ref, out_ref, work_ref):
    n = gram_ref.shape[0]
    work_ref[:, :n] = gram_ref[...]
    work_ref[:, n:] = (lax.broadcasted_iota(jnp.int32, (n, n), 0) == lax.broadcasted_iota(jnp.int32, (n, n), 1)).astype(jnp.float32)

    rows = lax.broadcasted_iota(jnp.int32, (n, 2 * n), 0)
    left_lanes = lax.broadcasted_iota(jnp.int32, (n, n), 1)
    lane = lax.broadcasted_iota(jnp.int32, (1, 2 * n), 1)

    def pick(vector, index):
        return jnp.sum(jnp.where(lane == index, vector, 0.0), axis=1, keepdims=True)

    def step(pair, carry):
        k = 2 * pair
        row_a = work_ref[pl.ds(k, 1), :]
        row_b = work_ref[pl.ds(k + 1, 1), :]
        scale_a = 1.0 / jnp.sqrt(pick(row_a, k))
        scaled_a = row_a * scale_a
        row_b = row_b - (pick(row_b, k) * scale_a) * scaled_a
        scale_b = 1.0 / jnp.sqrt(pick(row_b, k + 1))
        scaled_b = row_b * scale_b
        whole = work_ref[...]
        left = whole[:, :n]
        column_a = jnp.sum(jnp.where(left_lanes == k, left, 0.0), axis=1, keepdims=True) * scale_a
        next_column = jnp.sum(jnp.where(left_lanes == k + 1, left, 0.0), axis=1, keepdims=True)
        column_b = (next_column - column_a * pick(scaled_a, k + 1)) * scale_b
        updated = (whole - column_a * scaled_a) - column_b * scaled_b
        updated = jnp.where(rows > k + 1, updated, whole)
        updated = jnp.where(rows == k, scaled_a, updated)
        work_ref[...] = jnp.where(rows == k + 1, scaled_b, updated)
        return carry

    lax.fori_loop(0, n // 2, step, 0)
    out_ref[...] = work_ref[:, n:]


def lower_inverse(gram):
    n = gram.shape[0]
    return pl.pallas_call(
        _lower_inverse_kernel,
        out_shape=jax.ShapeDtypeStruct((n, n), jnp.float32),
        scratch_shapes=[pltpu.VMEM((n, 2 * n), jnp.float32)],
    )(gram)


def _step_kernel(first, rim_ref, below_ref, low_ref, high_ref, above_ref, older_low_ref,
                 older_high_ref, low_pot_ref, high_pot_ref, out_low_ref, out_high_ref):
    half = low_ref.shape[0]
    rows_y = low_ref.shape[1]
    rows_x = low_ref.shape[2]
    place = lax.broadcasted_iota(jnp.int32, (rows_x, low_ref.shape[3]), 0)
    sources = (below_ref, low_ref, high_ref, above_ref)

    def plane(index, y):
        value = sources[index // half][index % half, y].astype(jnp.float32)
        if index < half:
            return value * rim_ref[0]
        if index >= 3 * half:
            return value * rim_ref[1]
        return value

    for centre in range(half, 3 * half):
        own = centre - half
        older_ref = older_low_ref if own < half else older_high_ref
        potential_ref = low_pot_ref if own < half else high_pot_ref
        out_ref = out_low_ref if own < half else out_high_ref
        local = own % half
        for y in range(rows_y):
            inner = plane(centre, y)
            total = 3.0 * COEF[0] * inner
            for distance in (1, 2, 3):
                along_z = plane(centre + distance, y) + plane(centre - distance, y)
                up = plane(centre, y + distance) if y + distance < rows_y else None
                down = plane(centre, y - distance) if y - distance >= 0 else None
                if up is None:
                    along_y = down
                elif down is None:
                    along_y = up
                else:
                    along_y = up + down
                ahead = jnp.where(
                    place + distance < rows_x, pltpu.roll(inner, rows_x - distance, 0), 0.0
                )
                behind = jnp.where(place >= distance, pltpu.roll(inner, distance, 0), 0.0)
                along_x = ahead + behind
                total = total + COEF[distance] * (along_z + along_y + along_x)
            image = potential_ref[local, y] * inner - 0.5 * total
            if first:
                newer = (image - CSHIFT * inner) / EWIDTH
            else:
                newer = 2.0 / EWIDTH * (image - CSHIFT * inner) - older_ref[local, y].astype(
                    jnp.float32
                )
            out_ref[local, y] = newer.astype(out_ref.dtype)


def chebyshev_step(rim, below, low, high, above, older_low, older_high, potential, first):
    half, rows_y, rows_x, bands = low.shape
    lanes = 128
    block = (half, rows_y, rows_x, lanes)

    def spec(array, part):
        shift = part if array.shape[0] == 2 * half else 0
        return pl.BlockSpec(block, lambda j: (shift, 0, 0, j))

    piece = jax.ShapeDtypeStruct((half, rows_y, rows_x, bands), jnp.bfloat16)
    return pl.pallas_call(
        functools.partial(_step_kernel, first),
        out_shape=(piece, piece),
        grid=(bands // lanes,),
        in_specs=[
            pl.BlockSpec(memory_space=pltpu.SMEM),
            spec(below, 0),
            spec(low, 0),
            spec(high, 0),
            spec(above, 0),
            spec(older_low, 0),
            spec(older_high, 1),
            pl.BlockSpec(block, lambda j: (0, 0, 0, 0)),
            pl.BlockSpec(block, lambda j: (1, 0, 0, 0)),
        ],
        out_specs=(
            pl.BlockSpec(block, lambda j: (0, 0, 0, j)),
            pl.BlockSpec(block, lambda j: (0, 0, 0, j)),
        ),
    )(rim, below, low, high, above, older_low, older_high, potential, potential)


def extended_2(block, sides, width):
    for axis, dim in sides:
        count = lax.axis_size(axis)
        forward = [(i, i + 1) for i in range(count - 1)]
        backward = [(target, source) for source, target in forward]
        low = lax.ppermute(
            lax.slice_in_dim(block, block.shape[dim] - width, None, axis=dim), axis, forward
        )
        high = lax.ppermute(lax.slice_in_dim(block, 0, width, axis=dim), axis, backward)
        block = jnp.concatenate([low, block, high], axis=dim)
    return block


def hamiltonian(extended, potential):
    inner = extended[3:-3]
    planes = inner.shape[0]
    rows_y = inner.shape[1]
    rows_x = inner.shape[2]
    padded_y = jnp.pad(inner, ((0, 0), (3, 3), (0, 0), (0, 0)))
    padded_x = jnp.pad(inner, ((0, 0), (0, 0), (3, 3), (0, 0)))
    total = 3.0 * COEF[0] * inner
    for distance in (1, 2, 3):
        along_z = (
            extended[3 + distance : 3 + distance + planes]
            + extended[3 - distance : 3 - distance + planes]
        )
        along_y = (
            padded_y[:, 3 + distance : 3 + distance + rows_y]
            + padded_y[:, 3 - distance : 3 - distance + rows_y]
        )
        along_x = (
            padded_x[:, :, 3 + distance : 3 + distance + rows_x]
            + padded_x[:, :, 3 - distance : 3 - distance + rows_x]
        )
        total = total + COEF[distance] * (along_z + along_y + along_x)
    return potential[:, :, :, None] * inner - 0.5 * total


def shards(waves, potential, domain_of):
    slabs = lax.axis_size("gz")
    position = lax.axis_index("gz")
    planes = waves.shape[0]
    bands = waves.shape[3]
    grid = potential.reshape(planes, NY, NX)
    owner = domain_of[position]
    below = jnp.where(position > 0, domain_of[jnp.maximum(position - 1, 0)] == owner, False).astype(
        jnp.float32
    )
    above = jnp.where(
        position < slabs - 1, domain_of[jnp.minimum(position + 1, slabs - 1)] == owner, False
    ).astype(jnp.float32)
    mask_three = jnp.concatenate(
        [
            jnp.broadcast_to(below, (3,)),
            jnp.ones((planes,), jnp.float32),
            jnp.broadcast_to(above, (3,)),
        ]
    )[:, None, None, None]

    forward = [(i, i + 1) for i in range(slabs - 1)]
    backward = [(target, source) for source, target in forward]
    rim = jnp.stack([below, above])

    def rimmed(low, high):
        from_below = lax.ppermute(high, "gz", forward)
        from_above = lax.ppermute(low, "gz", backward)
        return from_below, from_above

    lanes = jnp.broadcast_to(grid[..., None], grid.shape + (128,))
    half = planes // 2
    low, high = waves[:half], waves[half:]
    from_below, from_above = rimmed(low, high)
    low, high = chebyshev_step(rim, from_below, low, high, from_above, waves, waves, lanes, True)
    older_low, older_high = waves, waves
    for turn in range(DEGREE - 1):
        from_below, from_above = rimmed(low, high)
        newer = chebyshev_step(
            rim, from_below, low, high, from_above, older_low, older_high, lanes, False
        )
        older_low, older_high = low, high
        low, high = newer
    current = jnp.concatenate([low, high], axis=0)
    cells = jnp.sum((domain_of == owner).astype(jnp.float32)) * (planes * NY * NX)
    rows = current.reshape(planes * NY * NX, bands)

    def domain_total(term):
        forward = term
        backward = term
        distance = 1
        while distance < slabs:
            ahead = [(i, i + distance) for i in range(slabs - distance)]
            behind = [(i + distance, i) for i in range(slabs - distance)]
            from_low = lax.ppermute(forward, "gz", ahead)
            from_high = lax.ppermute(backward, "gz", behind)
            low_same = jnp.where(
                position >= distance,
                domain_of[jnp.maximum(position - distance, 0)] == owner,
                False,
            ).astype(jnp.float32)
            high_same = jnp.where(
                position + distance < slabs,
                domain_of[jnp.minimum(position + distance, slabs - 1)] == owner,
                False,
            ).astype(jnp.float32)
            forward = forward + low_same * from_low
            backward = backward + high_same * from_high
            distance *= 2
        return forward + backward - term

    identity = jnp.eye(PANEL, dtype=jnp.float32)
    panels = bands // PANEL
    blocks = [rows[:, p * PANEL : (p + 1) * PANEL] for p in range(panels)]
    first = blocks[0]
    cross = jnp.einsum("ca,cb->ab", first, rows, preferred_element_type=jnp.float32)
    cross = domain_total(cross) / cells
    pieces = []
    whitenings = []
    for panel in range(panels):
        block = blocks[panel]
        if panel == 0:
            gram = cross[:, :PANEL]
        else:
            if panel == 1:
                correlation = jnp.dot(
                    whitenings[0].T.astype(jnp.float32),
                    cross[:, PANEL : 2 * PANEL],
                    preferred_element_type=jnp.float32,
                )
            else:
                earlier = jnp.concatenate(pieces, axis=1)
                correlation = (
                    domain_total(
                        jnp.einsum("ca,cb->ab", earlier, block, preferred_element_type=jnp.float32)
                    )
                    / cells
                )
            earlier = jnp.concatenate(pieces, axis=1)
            block = (
                block.astype(jnp.float32)
                - jnp.dot(
                    earlier, correlation.astype(jnp.bfloat16), preferred_element_type=jnp.float32
                )
            ).astype(jnp.bfloat16)
            gram = (
                domain_total(
                    jnp.einsum("ca,cb->ab", block, block, preferred_element_type=jnp.float32)
                )
                / cells
            )
        inverse = lower_inverse(gram)
        whitening = inverse.T.astype(jnp.bfloat16)
        whitenings.append(whitening)
        pieces.append(
            jnp.dot(block, whitening, preferred_element_type=jnp.float32).astype(jnp.bfloat16)
        )
    return jnp.concatenate(pieces, axis=1).reshape(planes, NY, NX, bands)


def solution(mesh):
    return jax.shard_map(
        shards,
        mesh=mesh,
        in_specs=(P(("groups", "gz"), None, None, None), P(("groups", "gz"), None), P("groups")),
        out_specs=P(("groups", "gz"), None, None, None),
        check_vma=False,
    )
```

```python
import functools

import jax
import jax.numpy as jnp
from jax import lax
from jax.experimental import pallas as pl
from jax.experimental.pallas import tpu as pltpu
from jax.sharding import PartitionSpec as P

PANEL = 128
NX = 64
NY = 8
DOMS = 8
DEGREE = 4


COEF = (-49.0 / 18.0, 1.5, -0.15, 1.0 / 90.0)
CSHIFT = 7.0
EWIDTH = 5.0


def _lower_inverse_kernel(gram_ref, out_ref, work_ref):
    n = gram_ref.shape[0]
    work_ref[:, :n] = gram_ref[...]
    work_ref[:, n:] = (lax.broadcasted_iota(jnp.int32, (n, n), 0) == lax.broadcasted_iota(jnp.int32, (n, n), 1)).astype(jnp.float32)

    rows = lax.broadcasted_iota(jnp.int32, (n, 2 * n), 0)
    lane = lax.broadcasted_iota(jnp.int32, (1, 2 * n), 1)

    def pick(vector, index):
        return jnp.sum(jnp.where(lane == index, vector, 0.0), axis=1, keepdims=True)

    def step(pair, carry):
        k = 2 * pair
        row_a = work_ref[pl.ds(k, 1), :]
        row_b = work_ref[pl.ds(k + 1, 1), :]
        first_row, second_row = row_a, row_b
        scale_a = 1.0 / jnp.sqrt(pick(row_a, k))
        scaled_a = row_a * scale_a
        row_b = row_b - (pick(row_b, k) * scale_a) * scaled_a
        scale_b = 1.0 / jnp.sqrt(pick(row_b, k + 1))
        scaled_b = row_b * scale_b
        whole = work_ref[...]
        sub = lax.broadcasted_iota(jnp.int32, (n, n), 0)
        pivots = jnp.where(sub == 0, first_row[:, :n], jnp.where(sub == 1, second_row[:, :n], 0.0))
        columns = pivots.T
        column_a = columns[:, 0:1] * scale_a
        next_column = columns[:, 1:2]
        column_b = (next_column - column_a * pick(scaled_a, k + 1)) * scale_b
        updated = (whole - column_a * scaled_a) - column_b * scaled_b
        updated = jnp.where(rows > k + 1, updated, whole)
        updated = jnp.where(rows == k, scaled_a, updated)
        work_ref[...] = jnp.where(rows == k + 1, scaled_b, updated)
        return carry

    lax.fori_loop(0, n // 2, step, 0)
    out_ref[...] = work_ref[:, n:]


def lower_inverse(gram):
    n = gram.shape[0]
    return pl.pallas_call(
        _lower_inverse_kernel,
        out_shape=jax.ShapeDtypeStruct((n, n), jnp.float32),
        scratch_shapes=[pltpu.VMEM((n, 2 * n), jnp.float32)],
    )(gram)


def _step_kernel(first, rim_ref, below_ref, low_ref, high_ref, above_ref, older_low_ref,
                 older_high_ref, low_pot_ref, high_pot_ref, out_low_ref, out_high_ref):
    half = low_ref.shape[0]
    rows_y = low_ref.shape[1]
    rows_x = low_ref.shape[2]
    place = lax.broadcasted_iota(jnp.int32, (rows_x, low_ref.shape[3]), 0)
    sources = (below_ref, low_ref, high_ref, above_ref)

    def plane(index, y):
        value = sources[index // half][index % half, y].astype(jnp.float32)
        if index < half:
            return value * rim_ref[0]
        if index >= 3 * half:
            return value * rim_ref[1]
        return value

    for centre in range(half, 3 * half):
        own = centre - half
        older_ref = older_low_ref if own < half else older_high_ref
        potential_ref = low_pot_ref if own < half else high_pot_ref
        out_ref = out_low_ref if own < half else out_high_ref
        local = own % half
        for y in range(rows_y):
            inner = plane(centre, y)
            total = 3.0 * COEF[0] * inner
            for distance in (1, 2, 3):
                along_z = plane(centre + distance, y) + plane(centre - distance, y)
                up = plane(centre, y + distance) if y + distance < rows_y else None
                down = plane(centre, y - distance) if y - distance >= 0 else None
                if up is None:
                    along_y = down
                elif down is None:
                    along_y = up
                else:
                    along_y = up + down
                ahead = jnp.where(
                    place + distance < rows_x, pltpu.roll(inner, rows_x - distance, 0), 0.0
                )
                behind = jnp.where(place >= distance, pltpu.roll(inner, distance, 0), 0.0)
                along_x = ahead + behind
                total = total + COEF[distance] * (along_z + along_y + along_x)
            image = potential_ref[local, y] * inner - 0.5 * total
            if first:
                newer = (image - CSHIFT * inner) / EWIDTH
            else:
                newer = 2.0 / EWIDTH * (image - CSHIFT * inner) - older_ref[local, y].astype(
                    jnp.float32
                )
            out_ref[local, y] = newer.astype(out_ref.dtype)


def chebyshev_step(rim, below, low, high, above, older_low, older_high, potential, first):
    half, rows_y, rows_x, bands = low.shape
    lanes = 128
    block = (half, rows_y, rows_x, lanes)

    def spec(array, part):
        shift = part if array.shape[0] == 2 * half else 0
        return pl.BlockSpec(block, lambda j: (shift, 0, 0, j))

    piece = jax.ShapeDtypeStruct((half, rows_y, rows_x, bands), jnp.bfloat16)
    return pl.pallas_call(
        functools.partial(_step_kernel, first),
        out_shape=(piece, piece),
        grid=(bands // lanes,),
        in_specs=[
            pl.BlockSpec(memory_space=pltpu.SMEM),
            spec(below, 0),
            spec(low, 0),
            spec(high, 0),
            spec(above, 0),
            spec(older_low, 0),
            spec(older_high, 1),
            pl.BlockSpec(block, lambda j: (0, 0, 0, 0)),
            pl.BlockSpec(block, lambda j: (1, 0, 0, 0)),
        ],
        out_specs=(
            pl.BlockSpec(block, lambda j: (0, 0, 0, j)),
            pl.BlockSpec(block, lambda j: (0, 0, 0, j)),
        ),
    )(rim, below, low, high, above, older_low, older_high, potential, potential)


def extended_2(block, sides, width):
    for axis, dim in sides:
        count = lax.axis_size(axis)
        forward = [(i, i + 1) for i in range(count - 1)]
        backward = [(target, source) for source, target in forward]
        low = lax.ppermute(
            lax.slice_in_dim(block, block.shape[dim] - width, None, axis=dim), axis, forward
        )
        high = lax.ppermute(lax.slice_in_dim(block, 0, width, axis=dim), axis, backward)
        block = jnp.concatenate([low, block, high], axis=dim)
    return block


def hamiltonian(extended, potential):
    inner = extended[3:-3]
    planes = inner.shape[0]
    rows_y = inner.shape[1]
    rows_x = inner.shape[2]
    padded_y = jnp.pad(inner, ((0, 0), (3, 3), (0, 0), (0, 0)))
    padded_x = jnp.pad(inner, ((0, 0), (0, 0), (3, 3), (0, 0)))
    total = 3.0 * COEF[0] * inner
    for distance in (1, 2, 3):
        along_z = (
            extended[3 + distance : 3 + distance + planes]
            + extended[3 - distance : 3 - distance + planes]
        )
        along_y = (
            padded_y[:, 3 + distance : 3 + distance + rows_y]
            + padded_y[:, 3 - distance : 3 - distance + rows_y]
        )
        along_x = (
            padded_x[:, :, 3 + distance : 3 + distance + rows_x]
            + padded_x[:, :, 3 - distance : 3 - distance + rows_x]
        )
        total = total + COEF[distance] * (along_z + along_y + along_x)
    return potential[:, :, :, None] * inner - 0.5 * total


def shards(waves, potential, domain_of):
    slabs = lax.axis_size("gz")
    position = lax.axis_index("gz")
    planes = waves.shape[0]
    bands = waves.shape[3]
    grid = potential.reshape(planes, NY, NX)
    owner = domain_of[position]
    below = jnp.where(position > 0, domain_of[jnp.maximum(position - 1, 0)] == owner, False).astype(
        jnp.float32
    )
    above = jnp.where(
        position < slabs - 1, domain_of[jnp.minimum(position + 1, slabs - 1)] == owner, False
    ).astype(jnp.float32)
    mask_three = jnp.concatenate(
        [
            jnp.broadcast_to(below, (3,)),
            jnp.ones((planes,), jnp.float32),
            jnp.broadcast_to(above, (3,)),
        ]
    )[:, None, None, None]

    forward = [(i, i + 1) for i in range(slabs - 1)]
    backward = [(target, source) for source, target in forward]
    rim = jnp.stack([below, above])

    def rimmed(low, high):
        from_below = lax.ppermute(high, "gz", forward)
        from_above = lax.ppermute(low, "gz", backward)
        return from_below, from_above

    lanes = jnp.broadcast_to(grid[..., None], grid.shape + (128,))
    half = planes // 2
    low, high = waves[:half], waves[half:]
    from_below, from_above = rimmed(low, high)
    low, high = chebyshev_step(rim, from_below, low, high, from_above, waves, waves, lanes, True)
    older_low, older_high = waves, waves
    for turn in range(DEGREE - 1):
        from_below, from_above = rimmed(low, high)
        newer = chebyshev_step(
            rim, from_below, low, high, from_above, older_low, older_high, lanes, False
        )
        older_low, older_high = low, high
        low, high = newer
    current = jnp.concatenate([low, high], axis=0)
    cells = jnp.sum((domain_of == owner).astype(jnp.float32)) * (planes * NY * NX)
    rows = current.reshape(planes * NY * NX, bands)

    def domain_total(term):
        forward = term
        backward = term
        distance = 1
        while distance < slabs:
            ahead = [(i, i + distance) for i in range(slabs - distance)]
            behind = [(i + distance, i) for i in range(slabs - distance)]
            from_low = lax.ppermute(forward, "gz", ahead)
            from_high = lax.ppermute(backward, "gz", behind)
            low_same = jnp.where(
                position >= distance,
                domain_of[jnp.maximum(position - distance, 0)] == owner,
                False,
            ).astype(jnp.float32)
            high_same = jnp.where(
                position + distance < slabs,
                domain_of[jnp.minimum(position + distance, slabs - 1)] == owner,
                False,
            ).astype(jnp.float32)
            forward = forward + low_same * from_low
            backward = backward + high_same * from_high
            distance *= 2
        return forward + backward - term

    identity = jnp.eye(PANEL, dtype=jnp.float32)
    panels = bands // PANEL
    blocks = [rows[:, p * PANEL : (p + 1) * PANEL] for p in range(panels)]
    first = blocks[0]
    cross = jnp.einsum("ca,cb->ab", first, rows, preferred_element_type=jnp.float32)
    cross = domain_total(cross) / cells
    pieces = []
    whitenings = []
    for panel in range(panels):
        block = blocks[panel]
        if panel == 0:
            gram = cross[:, :PANEL]
        else:
            if panel == 1:
                correlation = jnp.dot(
                    whitenings[0].T.astype(jnp.float32),
                    cross[:, PANEL : 2 * PANEL],
                    preferred_element_type=jnp.float32,
                )
            else:
                earlier = jnp.concatenate(pieces, axis=1)
                correlation = (
                    domain_total(
                        jnp.einsum("ca,cb->ab", earlier, block, preferred_element_type=jnp.float32)
                    )
                    / cells
                )
            earlier = jnp.concatenate(pieces, axis=1)
            block = (
                block.astype(jnp.float32)
                - jnp.dot(
                    earlier, correlation.astype(jnp.bfloat16), preferred_element_type=jnp.float32
                )
            ).astype(jnp.bfloat16)
            gram = (
                domain_total(
                    jnp.einsum("ca,cb->ab", block, block, preferred_element_type=jnp.float32)
                )
                / cells
            )
        inverse = lower_inverse(gram)
        whitening = inverse.T.astype(jnp.bfloat16)
        whitenings.append(whitening)
        pieces.append(
            jnp.dot(block, whitening, preferred_element_type=jnp.float32).astype(jnp.bfloat16)
        )
    return jnp.concatenate(pieces, axis=1).reshape(planes, NY, NX, bands)


def solution(mesh):
    return jax.shard_map(
        shards,
        mesh=mesh,
        in_specs=(P(("groups", "gz"), None, None, None), P(("groups", "gz"), None), P("groups")),
        out_specs=P(("groups", "gz"), None, None, None),
        check_vma=False,
    )
```

```python
import functools

import jax
import jax.numpy as jnp
from jax import lax
from jax.experimental import pallas as pl
from jax.experimental.pallas import tpu as pltpu
from jax.sharding import PartitionSpec as P

PANEL = 128
NX = 64
NY = 8
DOMS = 8
DEGREE = 4


COEF = (-49.0 / 18.0, 1.5, -0.15, 1.0 / 90.0)
CSHIFT = 7.0
EWIDTH = 5.0


def _lower_inverse_kernel(gram_ref, out_ref, work_ref):
    n = gram_ref.shape[0]
    work_ref[:, :n] = gram_ref[...]
    work_ref[:, n:] = (lax.broadcasted_iota(jnp.int32, (n, n), 0) == lax.broadcasted_iota(jnp.int32, (n, n), 1)).astype(jnp.float32)

    rows = lax.broadcasted_iota(jnp.int32, (n, 2 * n), 0)
    left_lanes = lax.broadcasted_iota(jnp.int32, (n, n), 1)
    lane = lax.broadcasted_iota(jnp.int32, (1, 2 * n), 1)

    def pick(vector, index):
        return jnp.sum(jnp.where(lane == index, vector, 0.0), axis=1, keepdims=True)

    def step(pair, carry):
        k = 2 * pair
        row_a = work_ref[pl.ds(k, 1), :]
        row_b = work_ref[pl.ds(k + 1, 1), :]
        scale_a = 1.0 / jnp.sqrt(pick(row_a, k))
        scaled_a = row_a * scale_a
        row_b = row_b - (pick(row_b, k) * scale_a) * scaled_a
        scale_b = 1.0 / jnp.sqrt(pick(row_b, k + 1))
        scaled_b = row_b * scale_b
        whole = work_ref[...]
        left = whole[:, :n]
        column_a = jnp.sum(jnp.where(left_lanes == k, left, 0.0), axis=1, keepdims=True) * scale_a
        next_column = jnp.sum(jnp.where(left_lanes == k + 1, left, 0.0), axis=1, keepdims=True)
        column_b = (next_column - column_a * pick(scaled_a, k + 1)) * scale_b
        updated = (whole - column_a * scaled_a) - column_b * scaled_b
        updated = jnp.where(rows > k + 1, updated, whole)
        updated = jnp.where(rows == k, scaled_a, updated)
        work_ref[...] = jnp.where(rows == k + 1, scaled_b, updated)
        return carry

    lax.fori_loop(0, n // 2, step, 0)
    out_ref[...] = work_ref[:, n:]


def lower_inverse(gram):
    n = gram.shape[0]
    return pl.pallas_call(
        _lower_inverse_kernel,
        out_shape=jax.ShapeDtypeStruct((n, n), jnp.float32),
        scratch_shapes=[pltpu.VMEM((n, 2 * n), jnp.float32)],
    )(gram)


def _step_kernel(first, rim_ref, below_ref, low_ref, high_ref, above_ref, older_low_ref,
                 older_high_ref, low_pot_ref, high_pot_ref, out_low_ref, out_high_ref, wide_ref):
    half = low_ref.shape[0]
    rows_y = low_ref.shape[1]
    rows_x = low_ref.shape[2]
    place = lax.broadcasted_iota(jnp.int32, (rows_x, low_ref.shape[3]), 0)
    sources = (below_ref, low_ref, high_ref, above_ref)

    for index in range(4 * half):
        value = sources[index // half][index % half].astype(jnp.float32)
        if index < half:
            value = value * rim_ref[0]
        elif index >= 3 * half:
            value = value * rim_ref[1]
        wide_ref[index] = value

    def plane(index, y):
        return wide_ref[index, y]

    for centre in range(half, 3 * half):
        own = centre - half
        older_ref = older_low_ref if own < half else older_high_ref
        potential_ref = low_pot_ref if own < half else high_pot_ref
        out_ref = out_low_ref if own < half else out_high_ref
        local = own % half
        for y in range(rows_y):
            inner = plane(centre, y)
            total = 3.0 * COEF[0] * inner
            for distance in (1, 2, 3):
                along_z = plane(centre + distance, y) + plane(centre - distance, y)
                up = plane(centre, y + distance) if y + distance < rows_y else None
                down = plane(centre, y - distance) if y - distance >= 0 else None
                if up is None:
                    along_y = down
                elif down is None:
                    along_y = up
                else:
                    along_y = up + down
                ahead = jnp.where(
                    place + distance < rows_x, pltpu.roll(inner, rows_x - distance, 0), 0.0
                )
                behind = jnp.where(place >= distance, pltpu.roll(inner, distance, 0), 0.0)
                along_x = ahead + behind
                total = total + COEF[distance] * (along_z + along_y + along_x)
            image = potential_ref[local, y] * inner - 0.5 * total
            if first:
                newer = (image - CSHIFT * inner) / EWIDTH
            else:
                newer = 2.0 / EWIDTH * (image - CSHIFT * inner) - older_ref[local, y].astype(
                    jnp.float32
                )
            out_ref[local, y] = newer.astype(out_ref.dtype)


def chebyshev_step(rim, below, low, high, above, older_low, older_high, potential, first):
    half, rows_y, rows_x, bands = low.shape
    lanes = 128
    block = (half, rows_y, rows_x, lanes)

    def spec(array, part):
        shift = part if array.shape[0] == 2 * half else 0
        return pl.BlockSpec(block, lambda j: (shift, 0, 0, j))

    piece = jax.ShapeDtypeStruct((half, rows_y, rows_x, bands), jnp.bfloat16)
    return pl.pallas_call(
        functools.partial(_step_kernel, first),
        out_shape=(piece, piece),
        grid=(bands // lanes,),
        in_specs=[
            pl.BlockSpec(memory_space=pltpu.SMEM),
            spec(below, 0),
            spec(low, 0),
            spec(high, 0),
            spec(above, 0),
            spec(older_low, 0),
            spec(older_high, 1),
            pl.BlockSpec(block, lambda j: (0, 0, 0, 0)),
            pl.BlockSpec(block, lambda j: (1, 0, 0, 0)),
        ],
        out_specs=(
            pl.BlockSpec(block, lambda j: (0, 0, 0, j)),
            pl.BlockSpec(block, lambda j: (0, 0, 0, j)),
        ),
        scratch_shapes=[pltpu.VMEM((4 * half, rows_y, rows_x, lanes), jnp.float32)],
    )(rim, below, low, high, above, older_low, older_high, potential, potential)


def extended_2(block, sides, width):
    for axis, dim in sides:
        count = lax.axis_size(axis)
        forward = [(i, i + 1) for i in range(count - 1)]
        backward = [(target, source) for source, target in forward]
        low = lax.ppermute(
            lax.slice_in_dim(block, block.shape[dim] - width, None, axis=dim), axis, forward
        )
        high = lax.ppermute(lax.slice_in_dim(block, 0, width, axis=dim), axis, backward)
        block = jnp.concatenate([low, block, high], axis=dim)
    return block


def hamiltonian(extended, potential):
    inner = extended[3:-3]
    planes = inner.shape[0]
    rows_y = inner.shape[1]
    rows_x = inner.shape[2]
    padded_y = jnp.pad(inner, ((0, 0), (3, 3), (0, 0), (0, 0)))
    padded_x = jnp.pad(inner, ((0, 0), (0, 0), (3, 3), (0, 0)))
    total = 3.0 * COEF[0] * inner
    for distance in (1, 2, 3):
        along_z = (
            extended[3 + distance : 3 + distance + planes]
            + extended[3 - distance : 3 - distance + planes]
        )
        along_y = (
            padded_y[:, 3 + distance : 3 + distance + rows_y]
            + padded_y[:, 3 - distance : 3 - distance + rows_y]
        )
        along_x = (
            padded_x[:, :, 3 + distance : 3 + distance + rows_x]
            + padded_x[:, :, 3 - distance : 3 - distance + rows_x]
        )
        total = total + COEF[distance] * (along_z + along_y + along_x)
    return potential[:, :, :, None] * inner - 0.5 * total


def shards(waves, potential, domain_of):
    slabs = lax.axis_size("gz")
    position = lax.axis_index("gz")
    planes = waves.shape[0]
    bands = waves.shape[3]
    grid = potential.reshape(planes, NY, NX)
    owner = domain_of[position]
    below = jnp.where(position > 0, domain_of[jnp.maximum(position - 1, 0)] == owner, False).astype(
        jnp.float32
    )
    above = jnp.where(
        position < slabs - 1, domain_of[jnp.minimum(position + 1, slabs - 1)] == owner, False
    ).astype(jnp.float32)
    mask_three = jnp.concatenate(
        [
            jnp.broadcast_to(below, (3,)),
            jnp.ones((planes,), jnp.float32),
            jnp.broadcast_to(above, (3,)),
        ]
    )[:, None, None, None]

    forward = [(i, i + 1) for i in range(slabs - 1)]
    backward = [(target, source) for source, target in forward]
    rim = jnp.stack([below, above])

    def rimmed(low, high):
        from_below = lax.ppermute(high, "gz", forward)
        from_above = lax.ppermute(low, "gz", backward)
        return from_below, from_above

    lanes = jnp.broadcast_to(grid[..., None], grid.shape + (128,))
    half = planes // 2
    low, high = waves[:half], waves[half:]
    from_below, from_above = rimmed(low, high)
    low, high = chebyshev_step(rim, from_below, low, high, from_above, waves, waves, lanes, True)
    older_low, older_high = waves, waves
    for turn in range(DEGREE - 1):
        from_below, from_above = rimmed(low, high)
        newer = chebyshev_step(
            rim, from_below, low, high, from_above, older_low, older_high, lanes, False
        )
        older_low, older_high = low, high
        low, high = newer
    current = jnp.concatenate([low, high], axis=0)
    cells = jnp.sum((domain_of == owner).astype(jnp.float32)) * (planes * NY * NX)
    rows = current.reshape(planes * NY * NX, bands)

    def domain_total(term):
        forward = term
        backward = term
        distance = 1
        while distance < slabs:
            ahead = [(i, i + distance) for i in range(slabs - distance)]
            behind = [(i + distance, i) for i in range(slabs - distance)]
            from_low = lax.ppermute(forward, "gz", ahead)
            from_high = lax.ppermute(backward, "gz", behind)
            low_same = jnp.where(
                position >= distance,
                domain_of[jnp.maximum(position - distance, 0)] == owner,
                False,
            ).astype(jnp.float32)
            high_same = jnp.where(
                position + distance < slabs,
                domain_of[jnp.minimum(position + distance, slabs - 1)] == owner,
                False,
            ).astype(jnp.float32)
            forward = forward + low_same * from_low
            backward = backward + high_same * from_high
            distance *= 2
        return forward + backward - term

    identity = jnp.eye(PANEL, dtype=jnp.float32)
    panels = bands // PANEL
    blocks = [rows[:, p * PANEL : (p + 1) * PANEL] for p in range(panels)]
    first = blocks[0]
    cross = jnp.einsum("ca,cb->ab", first, rows, preferred_element_type=jnp.float32)
    cross = domain_total(cross) / cells
    pieces = []
    whitenings = []
    for panel in range(panels):
        block = blocks[panel]
        if panel == 0:
            gram = cross[:, :PANEL]
        else:
            if panel == 1:
                correlation = jnp.dot(
                    whitenings[0].T.astype(jnp.float32),
                    cross[:, PANEL : 2 * PANEL],
                    preferred_element_type=jnp.float32,
                )
            else:
                earlier = jnp.concatenate(pieces, axis=1)
                correlation = (
                    domain_total(
                        jnp.einsum("ca,cb->ab", earlier, block, preferred_element_type=jnp.float32)
                    )
                    / cells
                )
            earlier = jnp.concatenate(pieces, axis=1)
            block = (
                block.astype(jnp.float32)
                - jnp.dot(
                    earlier, correlation.astype(jnp.bfloat16), preferred_element_type=jnp.float32
                )
            ).astype(jnp.bfloat16)
            gram = (
                domain_total(
                    jnp.einsum("ca,cb->ab", block, block, preferred_element_type=jnp.float32)
                )
                / cells
            )
        inverse = lower_inverse(gram)
        whitening = inverse.T.astype(jnp.bfloat16)
        whitenings.append(whitening)
        pieces.append(
            jnp.dot(block, whitening, preferred_element_type=jnp.float32).astype(jnp.bfloat16)
        )
    return jnp.concatenate(pieces, axis=1).reshape(planes, NY, NX, bands)


def solution(mesh):
    return jax.shard_map(
        shards,
        mesh=mesh,
        in_specs=(P(("groups", "gz"), None, None, None), P(("groups", "gz"), None), P("groups")),
        out_specs=P(("groups", "gz"), None, None, None),
        check_vma=False,
    )
```

```python
import functools

import jax
import jax.numpy as jnp
from jax import lax
from jax.experimental import pallas as pl
from jax.experimental.pallas import tpu as pltpu
from jax.sharding import PartitionSpec as P

PANEL = 128
NX = 64
NY = 8
DOMS = 8
DEGREE = 4


COEF = (-49.0 / 18.0, 1.5, -0.15, 1.0 / 90.0)
CSHIFT = 7.0
EWIDTH = 5.0


def _lower_inverse_kernel(gram_ref, out_ref, work_ref):
    n = gram_ref.shape[0]
    work_ref[:, :n] = gram_ref[...]
    work_ref[:, n:] = (lax.broadcasted_iota(jnp.int32, (n, n), 0) == lax.broadcasted_iota(jnp.int32, (n, n), 1)).astype(jnp.float32)

    rows = lax.broadcasted_iota(jnp.int32, (n, 2 * n), 0)
    left_lanes = lax.broadcasted_iota(jnp.int32, (n, n), 1)
    lane = lax.broadcasted_iota(jnp.int32, (1, 2 * n), 1)

    def pick(vector, index):
        return jnp.sum(jnp.where(lane == index, vector, 0.0), axis=1, keepdims=True)

    def step(pair, carry):
        k = 2 * pair
        row_a = work_ref[pl.ds(k, 1), :]
        row_b = work_ref[pl.ds(k + 1, 1), :]
        scale_a = 1.0 / jnp.sqrt(pick(row_a, k))
        scaled_a = row_a * scale_a
        row_b = row_b - (pick(row_b, k) * scale_a) * scaled_a
        scale_b = 1.0 / jnp.sqrt(pick(row_b, k + 1))
        scaled_b = row_b * scale_b
        whole = work_ref[...]
        left = whole[:, :n]
        column_a = jnp.sum(jnp.where(left_lanes == k, left, 0.0), axis=1, keepdims=True) * scale_a
        next_column = jnp.sum(jnp.where(left_lanes == k + 1, left, 0.0), axis=1, keepdims=True)
        column_b = (next_column - column_a * pick(scaled_a, k + 1)) * scale_b
        updated = (whole - column_a * scaled_a) - column_b * scaled_b
        updated = jnp.where(rows > k + 1, updated, whole)
        updated = jnp.where(rows == k, scaled_a, updated)
        work_ref[...] = jnp.where(rows == k + 1, scaled_b, updated)
        return carry

    lax.fori_loop(0, n // 2, step, 0)
    out_ref[...] = work_ref[:, n:]


def lower_inverse(gram):
    n = gram.shape[0]
    return pl.pallas_call(
        _lower_inverse_kernel,
        out_shape=jax.ShapeDtypeStruct((n, n), jnp.float32),
        scratch_shapes=[pltpu.VMEM((n, 2 * n), jnp.float32)],
    )(gram)


def _step_kernel(first, rim_ref, below_ref, low_ref, high_ref, above_ref, older_low_ref,
                 older_high_ref, low_pot_ref, high_pot_ref, out_low_ref, out_high_ref, wide_ref):
    half = low_ref.shape[0]
    rows_y = low_ref.shape[1]
    rows_x = low_ref.shape[2]
    sources = (below_ref, low_ref, high_ref, above_ref)

    for index in range(4 * half):
        value = sources[index // half][index % half].astype(jnp.float32)
        if index < half:
            value = value * rim_ref[0]
        elif index >= 3 * half:
            value = value * rim_ref[1]
        wide_ref[index, :, 8 : 8 + rows_x] = value
        if half <= index < 3 * half:
            wide_ref[index, :, 0:8] = jnp.zeros((rows_y, 8, value.shape[-1]), jnp.float32)
            wide_ref[index, :, 8 + rows_x : 16 + rows_x] = jnp.zeros(
                (rows_y, 8, value.shape[-1]), jnp.float32
            )

    def plane(index, y):
        return wide_ref[index, y, 8 : 8 + rows_x]

    for centre in range(half, 3 * half):
        own = centre - half
        older_ref = older_low_ref if own < half else older_high_ref
        potential_ref = low_pot_ref if own < half else high_pot_ref
        out_ref = out_low_ref if own < half else out_high_ref
        local = own % half
        for y in range(rows_y):
            inner = plane(centre, y)
            total = 3.0 * COEF[0] * inner
            for distance in (1, 2, 3):
                along_z = plane(centre + distance, y) + plane(centre - distance, y)
                up = plane(centre, y + distance) if y + distance < rows_y else None
                down = plane(centre, y - distance) if y - distance >= 0 else None
                if up is None:
                    along_y = down
                elif down is None:
                    along_y = up
                else:
                    along_y = up + down
                ahead = wide_ref[centre, y, 8 + distance : 8 + distance + rows_x]
                behind = wide_ref[centre, y, 8 - distance : 8 - distance + rows_x]
                along_x = ahead + behind
                total = total + COEF[distance] * (along_z + along_y + along_x)
            image = potential_ref[local, y] * inner - 0.5 * total
            if first:
                newer = (image - CSHIFT * inner) / EWIDTH
            else:
                newer = 2.0 / EWIDTH * (image - CSHIFT * inner) - older_ref[local, y].astype(
                    jnp.float32
                )
            out_ref[local, y] = newer.astype(out_ref.dtype)


def chebyshev_step(rim, below, low, high, above, older_low, older_high, potential, first):
    half, rows_y, rows_x, bands = low.shape
    lanes = 128
    block = (half, rows_y, rows_x, lanes)

    def spec(array, part):
        shift = part if array.shape[0] == 2 * half else 0
        return pl.BlockSpec(block, lambda j: (shift, 0, 0, j))

    piece = jax.ShapeDtypeStruct((half, rows_y, rows_x, bands), jnp.bfloat16)
    return pl.pallas_call(
        functools.partial(_step_kernel, first),
        out_shape=(piece, piece),
        grid=(bands // lanes,),
        in_specs=[
            pl.BlockSpec(memory_space=pltpu.SMEM),
            spec(below, 0),
            spec(low, 0),
            spec(high, 0),
            spec(above, 0),
            spec(older_low, 0),
            spec(older_high, 1),
            pl.BlockSpec(block, lambda j: (0, 0, 0, 0)),
            pl.BlockSpec(block, lambda j: (1, 0, 0, 0)),
        ],
        out_specs=(
            pl.BlockSpec(block, lambda j: (0, 0, 0, j)),
            pl.BlockSpec(block, lambda j: (0, 0, 0, j)),
        ),
        scratch_shapes=[pltpu.VMEM((4 * half, rows_y, rows_x + 16, lanes), jnp.float32)],
    )(rim, below, low, high, above, older_low, older_high, potential, potential)


def extended_2(block, sides, width):
    for axis, dim in sides:
        count = lax.axis_size(axis)
        forward = [(i, i + 1) for i in range(count - 1)]
        backward = [(target, source) for source, target in forward]
        low = lax.ppermute(
            lax.slice_in_dim(block, block.shape[dim] - width, None, axis=dim), axis, forward
        )
        high = lax.ppermute(lax.slice_in_dim(block, 0, width, axis=dim), axis, backward)
        block = jnp.concatenate([low, block, high], axis=dim)
    return block


def hamiltonian(extended, potential):
    inner = extended[3:-3]
    planes = inner.shape[0]
    rows_y = inner.shape[1]
    rows_x = inner.shape[2]
    padded_y = jnp.pad(inner, ((0, 0), (3, 3), (0, 0), (0, 0)))
    padded_x = jnp.pad(inner, ((0, 0), (0, 0), (3, 3), (0, 0)))
    total = 3.0 * COEF[0] * inner
    for distance in (1, 2, 3):
        along_z = (
            extended[3 + distance : 3 + distance + planes]
            + extended[3 - distance : 3 - distance + planes]
        )
        along_y = (
            padded_y[:, 3 + distance : 3 + distance + rows_y]
            + padded_y[:, 3 - distance : 3 - distance + rows_y]
        )
        along_x = (
            padded_x[:, :, 3 + distance : 3 + distance + rows_x]
            + padded_x[:, :, 3 - distance : 3 - distance + rows_x]
        )
        total = total + COEF[distance] * (along_z + along_y + along_x)
    return potential[:, :, :, None] * inner - 0.5 * total


def shards(waves, potential, domain_of):
    slabs = lax.axis_size("gz")
    position = lax.axis_index("gz")
    planes = waves.shape[0]
    bands = waves.shape[3]
    grid = potential.reshape(planes, NY, NX)
    owner = domain_of[position]
    below = jnp.where(position > 0, domain_of[jnp.maximum(position - 1, 0)] == owner, False).astype(
        jnp.float32
    )
    above = jnp.where(
        position < slabs - 1, domain_of[jnp.minimum(position + 1, slabs - 1)] == owner, False
    ).astype(jnp.float32)
    mask_three = jnp.concatenate(
        [
            jnp.broadcast_to(below, (3,)),
            jnp.ones((planes,), jnp.float32),
            jnp.broadcast_to(above, (3,)),
        ]
    )[:, None, None, None]

    forward = [(i, i + 1) for i in range(slabs - 1)]
    backward = [(target, source) for source, target in forward]
    rim = jnp.stack([below, above])

    def rimmed(low, high):
        from_below = lax.ppermute(high, "gz", forward)
        from_above = lax.ppermute(low, "gz", backward)
        return from_below, from_above

    lanes = jnp.broadcast_to(grid[..., None], grid.shape + (128,))
    half = planes // 2
    low, high = waves[:half], waves[half:]
    from_below, from_above = rimmed(low, high)
    low, high = chebyshev_step(rim, from_below, low, high, from_above, waves, waves, lanes, True)
    older_low, older_high = waves, waves
    for turn in range(DEGREE - 1):
        from_below, from_above = rimmed(low, high)
        newer = chebyshev_step(
            rim, from_below, low, high, from_above, older_low, older_high, lanes, False
        )
        older_low, older_high = low, high
        low, high = newer
    current = jnp.concatenate([low, high], axis=0)
    cells = jnp.sum((domain_of == owner).astype(jnp.float32)) * (planes * NY * NX)
    rows = current.reshape(planes * NY * NX, bands)

    def domain_total(term):
        forward = term
        backward = term
        distance = 1
        while distance < slabs:
            ahead = [(i, i + distance) for i in range(slabs - distance)]
            behind = [(i + distance, i) for i in range(slabs - distance)]
            from_low = lax.ppermute(forward, "gz", ahead)
            from_high = lax.ppermute(backward, "gz", behind)
            low_same = jnp.where(
                position >= distance,
                domain_of[jnp.maximum(position - distance, 0)] == owner,
                False,
            ).astype(jnp.float32)
            high_same = jnp.where(
                position + distance < slabs,
                domain_of[jnp.minimum(position + distance, slabs - 1)] == owner,
                False,
            ).astype(jnp.float32)
            forward = forward + low_same * from_low
            backward = backward + high_same * from_high
            distance *= 2
        return forward + backward - term

    identity = jnp.eye(PANEL, dtype=jnp.float32)
    panels = bands // PANEL
    blocks = [rows[:, p * PANEL : (p + 1) * PANEL] for p in range(panels)]
    first = blocks[0]
    cross = jnp.einsum("ca,cb->ab", first, rows, preferred_element_type=jnp.float32)
    cross = domain_total(cross) / cells
    pieces = []
    whitenings = []
    for panel in range(panels):
        block = blocks[panel]
        if panel == 0:
            gram = cross[:, :PANEL]
        else:
            if panel == 1:
                correlation = jnp.dot(
                    whitenings[0].T.astype(jnp.float32),
                    cross[:, PANEL : 2 * PANEL],
                    preferred_element_type=jnp.float32,
                )
            else:
                earlier = jnp.concatenate(pieces, axis=1)
                correlation = (
                    domain_total(
                        jnp.einsum("ca,cb->ab", earlier, block, preferred_element_type=jnp.float32)
                    )
                    / cells
                )
            earlier = jnp.concatenate(pieces, axis=1)
            block = (
                block.astype(jnp.float32)
                - jnp.dot(
                    earlier, correlation.astype(jnp.bfloat16), preferred_element_type=jnp.float32
                )
            ).astype(jnp.bfloat16)
            gram = (
                domain_total(
                    jnp.einsum("ca,cb->ab", block, block, preferred_element_type=jnp.float32)
                )
                / cells
            )
        inverse = lower_inverse(gram)
        whitening = inverse.T.astype(jnp.bfloat16)
        whitenings.append(whitening)
        pieces.append(
            jnp.dot(block, whitening, preferred_element_type=jnp.float32).astype(jnp.bfloat16)
        )
    return jnp.concatenate(pieces, axis=1).reshape(planes, NY, NX, bands)


def solution(mesh):
    return jax.shard_map(
        shards,
        mesh=mesh,
        in_specs=(P(("groups", "gz"), None, None, None), P(("groups", "gz"), None), P("groups")),
        out_specs=P(("groups", "gz"), None, None, None),
        check_vma=False,
    )
```

```python
import functools

import jax
import jax.numpy as jnp
from jax import lax
from jax.experimental import pallas as pl
from jax.experimental.pallas import tpu as pltpu
from jax.sharding import PartitionSpec as P

PANEL = 128
NX = 64
NY = 8
DOMS = 8
DEGREE = 4


COEF = (-49.0 / 18.0, 1.5, -0.15, 1.0 / 90.0)
CSHIFT = 7.0
EWIDTH = 5.0


def _lower_inverse_kernel(gram_ref, out_ref, work_ref):
    n = gram_ref.shape[0]
    work_ref[:, :n] = gram_ref[...]
    work_ref[:, n:] = (lax.broadcasted_iota(jnp.int32, (n, n), 0) == lax.broadcasted_iota(jnp.int32, (n, n), 1)).astype(jnp.float32)

    rows = lax.broadcasted_iota(jnp.int32, (n, 2 * n), 0)
    left_lanes = lax.broadcasted_iota(jnp.int32, (n, n), 1)
    lane = lax.broadcasted_iota(jnp.int32, (1, 2 * n), 1)

    def pick(vector, index):
        return jnp.sum(jnp.where(lane == index, vector, 0.0), axis=1, keepdims=True)

    def step(pair, carry):
        k = 2 * pair
        row_a = work_ref[pl.ds(k, 1), :]
        row_b = work_ref[pl.ds(k + 1, 1), :]
        scale_a = lax.rsqrt(pick(row_a, k))
        scaled_a = row_a * scale_a
        row_b = row_b - (pick(row_b, k) * scale_a) * scaled_a
        scale_b = lax.rsqrt(pick(row_b, k + 1))
        scaled_b = row_b * scale_b
        whole = work_ref[...]
        left = whole[:, :n]
        column_a = jnp.sum(jnp.where(left_lanes == k, left, 0.0), axis=1, keepdims=True) * scale_a
        next_column = jnp.sum(jnp.where(left_lanes == k + 1, left, 0.0), axis=1, keepdims=True)
        column_b = (next_column - column_a * pick(scaled_a, k + 1)) * scale_b
        updated = (whole - column_a * scaled_a) - column_b * scaled_b
        updated = jnp.where(rows > k + 1, updated, whole)
        updated = jnp.where(rows == k, scaled_a, updated)
        work_ref[...] = jnp.where(rows == k + 1, scaled_b, updated)
        return carry

    lax.fori_loop(0, n // 2, step, 0)
    out_ref[...] = work_ref[:, n:]


def lower_inverse(gram):
    n = gram.shape[0]
    return pl.pallas_call(
        _lower_inverse_kernel,
        out_shape=jax.ShapeDtypeStruct((n, n), jnp.float32),
        scratch_shapes=[pltpu.VMEM((n, 2 * n), jnp.float32)],
    )(gram)


def _step_kernel(first, rim_ref, below_ref, low_ref, high_ref, above_ref, older_low_ref,
                 older_high_ref, low_pot_ref, high_pot_ref, out_low_ref, out_high_ref, wide_ref):
    half = low_ref.shape[0]
    rows_y = low_ref.shape[1]
    rows_x = low_ref.shape[2]
    sources = (below_ref, low_ref, high_ref, above_ref)

    for index in range(4 * half):
        value = sources[index // half][index % half].astype(jnp.float32)
        if index < half:
            value = value * rim_ref[0]
        elif index >= 3 * half:
            value = value * rim_ref[1]
        wide_ref[index, :, 8 : 8 + rows_x] = value
        if half <= index < 3 * half:
            wide_ref[index, :, 0:8] = jnp.zeros((rows_y, 8, value.shape[-1]), jnp.float32)
            wide_ref[index, :, 8 + rows_x : 16 + rows_x] = jnp.zeros(
                (rows_y, 8, value.shape[-1]), jnp.float32
            )

    def plane(index, y):
        return wide_ref[index, y, 8 : 8 + rows_x]

    for centre in range(half, 3 * half):
        own = centre - half
        older_ref = older_low_ref if own < half else older_high_ref
        potential_ref = low_pot_ref if own < half else high_pot_ref
        out_ref = out_low_ref if own < half else out_high_ref
        local = own % half
        for y in range(rows_y):
            inner = plane(centre, y)
            total = 3.0 * COEF[0] * inner
            for distance in (1, 2, 3):
                along_z = plane(centre + distance, y) + plane(centre - distance, y)
                up = plane(centre, y + distance) if y + distance < rows_y else None
                down = plane(centre, y - distance) if y - distance >= 0 else None
                if up is None:
                    along_y = down
                elif down is None:
                    along_y = up
                else:
                    along_y = up + down
                ahead = wide_ref[centre, y, 8 + distance : 8 + distance + rows_x]
                behind = wide_ref[centre, y, 8 - distance : 8 - distance + rows_x]
                along_x = ahead + behind
                total = total + COEF[distance] * (along_z + along_y + along_x)
            image = potential_ref[local, y] * inner - 0.5 * total
            if first:
                newer = (image - CSHIFT * inner) / EWIDTH
            else:
                newer = 2.0 / EWIDTH * (image - CSHIFT * inner) - older_ref[local, y].astype(
                    jnp.float32
                )
            out_ref[local, y] = newer.astype(out_ref.dtype)


def chebyshev_step(rim, below, low, high, above, older_low, older_high, potential, first):
    half, rows_y, rows_x, bands = low.shape
    lanes = 128
    block = (half, rows_y, rows_x, lanes)

    def spec(array, part):
        shift = part if array.shape[0] == 2 * half else 0
        return pl.BlockSpec(block, lambda j: (shift, 0, 0, j))

    piece = jax.ShapeDtypeStruct((half, rows_y, rows_x, bands), jnp.bfloat16)
    return pl.pallas_call(
        functools.partial(_step_kernel, first),
        out_shape=(piece, piece),
        grid=(bands // lanes,),
        in_specs=[
            pl.BlockSpec(memory_space=pltpu.SMEM),
            spec(below, 0),
            spec(low, 0),
            spec(high, 0),
            spec(above, 0),
            spec(older_low, 0),
            spec(older_high, 1),
            pl.BlockSpec(block, lambda j: (0, 0, 0, 0)),
            pl.BlockSpec(block, lambda j: (1, 0, 0, 0)),
        ],
        out_specs=(
            pl.BlockSpec(block, lambda j: (0, 0, 0, j)),
            pl.BlockSpec(block, lambda j: (0, 0, 0, j)),
        ),
        scratch_shapes=[pltpu.VMEM((4 * half, rows_y, rows_x + 16, lanes), jnp.float32)],
    )(rim, below, low, high, above, older_low, older_high, potential, potential)


def extended_2(block, sides, width):
    for axis, dim in sides:
        count = lax.axis_size(axis)
        forward = [(i, i + 1) for i in range(count - 1)]
        backward = [(target, source) for source, target in forward]
        low = lax.ppermute(
            lax.slice_in_dim(block, block.shape[dim] - width, None, axis=dim), axis, forward
        )
        high = lax.ppermute(lax.slice_in_dim(block, 0, width, axis=dim), axis, backward)
        block = jnp.concatenate([low, block, high], axis=dim)
    return block


def hamiltonian(extended, potential):
    inner = extended[3:-3]
    planes = inner.shape[0]
    rows_y = inner.shape[1]
    rows_x = inner.shape[2]
    padded_y = jnp.pad(inner, ((0, 0), (3, 3), (0, 0), (0, 0)))
    padded_x = jnp.pad(inner, ((0, 0), (0, 0), (3, 3), (0, 0)))
    total = 3.0 * COEF[0] * inner
    for distance in (1, 2, 3):
        along_z = (
            extended[3 + distance : 3 + distance + planes]
            + extended[3 - distance : 3 - distance + planes]
        )
        along_y = (
            padded_y[:, 3 + distance : 3 + distance + rows_y]
            + padded_y[:, 3 - distance : 3 - distance + rows_y]
        )
        along_x = (
            padded_x[:, :, 3 + distance : 3 + distance + rows_x]
            + padded_x[:, :, 3 - distance : 3 - distance + rows_x]
        )
        total = total + COEF[distance] * (along_z + along_y + along_x)
    return potential[:, :, :, None] * inner - 0.5 * total


def shards(waves, potential, domain_of):
    slabs = lax.axis_size("gz")
    position = lax.axis_index("gz")
    planes = waves.shape[0]
    bands = waves.shape[3]
    grid = potential.reshape(planes, NY, NX)
    owner = domain_of[position]
    below = jnp.where(position > 0, domain_of[jnp.maximum(position - 1, 0)] == owner, False).astype(
        jnp.float32
    )
    above = jnp.where(
        position < slabs - 1, domain_of[jnp.minimum(position + 1, slabs - 1)] == owner, False
    ).astype(jnp.float32)
    mask_three = jnp.concatenate(
        [
            jnp.broadcast_to(below, (3,)),
            jnp.ones((planes,), jnp.float32),
            jnp.broadcast_to(above, (3,)),
        ]
    )[:, None, None, None]

    forward = [(i, i + 1) for i in range(slabs - 1)]
    backward = [(target, source) for source, target in forward]
    rim = jnp.stack([below, above])

    def rimmed(low, high):
        from_below = lax.ppermute(high, "gz", forward)
        from_above = lax.ppermute(low, "gz", backward)
        return from_below, from_above

    lanes = jnp.broadcast_to(grid[..., None], grid.shape + (128,))
    half = planes // 2
    low, high = waves[:half], waves[half:]
    from_below, from_above = rimmed(low, high)
    low, high = chebyshev_step(rim, from_below, low, high, from_above, waves, waves, lanes, True)
    older_low, older_high = waves, waves
    for turn in range(DEGREE - 1):
        from_below, from_above = rimmed(low, high)
        newer = chebyshev_step(
            rim, from_below, low, high, from_above, older_low, older_high, lanes, False
        )
        older_low, older_high = low, high
        low, high = newer
    current = jnp.concatenate([low, high], axis=0)
    cells = jnp.sum((domain_of == owner).astype(jnp.float32)) * (planes * NY * NX)
    rows = current.reshape(planes * NY * NX, bands)

    def domain_total(term):
        forward = term
        backward = term
        distance = 1
        while distance < slabs:
            ahead = [(i, i + distance) for i in range(slabs - distance)]
            behind = [(i + distance, i) for i in range(slabs - distance)]
            from_low = lax.ppermute(forward, "gz", ahead)
            from_high = lax.ppermute(backward, "gz", behind)
            low_same = jnp.where(
                position >= distance,
                domain_of[jnp.maximum(position - distance, 0)] == owner,
                False,
            ).astype(jnp.float32)
            high_same = jnp.where(
                position + distance < slabs,
                domain_of[jnp.minimum(position + distance, slabs - 1)] == owner,
                False,
            ).astype(jnp.float32)
            forward = forward + low_same * from_low
            backward = backward + high_same * from_high
            distance *= 2
        return forward + backward - term

    identity = jnp.eye(PANEL, dtype=jnp.float32)
    panels = bands // PANEL
    blocks = [rows[:, p * PANEL : (p + 1) * PANEL] for p in range(panels)]
    first = blocks[0]
    cross = jnp.einsum("ca,cb->ab", first, rows, preferred_element_type=jnp.float32)
    cross = domain_total(cross) / cells
    pieces = []
    whitenings = []
    for panel in range(panels):
        block = blocks[panel]
        if panel == 0:
            gram = cross[:, :PANEL]
        else:
            if panel == 1:
                correlation = jnp.dot(
                    whitenings[0].T.astype(jnp.float32),
                    cross[:, PANEL : 2 * PANEL],
                    preferred_element_type=jnp.float32,
                )
            else:
                earlier = jnp.concatenate(pieces, axis=1)
                correlation = (
                    domain_total(
                        jnp.einsum("ca,cb->ab", earlier, block, preferred_element_type=jnp.float32)
                    )
                    / cells
                )
            earlier = jnp.concatenate(pieces, axis=1)
            block = (
                block.astype(jnp.float32)
                - jnp.dot(
                    earlier, correlation.astype(jnp.bfloat16), preferred_element_type=jnp.float32
                )
            ).astype(jnp.bfloat16)
            gram = (
                domain_total(
                    jnp.einsum("ca,cb->ab", block, block, preferred_element_type=jnp.float32)
                )
                / cells
            )
        inverse = lower_inverse(gram)
        whitening = inverse.T.astype(jnp.bfloat16)
        whitenings.append(whitening)
        pieces.append(
            jnp.dot(block, whitening, preferred_element_type=jnp.float32).astype(jnp.bfloat16)
        )
    return jnp.concatenate(pieces, axis=1).reshape(planes, NY, NX, bands)


def solution(mesh):
    return jax.shard_map(
        shards,
        mesh=mesh,
        in_specs=(P(("groups", "gz"), None, None, None), P(("groups", "gz"), None), P("groups")),
        out_specs=P(("groups", "gz"), None, None, None),
        check_vma=False,
    )
```

```python
import functools

import jax
import jax.numpy as jnp
from jax import lax
from jax.experimental import pallas as pl
from jax.experimental.pallas import tpu as pltpu
from jax.sharding import PartitionSpec as P

PANEL = 128
NX = 64
NY = 8
DOMS = 8
DEGREE = 4


COEF = (-49.0 / 18.0, 1.5, -0.15, 1.0 / 90.0)
CSHIFT = 7.0
EWIDTH = 5.0


def _lower_inverse_kernel(gram_ref, out_ref, work_ref):
    n = gram_ref.shape[0]
    work_ref[:, :n] = gram_ref[...]
    work_ref[:, n:] = (lax.broadcasted_iota(jnp.int32, (n, n), 0) == lax.broadcasted_iota(jnp.int32, (n, n), 1)).astype(jnp.float32)

    rows = lax.broadcasted_iota(jnp.int32, (n, 2 * n), 0)
    left_lanes = lax.broadcasted_iota(jnp.int32, (n, n), 1)
    lane = lax.broadcasted_iota(jnp.int32, (1, 2 * n), 1)

    def pick(vector, index):
        return jnp.sum(jnp.where(lane == index, vector, 0.0), axis=1, keepdims=True)

    def step(pair, carry):
        k = 2 * pair
        row_a = work_ref[pl.ds(k, 1), :]
        row_b = work_ref[pl.ds(k + 1, 1), :]
        scale_a = lax.rsqrt(pick(row_a, k))
        scaled_a = row_a * scale_a
        row_b = row_b - (pick(row_b, k) * scale_a) * scaled_a
        scale_b = lax.rsqrt(pick(row_b, k + 1))
        scaled_b = row_b * scale_b
        whole = work_ref[...]
        left = whole[:, :n]
        column_a = jnp.sum(jnp.where(left_lanes == k, left, 0.0), axis=1, keepdims=True) * scale_a
        next_column = jnp.sum(jnp.where(left_lanes == k + 1, left, 0.0), axis=1, keepdims=True)
        column_b = (next_column - column_a * pick(scaled_a, k + 1)) * scale_b
        updated = (whole - column_a * scaled_a) - column_b * scaled_b
        updated = jnp.where(rows > k + 1, updated, whole)
        updated = jnp.where(rows == k, scaled_a, updated)
        work_ref[...] = jnp.where(rows == k + 1, scaled_b, updated)
        return carry

    lax.fori_loop(0, n // 2, step, 0)
    out_ref[...] = work_ref[:, n:]


def lower_inverse(gram):
    n = gram.shape[0]
    return pl.pallas_call(
        _lower_inverse_kernel,
        out_shape=jax.ShapeDtypeStruct((n, n), jnp.float32),
        scratch_shapes=[pltpu.VMEM((n, 2 * n), jnp.float32)],
    )(gram)


def _step_kernel(first, rim_ref, below_ref, low_ref, high_ref, above_ref, older_low_ref,
                 older_high_ref, low_pot_ref, high_pot_ref, out_low_ref, out_high_ref, wide_ref):
    half = low_ref.shape[0]
    rows_y = low_ref.shape[1]
    rows_x = low_ref.shape[2]
    sources = (below_ref, low_ref, high_ref, above_ref)

    for index in range(4 * half):
        value = sources[index // half][index % half].astype(jnp.float32)
        if index < half:
            value = value * rim_ref[0]
        elif index >= 3 * half:
            value = value * rim_ref[1]
        wide_ref[index, :, 8 : 8 + rows_x] = value
        if half <= index < 3 * half:
            wide_ref[index, :, 0:8] = jnp.zeros((rows_y, 8, value.shape[-1]), jnp.float32)
            wide_ref[index, :, 8 + rows_x : 16 + rows_x] = jnp.zeros(
                (rows_y, 8, value.shape[-1]), jnp.float32
            )

    def plane(index, y):
        return wide_ref[index, y, 8 : 8 + rows_x]

    for centre in range(half, 3 * half):
        own = centre - half
        older_ref = older_low_ref if own < half else older_high_ref
        potential_ref = low_pot_ref if own < half else high_pot_ref
        out_ref = out_low_ref if own < half else out_high_ref
        local = own % half
        for y in range(rows_y):
            inner = plane(centre, y)
            total = 3.0 * COEF[0] * inner
            for distance in (1, 2, 3):
                along_z = plane(centre + distance, y) + plane(centre - distance, y)
                up = plane(centre, y + distance) if y + distance < rows_y else None
                down = plane(centre, y - distance) if y - distance >= 0 else None
                if up is None:
                    along_y = down
                elif down is None:
                    along_y = up
                else:
                    along_y = up + down
                ahead = wide_ref[centre, y, 8 + distance : 8 + distance + rows_x]
                behind = wide_ref[centre, y, 8 - distance : 8 - distance + rows_x]
                along_x = ahead + behind
                total = total + COEF[distance] * (along_z + along_y + along_x)
            image = potential_ref[local, y] * inner - 0.5 * total
            if first:
                newer = (image - CSHIFT * inner) / EWIDTH
            else:
                newer = 2.0 / EWIDTH * (image - CSHIFT * inner) - older_ref[local, y].astype(
                    jnp.float32
                )
            out_ref[local, y] = newer.astype(out_ref.dtype)


def chebyshev_step(rim, below, low, high, above, older_low, older_high, potential, first):
    half, rows_y, rows_x, bands = low.shape
    lanes = 128
    block = (half, rows_y, rows_x, lanes)

    def spec(array, part):
        shift = part if array.shape[0] == 2 * half else 0
        return pl.BlockSpec(block, lambda j: (shift, 0, 0, j))

    piece = jax.ShapeDtypeStruct((half, rows_y, rows_x, bands), jnp.bfloat16)
    return pl.pallas_call(
        functools.partial(_step_kernel, first),
        out_shape=(piece, piece),
        grid=(bands // lanes,),
        in_specs=[
            pl.BlockSpec(memory_space=pltpu.SMEM),
            spec(below, 0),
            spec(low, 0),
            spec(high, 0),
            spec(above, 0),
            spec(older_low, 0),
            spec(older_high, 1),
            pl.BlockSpec((half, rows_y, rows_x, 1), lambda j: (0, 0, 0, 0)),
            pl.BlockSpec((half, rows_y, rows_x, 1), lambda j: (1, 0, 0, 0)),
        ],
        out_specs=(
            pl.BlockSpec(block, lambda j: (0, 0, 0, j)),
            pl.BlockSpec(block, lambda j: (0, 0, 0, j)),
        ),
        scratch_shapes=[pltpu.VMEM((4 * half, rows_y, rows_x + 16, lanes), jnp.float32)],
    )(rim, below, low, high, above, older_low, older_high, potential, potential)


def extended_2(block, sides, width):
    for axis, dim in sides:
        count = lax.axis_size(axis)
        forward = [(i, i + 1) for i in range(count - 1)]
        backward = [(target, source) for source, target in forward]
        low = lax.ppermute(
            lax.slice_in_dim(block, block.shape[dim] - width, None, axis=dim), axis, forward
        )
        high = lax.ppermute(lax.slice_in_dim(block, 0, width, axis=dim), axis, backward)
        block = jnp.concatenate([low, block, high], axis=dim)
    return block


def hamiltonian(extended, potential):
    inner = extended[3:-3]
    planes = inner.shape[0]
    rows_y = inner.shape[1]
    rows_x = inner.shape[2]
    padded_y = jnp.pad(inner, ((0, 0), (3, 3), (0, 0), (0, 0)))
    padded_x = jnp.pad(inner, ((0, 0), (0, 0), (3, 3), (0, 0)))
    total = 3.0 * COEF[0] * inner
    for distance in (1, 2, 3):
        along_z = (
            extended[3 + distance : 3 + distance + planes]
            + extended[3 - distance : 3 - distance + planes]
        )
        along_y = (
            padded_y[:, 3 + distance : 3 + distance + rows_y]
            + padded_y[:, 3 - distance : 3 - distance + rows_y]
        )
        along_x = (
            padded_x[:, :, 3 + distance : 3 + distance + rows_x]
            + padded_x[:, :, 3 - distance : 3 - distance + rows_x]
        )
        total = total + COEF[distance] * (along_z + along_y + along_x)
    return potential[:, :, :, None] * inner - 0.5 * total


def shards(waves, potential, domain_of):
    slabs = lax.axis_size("gz")
    position = lax.axis_index("gz")
    planes = waves.shape[0]
    bands = waves.shape[3]
    grid = potential.reshape(planes, NY, NX)
    owner = domain_of[position]
    below = jnp.where(position > 0, domain_of[jnp.maximum(position - 1, 0)] == owner, False).astype(
        jnp.float32
    )
    above = jnp.where(
        position < slabs - 1, domain_of[jnp.minimum(position + 1, slabs - 1)] == owner, False
    ).astype(jnp.float32)
    mask_three = jnp.concatenate(
        [
            jnp.broadcast_to(below, (3,)),
            jnp.ones((planes,), jnp.float32),
            jnp.broadcast_to(above, (3,)),
        ]
    )[:, None, None, None]

    forward = [(i, i + 1) for i in range(slabs - 1)]
    backward = [(target, source) for source, target in forward]
    rim = jnp.stack([below, above])

    def rimmed(low, high):
        from_below = lax.ppermute(high, "gz", forward)
        from_above = lax.ppermute(low, "gz", backward)
        return from_below, from_above

    lanes = grid[..., None]
    half = planes // 2
    low, high = waves[:half], waves[half:]
    from_below, from_above = rimmed(low, high)
    low, high = chebyshev_step(rim, from_below, low, high, from_above, waves, waves, lanes, True)
    older_low, older_high = waves, waves
    for turn in range(DEGREE - 1):
        from_below, from_above = rimmed(low, high)
        newer = chebyshev_step(
            rim, from_below, low, high, from_above, older_low, older_high, lanes, False
        )
        older_low, older_high = low, high
        low, high = newer
    current = jnp.concatenate([low, high], axis=0)
    cells = jnp.sum((domain_of == owner).astype(jnp.float32)) * (planes * NY * NX)
    rows = current.reshape(planes * NY * NX, bands)

    def domain_total(term):
        forward = term
        backward = term
        distance = 1
        while distance < slabs:
            ahead = [(i, i + distance) for i in range(slabs - distance)]
            behind = [(i + distance, i) for i in range(slabs - distance)]
            from_low = lax.ppermute(forward, "gz", ahead)
            from_high = lax.ppermute(backward, "gz", behind)
            low_same = jnp.where(
                position >= distance,
                domain_of[jnp.maximum(position - distance, 0)] == owner,
                False,
            ).astype(jnp.float32)
            high_same = jnp.where(
                position + distance < slabs,
                domain_of[jnp.minimum(position + distance, slabs - 1)] == owner,
                False,
            ).astype(jnp.float32)
            forward = forward + low_same * from_low
            backward = backward + high_same * from_high
            distance *= 2
        return forward + backward - term

    identity = jnp.eye(PANEL, dtype=jnp.float32)
    panels = bands // PANEL
    blocks = [rows[:, p * PANEL : (p + 1) * PANEL] for p in range(panels)]
    first = blocks[0]
    cross = jnp.einsum("ca,cb->ab", first, rows, preferred_element_type=jnp.float32)
    cross = domain_total(cross) / cells
    pieces = []
    whitenings = []
    for panel in range(panels):
        block = blocks[panel]
        if panel == 0:
            gram = cross[:, :PANEL]
        else:
            if panel == 1:
                correlation = jnp.dot(
                    whitenings[0].T.astype(jnp.float32),
                    cross[:, PANEL : 2 * PANEL],
                    preferred_element_type=jnp.float32,
                )
            else:
                earlier = jnp.concatenate(pieces, axis=1)
                correlation = (
                    domain_total(
                        jnp.einsum("ca,cb->ab", earlier, block, preferred_element_type=jnp.float32)
                    )
                    / cells
                )
            earlier = jnp.concatenate(pieces, axis=1)
            block = (
                block.astype(jnp.float32)
                - jnp.dot(
                    earlier, correlation.astype(jnp.bfloat16), preferred_element_type=jnp.float32
                )
            ).astype(jnp.bfloat16)
            gram = (
                domain_total(
                    jnp.einsum("ca,cb->ab", block, block, preferred_element_type=jnp.float32)
                )
                / cells
            )
        inverse = lower_inverse(gram)
        whitening = inverse.T.astype(jnp.bfloat16)
        whitenings.append(whitening)
        pieces.append(
            jnp.dot(block, whitening, preferred_element_type=jnp.float32).astype(jnp.bfloat16)
        )
    return jnp.concatenate(pieces, axis=1).reshape(planes, NY, NX, bands)


def solution(mesh):
    return jax.shard_map(
        shards,
        mesh=mesh,
        in_specs=(P(("groups", "gz"), None, None, None), P(("groups", "gz"), None), P("groups")),
        out_specs=P(("groups", "gz"), None, None, None),
        check_vma=False,
    )
```
